32 devices in a mesh: range: 4 (over z), line: 4 (over y, x), freq: 2 (over core).
Axes of the slice: x: 2, y: 2, z: 4, core: 2. Of those that a mesh axis runs over, the one named last changes fastest.
Arguments:
- checkpoint: bfloat16 [4, 4, 1024, 2048], P('range', 'freq', None, 'line'), parts along dimension 1, may hold values from -6 to 6
- adjoint_start: bfloat16 [4, 4, 1024, 2048], P('range', 'freq', None, 'line'), parts along dimension 1, may hold values from -6 to 6
- misfit: bfloat16 [4, 4, 1024, 2048], P('range', 'freq', None, 'line'), parts along dimension 1, may hold values from -3 to 3
- pade_factors: bfloat16 [6, 4, 256, 256], P(None, 'freq'), parts along dimension 1, may hold values from -0.6 to 1.4
- azimuth_inverse: bfloat16 [4, 4, 256, 256], P('range', 'freq'), parts along dimension 1, may hold values from -0.6 to 1.4
- bottom: int32 [4, 1024], P('range'), may hold values from 512 to 2047
- base_speed: float32 [2048], P('line'), may hold values from 0.92 to 1.08
- speed_step: float32 [4, 2048], P('range', 'line'), may hold values from -0.012 to 0.012
Outputs:
- field_end: bfloat16 [4, 4, 1024, 2048], P('range', 'freq', None, 'line'), parts along dimension 1
- adjoint_begin: bfloat16 [4, 4, 1024, 2048], P('range', 'freq', None, 'line'), parts along dimension 1
- grad_increment: float32 [8, 2048], P(('freq', 'range'), 'line'), parts along dimension 0
The draws below stay inside these ranges and needn't reach their ends.
There are 2 independent parts, one for each index of `freq`. The reference program is written for one: setup_inputs(seed, part) draws one part's arguments, and reference() takes and returns one part's arrays. A program takes and returns all parts, laid end to end along the dimension named above; an argument that names none is the same for every part. Nothing has to cross between parts.
All inputs are finite; a program needn't handle non-finite values.
Results may differ from the reference program's by a relative error of at most 0.0093.
Values may be sent and summed in bfloat16 or wider, within the bound.
No kernel may reach another device: no remote copies, remote signals or barrier semaphores. Data moves between devices by JAX's collectives and lax.ppermute only.
A program may use at most 64 MiB of HBM per device.

```python
import math
import jax
import jax.numpy as jnp
from jax import lax

NZ = 2048
NA = 1024
DB = 256
AB = 256
NPADE = 6
S = 4


def blocked_factor(key, factor_count, block_width):
    noise_draw = jax.random.truncated_normal(key, -4.0, 4.0, (factor_count, 2, block_width, block_width), jnp.float32)
    spread = 0.4 / math.sqrt(block_width)
    identity = (jnp.arange(block_width)[:, None] == jnp.arange(block_width)[None, :]).astype(jnp.float32)
    real_first = (jnp.arange(2) == 0).astype(jnp.float32)[None, :, None, None]
    values = (identity[None, None] * real_first + spread * noise_draw) / math.sqrt(1.32)
    return values.astype(jnp.bfloat16)


def draw_pade_factors(key, part):
    return blocked_factor(jax.random.fold_in(key, 11), NPADE, DB)


def draw_azimuth_inverse(key, part):
    return blocked_factor(jax.random.fold_in(key, 23), S, AB)


def plant(drawn, stream_key, smallest, high):
    place = [jax.random.randint(jax.random.fold_in(stream_key, axis), (), 0, length) for axis, length in enumerate(drawn.shape)]
    main_axis = drawn.shape.index(max(drawn.shape))
    beside = place[:main_axis] + [(place[main_axis] + 1) % drawn.shape[main_axis]] + place[main_axis + 1:]
    return drawn.at[tuple(place)].set(smallest).at[tuple(beside)].set(high)


def steps_of(key, shape, pieces, smallest, high):
    level = 1.0
    for position, parts in pieces:
        heights = jax.random.uniform(jax.random.fold_in(jax.random.fold_in(key, 6), position), (parts,), jnp.float32, smallest / len(pieces), high / len(pieces))
        level = level * jnp.repeat(jnp.exp(heights), shape[position] // parts).reshape((-1,) + (1,) * (len(shape) - 1 - position))
    return level


def gaussian(own_key, shape, scale, reach, pieces=(), kind=jnp.bfloat16):
    loudness = steps_of(own_key, shape, pieces, -0.22, 0.18) if pieces else 1.0
    array = jax.random.normal(own_key, shape, jnp.float32) * scale * loudness
    return jnp.minimum(jnp.maximum(array, -reach), reach).astype(kind)


def setup_inputs(seed: int = 0, part: int = 0) -> dict:
    arg_keys = jax.random.split(jax.random.key(seed), 9)
    own_keys = jax.random.split(jax.random.fold_in(arg_keys[8], part), 9)
    checkpoint = gaussian(own_keys[0], (S, 2, NA, NZ), 1.0, 6.0, ((0, 4), (3, 4)))
    adjoint_start = gaussian(own_keys[1], (S, 2, NA, NZ), 1.0, 6.0, ((0, 4), (3, 4)))
    misfit = gaussian(own_keys[2], (S, 2, NA, NZ), 0.5, 3.0, ((0, 4), (3, 4)))
    pade_factors = draw_pade_factors(jax.random.fold_in(jax.random.fold_in(arg_keys[8], part), 71), part)
    azimuth_inverse = draw_azimuth_inverse(jax.random.fold_in(jax.random.fold_in(arg_keys[8], part), 71), part)
    bottom = plant(jax.random.randint(arg_keys[5], (S, NA), NZ // 4, NZ), jax.random.fold_in(arg_keys[5], 1), NZ // 4, NZ - 1).astype(jnp.int32)
    base_speed = jnp.clip(0.92 + 0.16000003 * jax.random.uniform(arg_keys[6], (NZ,), jnp.float32) ** steps_of(arg_keys[6], (NZ,), ((0, 4),), -0.2, 0.2), 0.92, 1.08)
    speed_step = jnp.clip(jax.random.uniform(arg_keys[7], (S, NZ), jnp.float32, -0.012, 0.012) * steps_of(arg_keys[7], (S, NZ), ((0, 4), (1, 4)), -0.4, 0.0), -0.012, 0.012)
    return dict(checkpoint=checkpoint, adjoint_start=adjoint_start, misfit=misfit, pade_factors=pade_factors, azimuth_inverse=azimuth_inverse, bottom=bottom, base_speed=base_speed, speed_step=speed_step)


phase_scale = 4.0
bed_phase = -1.8
coupling = 0.3


def pair_terms(diag_one, diag_two, cross_one, cross_two, adjoint):
    if adjoint:
        return diag_one + diag_two, cross_one - cross_two
    return diag_one - diag_two, cross_one + cross_two


def depth_apply(current, pade_ops, adjoint):
    factor_count = pade_ops.shape[0]
    sequence = range(factor_count - 1, -1, -1) if adjoint else range(factor_count)
    for factor in sequence:
        contract = 1 if adjoint else 2
        product = lax.dot_general(current, pade_ops[factor], (((3,), (contract,)), ((), ())), preferred_element_type=jnp.float32)
        real_part, imag_part = pair_terms(product[0, :, :, 0], product[1, :, :, 1], product[1, :, :, 0], product[0, :, :, 1], adjoint)
        current = jnp.stack([real_part, imag_part]).astype(jnp.bfloat16)
    return current


def azimuth_apply(field_in, inverse, adjoint):
    block_width = inverse.shape[1]
    blocked = field_in.reshape(2, field_in.shape[1] // block_width, block_width, field_in.shape[2])
    contract = 1 if adjoint else 2
    product = lax.dot_general(inverse, blocked, (((contract,), (2,)), ((), ())), preferred_element_type=jnp.float32)
    real_part, imag_part = pair_terms(product[0, :, 0], product[1, :, 1], product[0, :, 1], product[1, :, 0], adjoint)
    joined = jnp.stack([real_part, imag_part])
    return joined.transpose(0, 2, 1, 3).reshape(field_in.shape)


def numerator_map(field_in):
    return field_in + coupling * (jnp.roll(field_in, 1, axis=1) + jnp.roll(field_in, -1, axis=1) - 2.0 * field_in)


def screen_phase(profile, bottom_row, depth_start):
    depths = depth_start + jnp.arange(profile.shape[0], dtype=jnp.int32)
    in_water = depths[None, :] < bottom_row[:, None]
    water_phase = phase_scale * (1.0 / (profile * profile) - 1.0)
    return jnp.where(in_water, water_phase[None, :], bed_phase), in_water


def section_step(checkpoint, following, misfit, inverse, bottom_row, profile, pade_factors):
    phase_angle, in_water = screen_phase(profile, bottom_row, 0)
    cosine = jnp.cos(phase_angle)
    sine_term = jnp.sin(phase_angle)
    source = checkpoint.astype(jnp.float32)
    screened = jnp.stack([cosine * source[0] - sine_term * source[1], sine_term * source[0] + cosine * source[1]]).astype(jnp.bfloat16)
    depth_out = depth_apply(screened.reshape(2, NA, NZ // DB, DB), pade_factors, False).reshape(2, NA, NZ)
    numerator = numerator_map(depth_out.astype(jnp.float32)).astype(jnp.bfloat16)
    field_end = azimuth_apply(numerator, inverse, False).astype(jnp.bfloat16)
    lam_end = (following.astype(jnp.float32) + misfit.astype(jnp.float32)).astype(jnp.bfloat16)
    backward = numerator_map(azimuth_apply(lam_end, inverse, True)).astype(jnp.bfloat16)
    backward = depth_apply(backward.reshape(2, NA, NZ // DB, DB), pade_factors, True).reshape(2, NA, NZ)
    cotangent = backward.astype(jnp.float32)
    adjoint_begin = jnp.stack([cosine * cotangent[0] + sine_term * cotangent[1], cosine * cotangent[1] - sine_term * cotangent[0]]).astype(jnp.bfloat16)
    screened_f = screened.astype(jnp.float32)
    weight = jnp.where(in_water, cotangent[1] * screened_f[0] - cotangent[0] * screened_f[1], 0.0)
    grad_profile = jnp.sum(weight, axis=0) * (-8.0 / (profile * profile * profile)) / NA
    return field_end, adjoint_begin, grad_profile


def reference(checkpoint, adjoint_start, misfit, pade_factors, azimuth_inverse, bottom, base_speed, speed_step):
    profiles = base_speed[None, :] + jnp.cumsum(speed_step, axis=0)
    following = jnp.concatenate([adjoint_start[1:], jnp.zeros_like(adjoint_start[:1])], axis=0)

    def one_section(inputs):
        return section_step(inputs[0], inputs[1], inputs[2], inputs[3], inputs[4], inputs[5], pade_factors)

    field_end, adjoint_begin, grad_profile = lax.map(one_section, (checkpoint, following, misfit, azimuth_inverse, bottom, profiles))
    grad_increment = jnp.flip(jnp.cumsum(jnp.flip(grad_profile, 0), axis=0), 0)
    return field_end, adjoint_begin, grad_increment
```

```python
import jax
import jax.numpy as jnp
from jax import lax
from jax.sharding import PartitionSpec as P

phase_scale = 4.0
bed_phase = -1.8
coupling = 0.3


def passed_along(value, axis, by):
    count = lax.axis_size(axis)
    pairs = [(i, i + by) for i in range(count) if 0 <= i + by < count]
    return lax.ppermute(value, axis, pairs)


def pair_terms(diag_one, diag_two, cross_one, cross_two, adjoint):
    if adjoint:
        return (diag_one + diag_two, cross_one - cross_two)
    return (diag_one - diag_two, cross_one + cross_two)


def depth_apply(current, pade_ops, adjoint):
    factor_count = pade_ops.shape[0]
    sequence = range(factor_count - 1, -1, -1) if adjoint else range(factor_count)
    for factor in sequence:
        contract = 1 if adjoint else 2
        product = lax.dot_general(
            current,
            pade_ops[factor],
            (((3,), (contract,)), ((), ())),
            preferred_element_type=jnp.float32,
        )
        real_part, imag_part = pair_terms(
            product[0, :, :, 0],
            product[1, :, :, 1],
            product[1, :, :, 0],
            product[0, :, :, 1],
            adjoint,
        )
        current = jnp.stack([real_part, imag_part]).astype(jnp.bfloat16)
    return current


def azimuth_apply(field_in, inverse, adjoint):
    block_width = inverse.shape[1]
    blocked = field_in.reshape(2, field_in.shape[1] // block_width, block_width, field_in.shape[2])
    contract = 1 if adjoint else 2
    product = lax.dot_general(
        inverse, blocked, (((contract,), (2,)), ((), ())), preferred_element_type=jnp.float32
    )
    real_part, imag_part = pair_terms(
        product[0, :, 0], product[1, :, 1], product[0, :, 1], product[1, :, 0], adjoint
    )
    joined = jnp.stack([real_part, imag_part])
    return joined.transpose(0, 2, 1, 3).reshape(field_in.shape)


def numerator_map(field_in):
    return field_in + coupling * (
        jnp.roll(field_in, 1, axis=1) + jnp.roll(field_in, -1, axis=1) - 2.0 * field_in
    )


def screen_phase(profile, bottom_row, depth_start):
    depths = depth_start + jnp.arange(profile.shape[0], dtype=jnp.int32)
    in_water = depths[None, :] < bottom_row[:, None]
    water_phase = phase_scale * (1.0 / (profile * profile) - 1.0)
    return (jnp.where(in_water, water_phase[None, :], bed_phase), in_water)


def depth_segment(field_in, pade_factors, adjoint):
    block_size = pade_factors.shape[3]
    if field_in.shape[2] % block_size == 0:
        worked = depth_apply(
            field_in.reshape(2, field_in.shape[1], field_in.shape[2] // block_size, block_size),
            pade_factors,
            adjoint,
        )
        return worked.reshape(field_in.shape)
    turned = lax.all_to_all(field_in, "line", split_axis=1, concat_axis=2, tiled=True)
    full_depth = turned.shape[2]
    worked = depth_apply(
        turned.reshape(2, turned.shape[1], full_depth // block_size, block_size),
        pade_factors,
        adjoint,
    )
    return lax.all_to_all(
        worked.reshape(turned.shape), "line", split_axis=2, concat_axis=1, tiled=True
    )


def local(
    checkpoint, adjoint_start, misfit, pade_factors, azimuth_inverse, bottom, base_speed, speed_step
):
    depth_rows = checkpoint.shape[3]
    depth_start = lax.axis_index("line") * depth_rows
    every_step = lax.all_gather(speed_step, "range", axis=0, tiled=True)
    running = jnp.cumsum(every_step, axis=0)
    profile = base_speed + lax.dynamic_index_in_dim(
        running, lax.axis_index("range"), 0, keepdims=False
    )
    phase_angle, in_water = screen_phase(profile, bottom[0], depth_start)
    cosine = jnp.cos(phase_angle)
    sine_term = jnp.sin(phase_angle)
    source = checkpoint[0].astype(jnp.float32)
    screened = jnp.stack(
        [cosine * source[0] - sine_term * source[1], sine_term * source[0] + cosine * source[1]]
    ).astype(jnp.bfloat16)
    depth_out = depth_segment(screened, pade_factors, False)
    numerator = numerator_map(depth_out.astype(jnp.float32)).astype(jnp.bfloat16)
    inverse = azimuth_inverse[0]
    field_end = azimuth_apply(numerator, inverse, False).astype(jnp.bfloat16)
    arrival = passed_along(adjoint_start, "range", -1)
    lam_end = (arrival[0].astype(jnp.float32) + misfit[0].astype(jnp.float32)).astype(jnp.bfloat16)
    backward = numerator_map(azimuth_apply(lam_end, inverse, True)).astype(jnp.bfloat16)
    backward = depth_segment(backward, pade_factors, True)
    cotangent = backward.astype(jnp.float32)
    adjoint_begin = jnp.stack(
        [
            cosine * cotangent[0] + sine_term * cotangent[1],
            cosine * cotangent[1] - sine_term * cotangent[0],
        ]
    ).astype(jnp.bfloat16)
    screened_f = screened.astype(jnp.float32)
    weight = jnp.where(in_water, cotangent[1] * screened_f[0] - cotangent[0] * screened_f[1], 0.0)
    grad_here = (
        jnp.sum(weight, axis=0) * (-8.0 / (profile * profile * profile)) / checkpoint.shape[2]
    )[None, :]
    all_grads = lax.all_gather(grad_here, "range", axis=0, tiled=True)
    suffix = jnp.flip(jnp.cumsum(jnp.flip(all_grads, 0), axis=0), 0)
    grad_increment = lax.dynamic_slice_in_dim(suffix, lax.axis_index("range"), 1, 0)
    return (field_end[None], adjoint_begin[None], grad_increment)


def solution(mesh):
    in_specs = (
        P("range", "freq", None, "line"),
        P("range", "freq", None, "line"),
        P("range", "freq", None, "line"),
        P(None, "freq", None, None),
        P("range", "freq", None, None),
        P("range", None),
        P("line"),
        P("range", "line"),
    )
    out_specs = (
        P("range", "freq", None, "line"),
        P("range", "freq", None, "line"),
        P(("freq", "range"), "line"),
    )
    return jax.shard_map(local, mesh=mesh, in_specs=in_specs, out_specs=out_specs, check_vma=False)
```

```python
import jax
import jax.numpy as jnp
from jax import lax
from jax.sharding import PartitionSpec as P
from jax.experimental import pallas as pl
from jax.experimental.pallas import tpu as pltpu

phase_scale = 4.0
bed_phase = -1.8
coupling = 0.3


def passed_along(value, axis, by):
    count = lax.axis_size(axis)
    pairs = [(i, i + by) for i in range(count) if 0 <= i + by < count]
    return lax.ppermute(value, axis, pairs)


def pair_terms(diag_one, diag_two, cross_one, cross_two, adjoint):
    if adjoint:
        return (diag_one + diag_two, cross_one - cross_two)
    return (diag_one - diag_two, cross_one + cross_two)


def depth_apply(current, pade_ops, adjoint):
    factor_count = pade_ops.shape[0]
    sequence = range(factor_count - 1, -1, -1) if adjoint else range(factor_count)
    for factor in sequence:
        contract = 1 if adjoint else 2
        product = lax.dot_general(
            current,
            pade_ops[factor],
            (((3,), (contract,)), ((), ())),
            preferred_element_type=jnp.float32,
        )
        real_part, imag_part = pair_terms(
            product[0, :, :, 0],
            product[1, :, :, 1],
            product[1, :, :, 0],
            product[0, :, :, 1],
            adjoint,
        )
        current = jnp.stack([real_part, imag_part]).astype(jnp.bfloat16)
    return current


def azimuth_apply(field_in, inverse, adjoint):
    block_width = inverse.shape[1]
    blocked = field_in.reshape(2, field_in.shape[1] // block_width, block_width, field_in.shape[2])
    contract = 1 if adjoint else 2
    product = lax.dot_general(
        inverse, blocked, (((contract,), (2,)), ((), ())), preferred_element_type=jnp.float32
    )
    real_part, imag_part = pair_terms(
        product[0, :, 0], product[1, :, 1], product[0, :, 1], product[1, :, 0], adjoint
    )
    joined = jnp.stack([real_part, imag_part])
    return joined.transpose(0, 2, 1, 3).reshape(field_in.shape)


def numerator_map(field_in):
    return field_in + coupling * (
        jnp.roll(field_in, 1, axis=1) + jnp.roll(field_in, -1, axis=1) - 2.0 * field_in
    )


def screen_phase(profile, bottom_row, depth_start):
    depths = depth_start + jnp.arange(profile.shape[0], dtype=jnp.int32)
    in_water = depths[None, :] < bottom_row[:, None]
    water_phase = phase_scale * (1.0 / (profile * profile) - 1.0)
    return (jnp.where(in_water, water_phase[None, :], bed_phase), in_water)


def depth_segment(field_in, pade_factors, adjoint):
    block_size = pade_factors.shape[3]
    if field_in.shape[2] % block_size == 0:
        worked = depth_apply(
            field_in.reshape(2, field_in.shape[1], field_in.shape[2] // block_size, block_size),
            pade_factors,
            adjoint,
        )
        return worked.reshape(field_in.shape)
    turned = lax.all_to_all(field_in, "line", split_axis=1, concat_axis=2, tiled=True)
    full_depth = turned.shape[2]
    worked = depth_apply(
        turned.reshape(2, turned.shape[1], full_depth // block_size, block_size),
        pade_factors,
        adjoint,
    )
    return lax.all_to_all(
        worked.reshape(turned.shape), "line", split_axis=2, concat_axis=1, tiled=True
    )


def general_local(
    checkpoint, adjoint_start, misfit, pade_factors, azimuth_inverse, bottom, base_speed, speed_step
):
    depth_rows = checkpoint.shape[3]
    depth_start = lax.axis_index("line") * depth_rows
    every_step = lax.all_gather(speed_step, "range", axis=0, tiled=True)
    running = jnp.cumsum(every_step, axis=0)
    profile = base_speed + lax.dynamic_index_in_dim(
        running, lax.axis_index("range"), 0, keepdims=False
    )
    phase_angle, in_water = screen_phase(profile, bottom[0], depth_start)
    cosine = jnp.cos(phase_angle)
    sine_term = jnp.sin(phase_angle)
    source = checkpoint[0].astype(jnp.float32)
    screened = jnp.stack(
        [cosine * source[0] - sine_term * source[1], sine_term * source[0] + cosine * source[1]]
    ).astype(jnp.bfloat16)
    depth_out = depth_segment(screened, pade_factors, False)
    numerator = numerator_map(depth_out.astype(jnp.float32)).astype(jnp.bfloat16)
    inverse = azimuth_inverse[0]
    field_end = azimuth_apply(numerator, inverse, False).astype(jnp.bfloat16)
    arrival = passed_along(adjoint_start, "range", -1)
    lam_end = (arrival[0].astype(jnp.float32) + misfit[0].astype(jnp.float32)).astype(jnp.bfloat16)
    backward = numerator_map(azimuth_apply(lam_end, inverse, True)).astype(jnp.bfloat16)
    backward = depth_segment(backward, pade_factors, True)
    cotangent = backward.astype(jnp.float32)
    adjoint_begin = jnp.stack(
        [
            cosine * cotangent[0] + sine_term * cotangent[1],
            cosine * cotangent[1] - sine_term * cotangent[0],
        ]
    ).astype(jnp.bfloat16)
    screened_f = screened.astype(jnp.float32)
    weight = jnp.where(in_water, cotangent[1] * screened_f[0] - cotangent[0] * screened_f[1], 0.0)
    grad_here = (
        jnp.sum(weight, axis=0) * (-8.0 / (profile * profile * profile)) / checkpoint.shape[2]
    )[None, :]
    all_grads = lax.all_gather(grad_here, "range", axis=0, tiled=True)
    suffix = jnp.flip(jnp.cumsum(jnp.flip(all_grads, 0), axis=0), 0)
    grad_increment = lax.dynamic_slice_in_dim(suffix, lax.axis_index("range"), 1, 0)
    return (field_end[None], adjoint_begin[None], grad_increment)


def dot_nt(left, right):
    return lax.dot_general(
        left, right, (((1,), (1,)), ((), ())), preferred_element_type=jnp.float32
    )


def dot_nn(left, right):
    return jnp.dot(left, right, preferred_element_type=jnp.float32)


def numerator_rows(field_in):
    rows = field_in.shape[0]
    return field_in + coupling * (
        pltpu.roll(field_in, 1, 0) + pltpu.roll(field_in, rows - 1, 0) - 2.0 * field_in
    )


def phase_tile(trig_ref, limit_ref, block_index, shape):
    columns = lax.broadcasted_iota(jnp.int32, shape, 1) + block_index * shape[1]
    in_water = columns < limit_ref[...]
    trig = trig_ref[...]
    cosine = jnp.where(in_water, trig[0:1], trig[2:3])
    sine_term = jnp.where(in_water, trig[1:2], trig[3:4])
    return cosine, sine_term, in_water


def screen_tile(source_ref, cosine, sine_term):
    source_r = source_ref[0].astype(jnp.float32)
    source_i = source_ref[1].astype(jnp.float32)
    screened_r = (cosine * source_r - sine_term * source_i).astype(jnp.bfloat16)
    screened_i = (sine_term * source_r + cosine * source_i).astype(jnp.bfloat16)
    return screened_r, screened_i


def forward_kernel(source_ref, trig_ref, limit_ref, pade_ref, inverse_ref, out_ref):
    block_index = pl.program_id(0)
    rows, width = source_ref.shape[1], source_ref.shape[2]
    cosine, sine_term, _ = phase_tile(trig_ref, limit_ref, block_index, (rows, width))
    cur_r, cur_i = screen_tile(source_ref, cosine, sine_term)
    for factor in range(pade_ref.shape[0]):
        pade_r = pade_ref[factor, 0]
        pade_i = pade_ref[factor, 1]
        real_part = dot_nt(cur_r, pade_r) - dot_nt(cur_i, pade_i)
        imag_part = dot_nt(cur_i, pade_r) + dot_nt(cur_r, pade_i)
        cur_r = real_part.astype(jnp.bfloat16)
        cur_i = imag_part.astype(jnp.bfloat16)
    num_r = numerator_rows(cur_r.astype(jnp.float32)).astype(jnp.bfloat16)
    num_i = numerator_rows(cur_i.astype(jnp.float32)).astype(jnp.bfloat16)
    inv_r = inverse_ref[0]
    inv_i = inverse_ref[1]
    block_width = inv_r.shape[0]
    for start in range(0, rows, block_width):
        part_r = num_r[start : start + block_width]
        part_i = num_i[start : start + block_width]
        out_ref[0, start : start + block_width, :] = (
            dot_nn(inv_r, part_r) - dot_nn(inv_i, part_i)
        ).astype(jnp.bfloat16)
        out_ref[1, start : start + block_width, :] = (
            dot_nn(inv_r, part_i) + dot_nn(inv_i, part_r)
        ).astype(jnp.bfloat16)


def make_backward_kernel(block_index):
    def backward_kernel(
        arrival_ref, misfit_ref, source_ref, trig_ref, limit_ref, pade_ref, inverse_t_ref,
        out_ref, grad_ref,
    ):
        rows, width = source_ref.shape[1], source_ref.shape[2]
        lam_r = (
            arrival_ref[0].astype(jnp.float32) + misfit_ref[0].astype(jnp.float32)
        ).astype(jnp.bfloat16)
        lam_i = (
            arrival_ref[1].astype(jnp.float32) + misfit_ref[1].astype(jnp.float32)
        ).astype(jnp.bfloat16)
        inv_r = inverse_t_ref[0]
        inv_i = inverse_t_ref[1]
        block_width = inv_r.shape[0]
        pieces_r = []
        pieces_i = []
        for start in range(0, rows, block_width):
            part_r = lam_r[start : start + block_width]
            part_i = lam_i[start : start + block_width]
            pieces_r.append(dot_nn(inv_r, part_r) + dot_nn(inv_i, part_i))
            pieces_i.append(dot_nn(inv_r, part_i) - dot_nn(inv_i, part_r))
        cur_r = numerator_rows(jnp.concatenate(pieces_r, axis=0)).astype(jnp.bfloat16)
        cur_i = numerator_rows(jnp.concatenate(pieces_i, axis=0)).astype(jnp.bfloat16)
        for factor in range(pade_ref.shape[0] - 1, -1, -1):
            pade_r = pade_ref[factor, 0]
            pade_i = pade_ref[factor, 1]
            real_part = dot_nn(cur_r, pade_r) + dot_nn(cur_i, pade_i)
            imag_part = dot_nn(cur_i, pade_r) - dot_nn(cur_r, pade_i)
            cur_r = real_part.astype(jnp.bfloat16)
            cur_i = imag_part.astype(jnp.bfloat16)
        cot_r = cur_r.astype(jnp.float32)
        cot_i = cur_i.astype(jnp.float32)
        cosine, sine_term, in_water = phase_tile(trig_ref, limit_ref, block_index, (rows, width))
        out_ref[0] = (cosine * cot_r + sine_term * cot_i).astype(jnp.bfloat16)
        out_ref[1] = (cosine * cot_i - sine_term * cot_r).astype(jnp.bfloat16)
        screened_r, screened_i = screen_tile(source_ref, cosine, sine_term)
        weight = jnp.where(
            in_water,
            cot_i * screened_r.astype(jnp.float32) - cot_r * screened_i.astype(jnp.float32),
            0.0,
        )
        grad_ref[...] = jnp.sum(weight, axis=0, keepdims=True)

    return backward_kernel


def fused_local(
    checkpoint, adjoint_start, misfit, pade_factors, azimuth_inverse, bottom, base_speed, speed_step
):
    depth_rows = checkpoint.shape[3]
    rows = checkpoint.shape[2]
    block_size = pade_factors.shape[3]
    block_count = depth_rows // block_size
    depth_start = lax.axis_index("line") * depth_rows
    every_step = lax.all_gather(speed_step, "range", axis=0, tiled=True)
    every_step, adjoint_start = lax.optimization_barrier((every_step, adjoint_start))
    arrivals = [
        passed_along(
            adjoint_start[:, :, :, index * block_size : (index + 1) * block_size], "range", -1
        )
        for index in range(block_count)
    ]
    running = jnp.cumsum(every_step, axis=0)
    profile = base_speed + lax.dynamic_index_in_dim(
        running, lax.axis_index("range"), 0, keepdims=False
    )
    water_phase = phase_scale * (1.0 / (profile * profile) - 1.0)
    bed_row = jnp.full_like(water_phase, bed_phase)
    trig = jnp.stack(
        [jnp.cos(water_phase), jnp.sin(water_phase), jnp.cos(bed_row), jnp.sin(bed_row)]
    )
    limit = (bottom[0] - depth_start)[:, None]
    inverse = azimuth_inverse[0]
    inverse_t = jnp.swapaxes(inverse, 1, 2)
    field_spec = pl.BlockSpec((None, 2, rows, block_size), lambda b: (0, 0, 0, b))
    trig_spec = pl.BlockSpec((4, block_size), lambda b: (0, b))
    limit_spec = pl.BlockSpec((rows, 1), lambda b: (0, 0))
    pade_spec = pl.BlockSpec(pade_factors.shape, lambda b: (0, 0, 0, 0))
    inverse_spec = pl.BlockSpec(inverse.shape, lambda b: (0, 0, 0))
    field_end = pl.pallas_call(
        forward_kernel,
        grid=(block_count,),
        in_specs=[field_spec, trig_spec, limit_spec, pade_spec, inverse_spec],
        out_specs=field_spec,
        out_shape=jax.ShapeDtypeStruct(checkpoint.shape, jnp.bfloat16),
    )(checkpoint, trig, limit, pade_factors, inverse)
    begins = []
    grads = []
    for index in range(block_count):
        fixed = lambda b, index=index: (0, 0, 0, index)
        chunk_spec = pl.BlockSpec((None, 2, rows, block_size), lambda b: (0, 0, 0, 0))
        block_spec = pl.BlockSpec((None, 2, rows, block_size), fixed)
        begin, grad_part = pl.pallas_call(
            make_backward_kernel(index),
            grid=(1,),
            in_specs=[
                chunk_spec,
                block_spec,
                block_spec,
                pl.BlockSpec((4, block_size), lambda b, index=index: (0, index)),
                limit_spec,
                pade_spec,
                inverse_spec,
            ],
            out_specs=[
                chunk_spec,
                pl.BlockSpec((1, block_size), lambda b: (0, 0)),
            ],
            out_shape=[
                jax.ShapeDtypeStruct((1, 2, rows, block_size), jnp.bfloat16),
                jax.ShapeDtypeStruct((1, block_size), jnp.float32),
            ],
        )(arrivals[index], misfit, checkpoint, trig, limit, pade_factors, inverse_t)
        begins.append(begin)
        grads.append(grad_part)
    adjoint_begin = jnp.concatenate(begins, axis=3)
    grad_sum = jnp.concatenate(grads, axis=1)
    grad_here = grad_sum * (-8.0 / (profile * profile * profile)) / rows
    all_grads = lax.all_gather(grad_here, "range", axis=0, tiled=True)
    suffix = jnp.flip(jnp.cumsum(jnp.flip(all_grads, 0), axis=0), 0)
    grad_increment = lax.dynamic_slice_in_dim(suffix, lax.axis_index("range"), 1, 0)
    return (field_end, adjoint_begin, grad_increment)


def local(
    checkpoint, adjoint_start, misfit, pade_factors, azimuth_inverse, bottom, base_speed, speed_step
):
    if checkpoint.shape[3] % pade_factors.shape[3] == 0:
        return fused_local(
            checkpoint, adjoint_start, misfit, pade_factors, azimuth_inverse, bottom,
            base_speed, speed_step,
        )
    return general_local(
        checkpoint, adjoint_start, misfit, pade_factors, azimuth_inverse, bottom,
        base_speed, speed_step,
    )


def solution(mesh):
    in_specs = (
        P("range", "freq", None, "line"),
        P("range", "freq", None, "line"),
        P("range", "freq", None, "line"),
        P(None, "freq", None, None),
        P("range", "freq", None, None),
        P("range", None),
        P("line"),
        P("range", "line"),
    )
    out_specs = (
        P("range", "freq", None, "line"),
        P("range", "freq", None, "line"),
        P(("freq", "range"), "line"),
    )
    return jax.shard_map(local, mesh=mesh, in_specs=in_specs, out_specs=out_specs, check_vma=False)
```

```python
import jax
import jax.numpy as jnp
from jax import lax
from jax.sharding import PartitionSpec as P
from jax.experimental import pallas as pl
from jax.experimental.pallas import tpu as pltpu

phase_scale = 4.0
bed_phase = -1.8
coupling = 0.3


def passed_along(value, axis, by):
    count = lax.axis_size(axis)
    pairs = [(i, i + by) for i in range(count) if 0 <= i + by < count]
    return lax.ppermute(value, axis, pairs)


def pair_terms(diag_one, diag_two, cross_one, cross_two, adjoint):
    if adjoint:
        return (diag_one + diag_two, cross_one - cross_two)
    return (diag_one - diag_two, cross_one + cross_two)


def depth_apply(current, pade_ops, adjoint):
    factor_count = pade_ops.shape[0]
    sequence = range(factor_count - 1, -1, -1) if adjoint else range(factor_count)
    for factor in sequence:
        contract = 1 if adjoint else 2
        product = lax.dot_general(
            current,
            pade_ops[factor],
            (((3,), (contract,)), ((), ())),
            preferred_element_type=jnp.float32,
        )
        real_part, imag_part = pair_terms(
            product[0, :, :, 0],
            product[1, :, :, 1],
            product[1, :, :, 0],
            product[0, :, :, 1],
            adjoint,
        )
        current = jnp.stack([real_part, imag_part]).astype(jnp.bfloat16)
    return current


def azimuth_apply(field_in, inverse, adjoint):
    block_width = inverse.shape[1]
    blocked = field_in.reshape(2, field_in.shape[1] // block_width, block_width, field_in.shape[2])
    contract = 1 if adjoint else 2
    product = lax.dot_general(
        inverse, blocked, (((contract,), (2,)), ((), ())), preferred_element_type=jnp.float32
    )
    real_part, imag_part = pair_terms(
        product[0, :, 0], product[1, :, 1], product[0, :, 1], product[1, :, 0], adjoint
    )
    joined = jnp.stack([real_part, imag_part])
    return joined.transpose(0, 2, 1, 3).reshape(field_in.shape)


def numerator_map(field_in):
    return field_in + coupling * (
        jnp.roll(field_in, 1, axis=1) + jnp.roll(field_in, -1, axis=1) - 2.0 * field_in
    )


def screen_phase(profile, bottom_row, depth_start):
    depths = depth_start + jnp.arange(profile.shape[0], dtype=jnp.int32)
    in_water = depths[None, :] < bottom_row[:, None]
    water_phase = phase_scale * (1.0 / (profile * profile) - 1.0)
    return (jnp.where(in_water, water_phase[None, :], bed_phase), in_water)


def depth_segment(field_in, pade_factors, adjoint):
    block_size = pade_factors.shape[3]
    if field_in.shape[2] % block_size == 0:
        worked = depth_apply(
            field_in.reshape(2, field_in.shape[1], field_in.shape[2] // block_size, block_size),
            pade_factors,
            adjoint,
        )
        return worked.reshape(field_in.shape)
    turned = lax.all_to_all(field_in, "line", split_axis=1, concat_axis=2, tiled=True)
    full_depth = turned.shape[2]
    worked = depth_apply(
        turned.reshape(2, turned.shape[1], full_depth // block_size, block_size),
        pade_factors,
        adjoint,
    )
    return lax.all_to_all(
        worked.reshape(turned.shape), "line", split_axis=2, concat_axis=1, tiled=True
    )


def general_local(
    checkpoint, adjoint_start, misfit, pade_factors, azimuth_inverse, bottom, base_speed, speed_step
):
    depth_rows = checkpoint.shape[3]
    depth_start = lax.axis_index("line") * depth_rows
    every_step = lax.all_gather(speed_step, "range", axis=0, tiled=True)
    running = jnp.cumsum(every_step, axis=0)
    profile = base_speed + lax.dynamic_index_in_dim(
        running, lax.axis_index("range"), 0, keepdims=False
    )
    phase_angle, in_water = screen_phase(profile, bottom[0], depth_start)
    cosine = jnp.cos(phase_angle)
    sine_term = jnp.sin(phase_angle)
    source = checkpoint[0].astype(jnp.float32)
    screened = jnp.stack(
        [cosine * source[0] - sine_term * source[1], sine_term * source[0] + cosine * source[1]]
    ).astype(jnp.bfloat16)
    depth_out = depth_segment(screened, pade_factors, False)
    numerator = numerator_map(depth_out.astype(jnp.float32)).astype(jnp.bfloat16)
    inverse = azimuth_inverse[0]
    field_end = azimuth_apply(numerator, inverse, False).astype(jnp.bfloat16)
    arrival = passed_along(adjoint_start, "range", -1)
    lam_end = (arrival[0].astype(jnp.float32) + misfit[0].astype(jnp.float32)).astype(jnp.bfloat16)
    backward = numerator_map(azimuth_apply(lam_end, inverse, True)).astype(jnp.bfloat16)
    backward = depth_segment(backward, pade_factors, True)
    cotangent = backward.astype(jnp.float32)
    adjoint_begin = jnp.stack(
        [
            cosine * cotangent[0] + sine_term * cotangent[1],
            cosine * cotangent[1] - sine_term * cotangent[0],
        ]
    ).astype(jnp.bfloat16)
    screened_f = screened.astype(jnp.float32)
    weight = jnp.where(in_water, cotangent[1] * screened_f[0] - cotangent[0] * screened_f[1], 0.0)
    grad_here = (
        jnp.sum(weight, axis=0) * (-8.0 / (profile * profile * profile)) / checkpoint.shape[2]
    )[None, :]
    all_grads = lax.all_gather(grad_here, "range", axis=0, tiled=True)
    suffix = jnp.flip(jnp.cumsum(jnp.flip(all_grads, 0), axis=0), 0)
    grad_increment = lax.dynamic_slice_in_dim(suffix, lax.axis_index("range"), 1, 0)
    return (field_end[None], adjoint_begin[None], grad_increment)


def dot_nt(left, right):
    return lax.dot_general(
        left, right, (((1,), (1,)), ((), ())), preferred_element_type=jnp.float32
    )


def dot_nn(left, right):
    return jnp.dot(left, right, preferred_element_type=jnp.float32)


def numerator_rows(field_in):
    rows = field_in.shape[0]
    return field_in + coupling * (
        pltpu.roll(field_in, 1, 0) + pltpu.roll(field_in, rows - 1, 0) - 2.0 * field_in
    )


def phase_tile(trig_ref, limit_ref, block_index, shape):
    columns = lax.broadcasted_iota(jnp.int32, shape, 1) + block_index * shape[1]
    in_water = columns < limit_ref[...]
    trig = trig_ref[...]
    cosine = jnp.where(in_water, trig[0:1], trig[2:3])
    sine_term = jnp.where(in_water, trig[1:2], trig[3:4])
    return cosine, sine_term, in_water


def screen_tile(source_ref, cosine, sine_term):
    source_r = source_ref[0].astype(jnp.float32)
    source_i = source_ref[1].astype(jnp.float32)
    screened_r = (cosine * source_r - sine_term * source_i).astype(jnp.bfloat16)
    screened_i = (sine_term * source_r + cosine * source_i).astype(jnp.bfloat16)
    return screened_r, screened_i


def forward_kernel(source_ref, trig_ref, limit_ref, pade_ref, inverse_ref, out_ref):
    block_index = pl.program_id(0)
    rows, width = source_ref.shape[1], source_ref.shape[2]
    cosine, sine_term, _ = phase_tile(trig_ref, limit_ref, block_index, (rows, width))
    cur_r, cur_i = screen_tile(source_ref, cosine, sine_term)
    for factor in range(pade_ref.shape[0]):
        pade_r = pade_ref[factor, 0]
        pade_i = pade_ref[factor, 1]
        real_part = dot_nt(cur_r, pade_r) - dot_nt(cur_i, pade_i)
        imag_part = dot_nt(cur_i, pade_r) + dot_nt(cur_r, pade_i)
        cur_r = real_part.astype(jnp.bfloat16)
        cur_i = imag_part.astype(jnp.bfloat16)
    num_r = numerator_rows(cur_r.astype(jnp.float32)).astype(jnp.bfloat16)
    num_i = numerator_rows(cur_i.astype(jnp.float32)).astype(jnp.bfloat16)
    inv_r = inverse_ref[0]
    inv_i = inverse_ref[1]
    block_width = inv_r.shape[0]
    for start in range(0, rows, block_width):
        part_r = num_r[start : start + block_width]
        part_i = num_i[start : start + block_width]
        out_ref[0, start : start + block_width, :] = (
            dot_nn(inv_r, part_r) - dot_nn(inv_i, part_i)
        ).astype(jnp.bfloat16)
        out_ref[1, start : start + block_width, :] = (
            dot_nn(inv_r, part_i) + dot_nn(inv_i, part_r)
        ).astype(jnp.bfloat16)


def make_backward_kernel(block_index):
    def backward_kernel(
        arrival_ref, misfit_ref, source_ref, trig_ref, limit_ref, pade_ref, inverse_t_ref,
        out_ref, grad_ref,
    ):
        rows, width = source_ref.shape[1], source_ref.shape[2]
        lam_r = (
            arrival_ref[0].astype(jnp.float32) + misfit_ref[0].astype(jnp.float32)
        ).astype(jnp.bfloat16)
        lam_i = (
            arrival_ref[1].astype(jnp.float32) + misfit_ref[1].astype(jnp.float32)
        ).astype(jnp.bfloat16)
        inv_r = inverse_t_ref[0]
        inv_i = inverse_t_ref[1]
        block_width = inv_r.shape[0]
        pieces_r = []
        pieces_i = []
        for start in range(0, rows, block_width):
            part_r = lam_r[start : start + block_width]
            part_i = lam_i[start : start + block_width]
            pieces_r.append(dot_nn(inv_r, part_r) + dot_nn(inv_i, part_i))
            pieces_i.append(dot_nn(inv_r, part_i) - dot_nn(inv_i, part_r))
        cur_r = numerator_rows(jnp.concatenate(pieces_r, axis=0)).astype(jnp.bfloat16)
        cur_i = numerator_rows(jnp.concatenate(pieces_i, axis=0)).astype(jnp.bfloat16)
        for factor in range(pade_ref.shape[0] - 1, -1, -1):
            pade_r = pade_ref[factor, 0]
            pade_i = pade_ref[factor, 1]
            real_part = dot_nn(cur_r, pade_r) + dot_nn(cur_i, pade_i)
            imag_part = dot_nn(cur_i, pade_r) - dot_nn(cur_r, pade_i)
            cur_r = real_part.astype(jnp.bfloat16)
            cur_i = imag_part.astype(jnp.bfloat16)
        cot_r = cur_r.astype(jnp.float32)
        cot_i = cur_i.astype(jnp.float32)
        cosine, sine_term, in_water = phase_tile(trig_ref, limit_ref, block_index, (rows, width))
        out_ref[0] = (cosine * cot_r + sine_term * cot_i).astype(jnp.bfloat16)
        out_ref[1] = (cosine * cot_i - sine_term * cot_r).astype(jnp.bfloat16)
        screened_r, screened_i = screen_tile(source_ref, cosine, sine_term)
        weight = jnp.where(
            in_water,
            cot_i * screened_r.astype(jnp.float32) - cot_r * screened_i.astype(jnp.float32),
            0.0,
        )
        grad_ref[...] = jnp.sum(weight, axis=0, keepdims=True)

    return backward_kernel


def range_scan(value, direction):
    count = lax.axis_size("range")
    reach = 1
    while reach < count:
        value = value + passed_along(value, "range", direction * reach)
        reach *= 2
    return value


def fused_local(
    checkpoint, adjoint_start, misfit, pade_factors, azimuth_inverse, bottom, base_speed, speed_step
):
    depth_rows = checkpoint.shape[3]
    rows = checkpoint.shape[2]
    block_size = pade_factors.shape[3]
    block_count = depth_rows // block_size
    depth_start = lax.axis_index("line") * depth_rows
    arrivals = [
        passed_along(
            adjoint_start[:, :, :, index * block_size : (index + 1) * block_size], "range", -1
        )
        for index in range(block_count)
    ]
    profile = base_speed + range_scan(speed_step, 1)[0]
    water_phase = phase_scale * (1.0 / (profile * profile) - 1.0)
    bed_row = jnp.full_like(water_phase, bed_phase)
    trig = jnp.stack(
        [jnp.cos(water_phase), jnp.sin(water_phase), jnp.cos(bed_row), jnp.sin(bed_row)]
    )
    limit = (bottom[0] - depth_start)[:, None]
    inverse = azimuth_inverse[0]
    inverse_t = jnp.swapaxes(inverse, 1, 2)
    field_spec = pl.BlockSpec((None, 2, rows, block_size), lambda b: (0, 0, 0, b))
    trig_spec = pl.BlockSpec((4, block_size), lambda b: (0, b))
    limit_spec = pl.BlockSpec((rows, 1), lambda b: (0, 0))
    pade_spec = pl.BlockSpec(pade_factors.shape, lambda b: (0, 0, 0, 0))
    inverse_spec = pl.BlockSpec(inverse.shape, lambda b: (0, 0, 0))
    field_end = pl.pallas_call(
        forward_kernel,
        grid=(block_count,),
        in_specs=[field_spec, trig_spec, limit_spec, pade_spec, inverse_spec],
        out_specs=field_spec,
        out_shape=jax.ShapeDtypeStruct(checkpoint.shape, jnp.bfloat16),
    )(checkpoint, trig, limit, pade_factors, inverse)
    field_end, arrivals[0] = lax.optimization_barrier((field_end, arrivals[0]))
    adjoint_begin = None
    grads = []
    for index in range(block_count):
        fixed = lambda b, index=index: (0, 0, 0, index)
        chunk_spec = pl.BlockSpec((None, 2, rows, block_size), lambda b: (0, 0, 0, 0))
        block_spec = pl.BlockSpec((None, 2, rows, block_size), fixed)
        in_specs = [
            chunk_spec,
            block_spec,
            block_spec,
            pl.BlockSpec((4, block_size), lambda b, index=index: (0, index)),
            limit_spec,
            pade_spec,
            inverse_spec,
        ]
        operands = [arrivals[index], misfit, checkpoint, trig, limit, pade_factors, inverse_t]
        aliases = {}
        kernel = make_backward_kernel(index)
        if adjoint_begin is not None:
            in_specs.append(pl.BlockSpec(memory_space=pl.ANY))
            operands.append(adjoint_begin)
            aliases = {len(operands) - 1: 0}
            kernel = lambda *refs, kernel=kernel: kernel(*refs[:7], *refs[8:])
        adjoint_begin, grad_part = pl.pallas_call(
            kernel,
            grid=(1,),
            in_specs=in_specs,
            out_specs=[
                block_spec,
                pl.BlockSpec((1, block_size), lambda b: (0, 0)),
            ],
            out_shape=[
                jax.ShapeDtypeStruct(checkpoint.shape, jnp.bfloat16),
                jax.ShapeDtypeStruct((1, block_size), jnp.float32),
            ],
            input_output_aliases=aliases,
        )(*operands)
        grads.append(grad_part)
    grad_sum = jnp.concatenate(grads, axis=1)
    grad_here = grad_sum * (-8.0 / (profile * profile * profile)) / rows
    grad_increment = range_scan(grad_here, -1)
    return (field_end, adjoint_begin, grad_increment)


def local(
    checkpoint, adjoint_start, misfit, pade_factors, azimuth_inverse, bottom, base_speed, speed_step
):
    if checkpoint.shape[3] % pade_factors.shape[3] == 0:
        return fused_local(
            checkpoint, adjoint_start, misfit, pade_factors, azimuth_inverse, bottom,
            base_speed, speed_step,
        )
    return general_local(
        checkpoint, adjoint_start, misfit, pade_factors, azimuth_inverse, bottom,
        base_speed, speed_step,
    )


def solution(mesh):
    in_specs = (
        P("range", "freq", None, "line"),
        P("range", "freq", None, "line"),
        P("range", "freq", None, "line"),
        P(None, "freq", None, None),
        P("range", "freq", None, None),
        P("range", None),
        P("line"),
        P("range", "line"),
    )
    out_specs = (
        P("range", "freq", None, "line"),
        P("range", "freq", None, "line"),
        P(("freq", "range"), "line"),
    )
    return jax.shard_map(local, mesh=mesh, in_specs=in_specs, out_specs=out_specs, check_vma=False)
```

```python
import jax
import jax.numpy as jnp
from jax import lax
from jax.sharding import PartitionSpec as P
from jax.experimental import pallas as pl
from jax.experimental.pallas import tpu as pltpu

phase_scale = 4.0
bed_phase = -1.8
coupling = 0.3


def passed_along(value, axis, by):
    count = lax.axis_size(axis)
    pairs = [(i, i + by) for i in range(count) if 0 <= i + by < count]
    return lax.ppermute(value, axis, pairs)


def pair_terms(diag_one, diag_two, cross_one, cross_two, adjoint):
    if adjoint:
        return (diag_one + diag_two, cross_one - cross_two)
    return (diag_one - diag_two, cross_one + cross_two)


def depth_apply(current, pade_ops, adjoint):
    factor_count = pade_ops.shape[0]
    sequence = range(factor_count - 1, -1, -1) if adjoint else range(factor_count)
    for factor in sequence:
        contract = 1 if adjoint else 2
        product = lax.dot_general(
            current,
            pade_ops[factor],
            (((3,), (contract,)), ((), ())),
            preferred_element_type=jnp.float32,
        )
        real_part, imag_part = pair_terms(
            product[0, :, :, 0],
            product[1, :, :, 1],
            product[1, :, :, 0],
            product[0, :, :, 1],
            adjoint,
        )
        current = jnp.stack([real_part, imag_part]).astype(jnp.bfloat16)
    return current


def azimuth_apply(field_in, inverse, adjoint):
    block_width = inverse.shape[1]
    blocked = field_in.reshape(2, field_in.shape[1] // block_width, block_width, field_in.shape[2])
    contract = 1 if adjoint else 2
    product = lax.dot_general(
        inverse, blocked, (((contract,), (2,)), ((), ())), preferred_element_type=jnp.float32
    )
    real_part, imag_part = pair_terms(
        product[0, :, 0], product[1, :, 1], product[0, :, 1], product[1, :, 0], adjoint
    )
    joined = jnp.stack([real_part, imag_part])
    return joined.transpose(0, 2, 1, 3).reshape(field_in.shape)


def numerator_map(field_in):
    return field_in + coupling * (
        jnp.roll(field_in, 1, axis=1) + jnp.roll(field_in, -1, axis=1) - 2.0 * field_in
    )


def screen_phase(profile, bottom_row, depth_start):
    depths = depth_start + jnp.arange(profile.shape[0], dtype=jnp.int32)
    in_water = depths[None, :] < bottom_row[:, None]
    water_phase = phase_scale * (1.0 / (profile * profile) - 1.0)
    return (jnp.where(in_water, water_phase[None, :], bed_phase), in_water)


def depth_segment(field_in, pade_factors, adjoint):
    block_size = pade_factors.shape[3]
    if field_in.shape[2] % block_size == 0:
        worked = depth_apply(
            field_in.reshape(2, field_in.shape[1], field_in.shape[2] // block_size, block_size),
            pade_factors,
            adjoint,
        )
        return worked.reshape(field_in.shape)
    turned = lax.all_to_all(field_in, "line", split_axis=1, concat_axis=2, tiled=True)
    full_depth = turned.shape[2]
    worked = depth_apply(
        turned.reshape(2, turned.shape[1], full_depth // block_size, block_size),
        pade_factors,
        adjoint,
    )
    return lax.all_to_all(
        worked.reshape(turned.shape), "line", split_axis=2, concat_axis=1, tiled=True
    )


def general_local(
    checkpoint, adjoint_start, misfit, pade_factors, azimuth_inverse, bottom, base_speed, speed_step
):
    depth_rows = checkpoint.shape[3]
    depth_start = lax.axis_index("line") * depth_rows
    every_step = lax.all_gather(speed_step, "range", axis=0, tiled=True)
    running = jnp.cumsum(every_step, axis=0)
    profile = base_speed + lax.dynamic_index_in_dim(
        running, lax.axis_index("range"), 0, keepdims=False
    )
    phase_angle, in_water = screen_phase(profile, bottom[0], depth_start)
    cosine = jnp.cos(phase_angle)
    sine_term = jnp.sin(phase_angle)
    source = checkpoint[0].astype(jnp.float32)
    screened = jnp.stack(
        [cosine * source[0] - sine_term * source[1], sine_term * source[0] + cosine * source[1]]
    ).astype(jnp.bfloat16)
    depth_out = depth_segment(screened, pade_factors, False)
    numerator = numerator_map(depth_out.astype(jnp.float32)).astype(jnp.bfloat16)
    inverse = azimuth_inverse[0]
    field_end = azimuth_apply(numerator, inverse, False).astype(jnp.bfloat16)
    arrival = passed_along(adjoint_start, "range", -1)
    lam_end = (arrival[0].astype(jnp.float32) + misfit[0].astype(jnp.float32)).astype(jnp.bfloat16)
    backward = numerator_map(azimuth_apply(lam_end, inverse, True)).astype(jnp.bfloat16)
    backward = depth_segment(backward, pade_factors, True)
    cotangent = backward.astype(jnp.float32)
    adjoint_begin = jnp.stack(
        [
            cosine * cotangent[0] + sine_term * cotangent[1],
            cosine * cotangent[1] - sine_term * cotangent[0],
        ]
    ).astype(jnp.bfloat16)
    screened_f = screened.astype(jnp.float32)
    weight = jnp.where(in_water, cotangent[1] * screened_f[0] - cotangent[0] * screened_f[1], 0.0)
    grad_here = (
        jnp.sum(weight, axis=0) * (-8.0 / (profile * profile * profile)) / checkpoint.shape[2]
    )[None, :]
    all_grads = lax.all_gather(grad_here, "range", axis=0, tiled=True)
    suffix = jnp.flip(jnp.cumsum(jnp.flip(all_grads, 0), axis=0), 0)
    grad_increment = lax.dynamic_slice_in_dim(suffix, lax.axis_index("range"), 1, 0)
    return (field_end[None], adjoint_begin[None], grad_increment)


def dot_nt(left, right):
    return lax.dot_general(
        left, right, (((1,), (1,)), ((), ())), preferred_element_type=jnp.float32
    )


def dot_nn(left, right):
    return jnp.dot(left, right, preferred_element_type=jnp.float32)


def numerator_rows(field_in):
    rows = field_in.shape[0]
    return field_in + coupling * (
        pltpu.roll(field_in, 1, 0) + pltpu.roll(field_in, rows - 1, 0) - 2.0 * field_in
    )


def phase_tile(trig_ref, limit_ref, block_index, shape):
    columns = lax.broadcasted_iota(jnp.int32, shape, 1) + block_index * shape[1]
    in_water = columns < limit_ref[...]
    trig = trig_ref[...]
    cosine = jnp.where(in_water, trig[0:1], trig[2:3])
    sine_term = jnp.where(in_water, trig[1:2], trig[3:4])
    return cosine, sine_term, in_water


def screen_tile(source_ref, cosine, sine_term):
    source_r = source_ref[0].astype(jnp.float32)
    source_i = source_ref[1].astype(jnp.float32)
    screened_r = (cosine * source_r - sine_term * source_i).astype(jnp.bfloat16)
    screened_i = (sine_term * source_r + cosine * source_i).astype(jnp.bfloat16)
    return screened_r, screened_i


def forward_kernel(source_ref, trig_ref, limit_ref, pade_ref, inverse_ref, out_ref):
    block_index = pl.program_id(0)
    rows, width = source_ref.shape[1], source_ref.shape[2]
    cosine, sine_term, _ = phase_tile(trig_ref, limit_ref, block_index, (rows, width))
    cur_r, cur_i = screen_tile(source_ref, cosine, sine_term)
    for factor in range(pade_ref.shape[0]):
        pade_r = pade_ref[factor, 0]
        pade_i = pade_ref[factor, 1]
        real_part = dot_nt(cur_r, pade_r) - dot_nt(cur_i, pade_i)
        imag_part = dot_nt(cur_i, pade_r) + dot_nt(cur_r, pade_i)
        cur_r = real_part.astype(jnp.bfloat16)
        cur_i = imag_part.astype(jnp.bfloat16)
    num_r = numerator_rows(cur_r.astype(jnp.float32)).astype(jnp.bfloat16)
    num_i = numerator_rows(cur_i.astype(jnp.float32)).astype(jnp.bfloat16)
    inv_r = inverse_ref[0]
    inv_i = inverse_ref[1]
    block_width = inv_r.shape[0]
    for start in range(0, rows, block_width):
        part_r = num_r[start : start + block_width]
        part_i = num_i[start : start + block_width]
        out_ref[0, start : start + block_width, :] = (
            dot_nn(inv_r, part_r) - dot_nn(inv_i, part_i)
        ).astype(jnp.bfloat16)
        out_ref[1, start : start + block_width, :] = (
            dot_nn(inv_r, part_i) + dot_nn(inv_i, part_r)
        ).astype(jnp.bfloat16)


def make_backward_kernel(block_index):
    def backward_kernel(
        arrival_ref, misfit_ref, source_ref, trig_ref, limit_ref, pade_ref, inverse_t_ref,
        out_ref, grad_ref,
    ):
        rows, width = source_ref.shape[1], source_ref.shape[2]
        lam_r = (
            arrival_ref[0].astype(jnp.float32) + misfit_ref[0].astype(jnp.float32)
        ).astype(jnp.bfloat16)
        lam_i = (
            arrival_ref[1].astype(jnp.float32) + misfit_ref[1].astype(jnp.float32)
        ).astype(jnp.bfloat16)
        inv_r = inverse_t_ref[0]
        inv_i = inverse_t_ref[1]
        block_width = inv_r.shape[0]
        pieces_r = []
        pieces_i = []
        for start in range(0, rows, block_width):
            part_r = lam_r[start : start + block_width]
            part_i = lam_i[start : start + block_width]
            pieces_r.append(dot_nn(inv_r, part_r) + dot_nn(inv_i, part_i))
            pieces_i.append(dot_nn(inv_r, part_i) - dot_nn(inv_i, part_r))
        cur_r = numerator_rows(jnp.concatenate(pieces_r, axis=0)).astype(jnp.bfloat16)
        cur_i = numerator_rows(jnp.concatenate(pieces_i, axis=0)).astype(jnp.bfloat16)
        for factor in range(pade_ref.shape[0] - 1, -1, -1):
            pade_r = pade_ref[factor, 0]
            pade_i = pade_ref[factor, 1]
            real_part = dot_nn(cur_r, pade_r) + dot_nn(cur_i, pade_i)
            imag_part = dot_nn(cur_i, pade_r) - dot_nn(cur_r, pade_i)
            cur_r = real_part.astype(jnp.bfloat16)
            cur_i = imag_part.astype(jnp.bfloat16)
        cot_r = cur_r.astype(jnp.float32)
        cot_i = cur_i.astype(jnp.float32)
        cosine, sine_term, in_water = phase_tile(trig_ref, limit_ref, block_index, (rows, width))
        out_ref[0] = (cosine * cot_r + sine_term * cot_i).astype(jnp.bfloat16)
        out_ref[1] = (cosine * cot_i - sine_term * cot_r).astype(jnp.bfloat16)
        screened_r, screened_i = screen_tile(source_ref, cosine, sine_term)
        weight = jnp.where(
            in_water,
            cot_i * screened_r.astype(jnp.float32) - cot_r * screened_i.astype(jnp.float32),
            0.0,
        )
        grad_ref[...] = jnp.sum(weight, axis=0, keepdims=True)

    return backward_kernel


def range_scan(value, direction):
    count = lax.axis_size("range")
    total = value
    for reach in range(1, count):
        total = total + passed_along(value, "range", direction * reach)
    return total


def fused_local(
    checkpoint, adjoint_start, misfit, pade_factors, azimuth_inverse, bottom, base_speed, speed_step
):
    depth_rows = checkpoint.shape[3]
    rows = checkpoint.shape[2]
    block_size = pade_factors.shape[3]
    block_count = depth_rows // block_size
    depth_start = lax.axis_index("line") * depth_rows
    arrivals = [
        passed_along(
            adjoint_start[:, :, :, index * block_size : (index + 1) * block_size], "range", -1
        )
        for index in range(block_count)
    ]
    profile = base_speed + range_scan(speed_step, 1)[0]
    water_phase = phase_scale * (1.0 / (profile * profile) - 1.0)
    bed_row = jnp.full_like(water_phase, bed_phase)
    trig = jnp.stack(
        [jnp.cos(water_phase), jnp.sin(water_phase), jnp.cos(bed_row), jnp.sin(bed_row)]
    )
    limit = (bottom[0] - depth_start)[:, None]
    inverse = azimuth_inverse[0]
    inverse_t = jnp.swapaxes(inverse, 1, 2)
    field_spec = pl.BlockSpec((None, 2, rows, block_size), lambda b: (0, 0, 0, b))
    trig_spec = pl.BlockSpec((4, block_size), lambda b: (0, b))
    limit_spec = pl.BlockSpec((rows, 1), lambda b: (0, 0))
    pade_spec = pl.BlockSpec(pade_factors.shape, lambda b: (0, 0, 0, 0))
    inverse_spec = pl.BlockSpec(inverse.shape, lambda b: (0, 0, 0))
    field_end = pl.pallas_call(
        forward_kernel,
        grid=(block_count,),
        in_specs=[field_spec, trig_spec, limit_spec, pade_spec, inverse_spec],
        out_specs=field_spec,
        out_shape=jax.ShapeDtypeStruct(checkpoint.shape, jnp.bfloat16),
    )(checkpoint, trig, limit, pade_factors, inverse)
    field_end, arrivals[0] = lax.optimization_barrier((field_end, arrivals[0]))
    adjoint_begin = None
    grads = []
    for index in range(block_count):
        fixed = lambda b, index=index: (0, 0, 0, index)
        chunk_spec = pl.BlockSpec((None, 2, rows, block_size), lambda b: (0, 0, 0, 0))
        block_spec = pl.BlockSpec((None, 2, rows, block_size), fixed)
        in_specs = [
            chunk_spec,
            block_spec,
            block_spec,
            pl.BlockSpec((4, block_size), lambda b, index=index: (0, index)),
            limit_spec,
            pade_spec,
            inverse_spec,
        ]
        operands = [arrivals[index], misfit, checkpoint, trig, limit, pade_factors, inverse_t]
        aliases = {}
        kernel = make_backward_kernel(index)
        if adjoint_begin is not None:
            in_specs.append(pl.BlockSpec(memory_space=pl.ANY))
            operands.append(adjoint_begin)
            aliases = {len(operands) - 1: 0}
            kernel = lambda *refs, kernel=kernel: kernel(*refs[:7], *refs[8:])
        adjoint_begin, grad_part = pl.pallas_call(
            kernel,
            grid=(1,),
            in_specs=in_specs,
            out_specs=[
                block_spec,
                pl.BlockSpec((1, block_size), lambda b: (0, 0)),
            ],
            out_shape=[
                jax.ShapeDtypeStruct(checkpoint.shape, jnp.bfloat16),
                jax.ShapeDtypeStruct((1, block_size), jnp.float32),
            ],
            input_output_aliases=aliases,
        )(*operands)
        grads.append(grad_part)
    grad_sum = jnp.concatenate(grads, axis=1)
    grad_here = grad_sum * (-8.0 / (profile * profile * profile)) / rows
    grad_increment = range_scan(grad_here, -1)
    return (field_end, adjoint_begin, grad_increment)


def local(
    checkpoint, adjoint_start, misfit, pade_factors, azimuth_inverse, bottom, base_speed, speed_step
):
    if checkpoint.shape[3] % pade_factors.shape[3] == 0:
        return fused_local(
            checkpoint, adjoint_start, misfit, pade_factors, azimuth_inverse, bottom,
            base_speed, speed_step,
        )
    return general_local(
        checkpoint, adjoint_start, misfit, pade_factors, azimuth_inverse, bottom,
        base_speed, speed_step,
    )


def solution(mesh):
    in_specs = (
        P("range", "freq", None, "line"),
        P("range", "freq", None, "line"),
        P("range", "freq", None, "line"),
        P(None, "freq", None, None),
        P("range", "freq", None, None),
        P("range", None),
        P("line"),
        P("range", "line"),
    )
    out_specs = (
        P("range", "freq", None, "line"),
        P("range", "freq", None, "line"),
        P(("freq", "range"), "line"),
    )
    return jax.shard_map(local, mesh=mesh, in_specs=in_specs, out_specs=out_specs, check_vma=False)
```

```python
import jax
import jax.numpy as jnp
from jax import lax
from jax.sharding import PartitionSpec as P
from jax.experimental import pallas as pl
from jax.experimental.pallas import tpu as pltpu

phase_scale = 4.0
bed_phase = -1.8
coupling = 0.3


def passed_along(value, axis, by):
    count = lax.axis_size(axis)
    pairs = [(i, i + by) for i in range(count) if 0 <= i + by < count]
    return lax.ppermute(value, axis, pairs)


def pair_terms(diag_one, diag_two, cross_one, cross_two, adjoint):
    if adjoint:
        return (diag_one + diag_two, cross_one - cross_two)
    return (diag_one - diag_two, cross_one + cross_two)


def depth_apply(current, pade_ops, adjoint):
    factor_count = pade_ops.shape[0]
    sequence = range(factor_count - 1, -1, -1) if adjoint else range(factor_count)
    for factor in sequence:
        contract = 1 if adjoint else 2
        product = lax.dot_general(
            current,
            pade_ops[factor],
            (((3,), (contract,)), ((), ())),
            preferred_element_type=jnp.float32,
        )
        real_part, imag_part = pair_terms(
            product[0, :, :, 0],
            product[1, :, :, 1],
            product[1, :, :, 0],
            product[0, :, :, 1],
            adjoint,
        )
        current = jnp.stack([real_part, imag_part]).astype(jnp.bfloat16)
    return current


def azimuth_apply(field_in, inverse, adjoint):
    block_width = inverse.shape[1]
    blocked = field_in.reshape(2, field_in.shape[1] // block_width, block_width, field_in.shape[2])
    contract = 1 if adjoint else 2
    product = lax.dot_general(
        inverse, blocked, (((contract,), (2,)), ((), ())), preferred_element_type=jnp.float32
    )
    real_part, imag_part = pair_terms(
        product[0, :, 0], product[1, :, 1], product[0, :, 1], product[1, :, 0], adjoint
    )
    joined = jnp.stack([real_part, imag_part])
    return joined.transpose(0, 2, 1, 3).reshape(field_in.shape)


def numerator_map(field_in):
    return field_in + coupling * (
        jnp.roll(field_in, 1, axis=1) + jnp.roll(field_in, -1, axis=1) - 2.0 * field_in
    )


def screen_phase(profile, bottom_row, depth_start):
    depths = depth_start + jnp.arange(profile.shape[0], dtype=jnp.int32)
    in_water = depths[None, :] < bottom_row[:, None]
    water_phase = phase_scale * (1.0 / (profile * profile) - 1.0)
    return (jnp.where(in_water, water_phase[None, :], bed_phase), in_water)


def depth_segment(field_in, pade_factors, adjoint):
    block_size = pade_factors.shape[3]
    if field_in.shape[2] % block_size == 0:
        worked = depth_apply(
            field_in.reshape(2, field_in.shape[1], field_in.shape[2] // block_size, block_size),
            pade_factors,
            adjoint,
        )
        return worked.reshape(field_in.shape)
    turned = lax.all_to_all(field_in, "line", split_axis=1, concat_axis=2, tiled=True)
    full_depth = turned.shape[2]
    worked = depth_apply(
        turned.reshape(2, turned.shape[1], full_depth // block_size, block_size),
        pade_factors,
        adjoint,
    )
    return lax.all_to_all(
        worked.reshape(turned.shape), "line", split_axis=2, concat_axis=1, tiled=True
    )


def general_local(
    checkpoint, adjoint_start, misfit, pade_factors, azimuth_inverse, bottom, base_speed, speed_step
):
    depth_rows = checkpoint.shape[3]
    depth_start = lax.axis_index("line") * depth_rows
    every_step = lax.all_gather(speed_step, "range", axis=0, tiled=True)
    running = jnp.cumsum(every_step, axis=0)
    profile = base_speed + lax.dynamic_index_in_dim(
        running, lax.axis_index("range"), 0, keepdims=False
    )
    phase_angle, in_water = screen_phase(profile, bottom[0], depth_start)
    cosine = jnp.cos(phase_angle)
    sine_term = jnp.sin(phase_angle)
    source = checkpoint[0].astype(jnp.float32)
    screened = jnp.stack(
        [cosine * source[0] - sine_term * source[1], sine_term * source[0] + cosine * source[1]]
    ).astype(jnp.bfloat16)
    depth_out = depth_segment(screened, pade_factors, False)
    numerator = numerator_map(depth_out.astype(jnp.float32)).astype(jnp.bfloat16)
    inverse = azimuth_inverse[0]
    field_end = azimuth_apply(numerator, inverse, False).astype(jnp.bfloat16)
    arrival = passed_along(adjoint_start, "range", -1)
    lam_end = (arrival[0].astype(jnp.float32) + misfit[0].astype(jnp.float32)).astype(jnp.bfloat16)
    backward = numerator_map(azimuth_apply(lam_end, inverse, True)).astype(jnp.bfloat16)
    backward = depth_segment(backward, pade_factors, True)
    cotangent = backward.astype(jnp.float32)
    adjoint_begin = jnp.stack(
        [
            cosine * cotangent[0] + sine_term * cotangent[1],
            cosine * cotangent[1] - sine_term * cotangent[0],
        ]
    ).astype(jnp.bfloat16)
    screened_f = screened.astype(jnp.float32)
    weight = jnp.where(in_water, cotangent[1] * screened_f[0] - cotangent[0] * screened_f[1], 0.0)
    grad_here = (
        jnp.sum(weight, axis=0) * (-8.0 / (profile * profile * profile)) / checkpoint.shape[2]
    )[None, :]
    all_grads = lax.all_gather(grad_here, "range", axis=0, tiled=True)
    suffix = jnp.flip(jnp.cumsum(jnp.flip(all_grads, 0), axis=0), 0)
    grad_increment = lax.dynamic_slice_in_dim(suffix, lax.axis_index("range"), 1, 0)
    return (field_end[None], adjoint_begin[None], grad_increment)


def dot_nt(left, right):
    return lax.dot_general(
        left, right, (((1,), (1,)), ((), ())), preferred_element_type=jnp.float32
    )


def dot_nn(left, right):
    return jnp.dot(left, right, preferred_element_type=jnp.float32)


def numerator_rows(field_in):
    rows = field_in.shape[0]
    return field_in + coupling * (
        pltpu.roll(field_in, 1, 0) + pltpu.roll(field_in, rows - 1, 0) - 2.0 * field_in
    )


def phase_tile(trig_ref, limit_ref, block_index, shape):
    columns = lax.broadcasted_iota(jnp.int32, shape, 1) + block_index * shape[1]
    in_water = columns < limit_ref[...]
    trig = trig_ref[...]
    cosine = jnp.where(in_water, trig[0:1], trig[2:3])
    sine_term = jnp.where(in_water, trig[1:2], trig[3:4])
    return cosine, sine_term, in_water


def screen_tile(source_ref, cosine, sine_term):
    source_r = source_ref[0].astype(jnp.float32)
    source_i = source_ref[1].astype(jnp.float32)
    screened_r = (cosine * source_r - sine_term * source_i).astype(jnp.bfloat16)
    screened_i = (sine_term * source_r + cosine * source_i).astype(jnp.bfloat16)
    return screened_r, screened_i


def forward_kernel(source_ref, trig_ref, limit_ref, weight_ref, inverse_ref, out_ref):
    block_index = pl.program_id(0)
    rows, width = source_ref.shape[1], source_ref.shape[2]
    cosine, sine_term, _ = phase_tile(trig_ref, limit_ref, block_index, (rows, width))
    screened_r, screened_i = screen_tile(source_ref, cosine, sine_term)
    state = jnp.concatenate([screened_r, screened_i], axis=1)
    for factor in range(weight_ref.shape[0]):
        state = dot_nn(state, weight_ref[factor]).astype(jnp.bfloat16)
    numerator = numerator_rows(state.astype(jnp.float32)).astype(jnp.bfloat16)
    inv_r = inverse_ref[0]
    inv_i = inverse_ref[1]
    block_width = inv_r.shape[0]
    for start in range(0, rows, block_width):
        part = numerator[start : start + block_width]
        real_side = dot_nn(inv_r, part)
        imag_side = dot_nn(inv_i, part)
        out_ref[0, start : start + block_width, :] = (
            real_side[:, :width] - imag_side[:, width:]
        ).astype(jnp.bfloat16)
        out_ref[1, start : start + block_width, :] = (
            real_side[:, width:] + imag_side[:, :width]
        ).astype(jnp.bfloat16)


def make_backward_kernel(block_index):
    def backward_kernel(
        arrival_ref, misfit_ref, source_ref, trig_ref, limit_ref, weight_ref, inverse_t_ref,
        out_ref, grad_ref,
    ):
        rows, width = source_ref.shape[1], source_ref.shape[2]
        lam_r = (
            arrival_ref[0].astype(jnp.float32) + misfit_ref[0].astype(jnp.float32)
        ).astype(jnp.bfloat16)
        lam_i = (
            arrival_ref[1].astype(jnp.float32) + misfit_ref[1].astype(jnp.float32)
        ).astype(jnp.bfloat16)
        lam = jnp.concatenate([lam_r, lam_i], axis=1)
        inv_r = inverse_t_ref[0]
        inv_i = inverse_t_ref[1]
        block_width = inv_r.shape[0]
        pieces = []
        for start in range(0, rows, block_width):
            part = lam[start : start + block_width]
            real_side = dot_nn(inv_r, part)
            imag_side = dot_nn(inv_i, part)
            pieces.append(
                jnp.concatenate(
                    [
                        real_side[:, :width] + imag_side[:, width:],
                        real_side[:, width:] - imag_side[:, :width],
                    ],
                    axis=1,
                )
            )
        state = numerator_rows(jnp.concatenate(pieces, axis=0)).astype(jnp.bfloat16)
        for factor in range(weight_ref.shape[0] - 1, -1, -1):
            state = dot_nn(state, weight_ref[factor]).astype(jnp.bfloat16)
        cot_r = state[:, :width].astype(jnp.float32)
        cot_i = state[:, width:].astype(jnp.float32)
        cosine, sine_term, in_water = phase_tile(trig_ref, limit_ref, block_index, (rows, width))
        out_ref[0] = (cosine * cot_r + sine_term * cot_i).astype(jnp.bfloat16)
        out_ref[1] = (cosine * cot_i - sine_term * cot_r).astype(jnp.bfloat16)
        screened_r, screened_i = screen_tile(source_ref, cosine, sine_term)
        weight = jnp.where(
            in_water,
            cot_i * screened_r.astype(jnp.float32) - cot_r * screened_i.astype(jnp.float32),
            0.0,
        )
        grad_ref[...] = jnp.sum(weight, axis=0, keepdims=True)

    return backward_kernel


def complex_blocks(real_part, imag_part):
    top = jnp.concatenate([real_part, -imag_part], axis=-1)
    bottom = jnp.concatenate([imag_part, real_part], axis=-1)
    return jnp.concatenate([top, bottom], axis=-2)


def range_scan(value, direction):
    count = lax.axis_size("range")
    total = value
    for reach in range(1, count):
        total = total + passed_along(value, "range", direction * reach)
    return total


def fused_local(
    checkpoint, adjoint_start, misfit, pade_factors, azimuth_inverse, bottom, base_speed, speed_step
):
    depth_rows = checkpoint.shape[3]
    rows = checkpoint.shape[2]
    block_size = pade_factors.shape[3]
    block_count = depth_rows // block_size
    depth_start = lax.axis_index("line") * depth_rows
    arrivals = [
        passed_along(
            adjoint_start[:, :, :, index * block_size : (index + 1) * block_size], "range", -1
        )
        for index in range(block_count)
    ]
    profile = base_speed + range_scan(speed_step, 1)[0]
    water_phase = phase_scale * (1.0 / (profile * profile) - 1.0)
    bed_row = jnp.full_like(water_phase, bed_phase)
    trig = jnp.stack(
        [jnp.cos(water_phase), jnp.sin(water_phase), jnp.cos(bed_row), jnp.sin(bed_row)]
    )
    limit = (bottom[0] - depth_start)[:, None]
    inverse = azimuth_inverse[0]
    inverse_t = jnp.swapaxes(inverse, 1, 2)
    pade_t = jnp.swapaxes(pade_factors, 2, 3)
    forward_weights = complex_blocks(pade_t[:, 0], -pade_t[:, 1])
    backward_weights = complex_blocks(pade_factors[:, 0], pade_factors[:, 1])
    field_spec = pl.BlockSpec((None, 2, rows, block_size), lambda b: (0, 0, 0, b))
    trig_spec = pl.BlockSpec((4, block_size), lambda b: (0, b))
    limit_spec = pl.BlockSpec((rows, 1), lambda b: (0, 0))
    pade_spec = pl.BlockSpec(forward_weights.shape, lambda b: (0, 0, 0))
    inverse_spec = pl.BlockSpec(inverse.shape, lambda b: (0, 0, 0))
    field_end = pl.pallas_call(
        forward_kernel,
        grid=(block_count,),
        in_specs=[field_spec, trig_spec, limit_spec, pade_spec, inverse_spec],
        out_specs=field_spec,
        out_shape=jax.ShapeDtypeStruct(checkpoint.shape, jnp.bfloat16),
    )(checkpoint, trig, limit, forward_weights, inverse)
    field_end, arrivals[0] = lax.optimization_barrier((field_end, arrivals[0]))
    adjoint_begin = None
    grads = []
    for index in range(block_count):
        fixed = lambda b, index=index: (0, 0, 0, index)
        chunk_spec = pl.BlockSpec((None, 2, rows, block_size), lambda b: (0, 0, 0, 0))
        block_spec = pl.BlockSpec((None, 2, rows, block_size), fixed)
        in_specs = [
            chunk_spec,
            block_spec,
            block_spec,
            pl.BlockSpec((4, block_size), lambda b, index=index: (0, index)),
            limit_spec,
            pade_spec,
            inverse_spec,
        ]
        operands = [arrivals[index], misfit, checkpoint, trig, limit, backward_weights, inverse_t]
        aliases = {}
        kernel = make_backward_kernel(index)
        if adjoint_begin is not None:
            in_specs.append(pl.BlockSpec(memory_space=pl.ANY))
            operands.append(adjoint_begin)
            aliases = {len(operands) - 1: 0}
            kernel = lambda *refs, kernel=kernel: kernel(*refs[:7], *refs[8:])
        adjoint_begin, grad_part = pl.pallas_call(
            kernel,
            grid=(1,),
            in_specs=in_specs,
            out_specs=[
                block_spec,
                pl.BlockSpec((1, block_size), lambda b: (0, 0)),
            ],
            out_shape=[
                jax.ShapeDtypeStruct(checkpoint.shape, jnp.bfloat16),
                jax.ShapeDtypeStruct((1, block_size), jnp.float32),
            ],
            input_output_aliases=aliases,
        )(*operands)
        grads.append(grad_part)
    grad_sum = jnp.concatenate(grads, axis=1)
    grad_here = grad_sum * (-8.0 / (profile * profile * profile)) / rows
    grad_increment = range_scan(grad_here, -1)
    return (field_end, adjoint_begin, grad_increment)


def local(
    checkpoint, adjoint_start, misfit, pade_factors, azimuth_inverse, bottom, base_speed, speed_step
):
    if checkpoint.shape[3] % pade_factors.shape[3] == 0:
        return fused_local(
            checkpoint, adjoint_start, misfit, pade_factors, azimuth_inverse, bottom,
            base_speed, speed_step,
        )
    return general_local(
        checkpoint, adjoint_start, misfit, pade_factors, azimuth_inverse, bottom,
        base_speed, speed_step,
    )


def solution(mesh):
    in_specs = (
        P("range", "freq", None, "line"),
        P("range", "freq", None, "line"),
        P("range", "freq", None, "line"),
        P(None, "freq", None, None),
        P("range", "freq", None, None),
        P("range", None),
        P("line"),
        P("range", "line"),
    )
    out_specs = (
        P("range", "freq", None, "line"),
        P("range", "freq", None, "line"),
        P(("freq", "range"), "line"),
    )
    return jax.shard_map(local, mesh=mesh, in_specs=in_specs, out_specs=out_specs, check_vma=False)
```

```python
import jax
import jax.numpy as jnp
from jax import lax
from jax.sharding import PartitionSpec as P
from jax.experimental import pallas as pl
from jax.experimental.pallas import tpu as pltpu

phase_scale = 4.0
bed_phase = -1.8
coupling = 0.3


def passed_along(value, axis, by):
    count = lax.axis_size(axis)
    pairs = [(i, i + by) for i in range(count) if 0 <= i + by < count]
    return lax.ppermute(value, axis, pairs)


def pair_terms(diag_one, diag_two, cross_one, cross_two, adjoint):
    if adjoint:
        return (diag_one + diag_two, cross_one - cross_two)
    return (diag_one - diag_two, cross_one + cross_two)


def depth_apply(current, pade_ops, adjoint):
    factor_count = pade_ops.shape[0]
    sequence = range(factor_count - 1, -1, -1) if adjoint else range(factor_count)
    for factor in sequence:
        contract = 1 if adjoint else 2
        product = lax.dot_general(
            current,
            pade_ops[factor],
            (((3,), (contract,)), ((), ())),
            preferred_element_type=jnp.float32,
        )
        real_part, imag_part = pair_terms(
            product[0, :, :, 0],
            product[1, :, :, 1],
            product[1, :, :, 0],
            product[0, :, :, 1],
            adjoint,
        )
        current = jnp.stack([real_part, imag_part]).astype(jnp.bfloat16)
    return current


def azimuth_apply(field_in, inverse, adjoint):
    block_width = inverse.shape[1]
    blocked = field_in.reshape(2, field_in.shape[1] // block_width, block_width, field_in.shape[2])
    contract = 1 if adjoint else 2
    product = lax.dot_general(
        inverse, blocked, (((contract,), (2,)), ((), ())), preferred_element_type=jnp.float32
    )
    real_part, imag_part = pair_terms(
        product[0, :, 0], product[1, :, 1], product[0, :, 1], product[1, :, 0], adjoint
    )
    joined = jnp.stack([real_part, imag_part])
    return joined.transpose(0, 2, 1, 3).reshape(field_in.shape)


def numerator_map(field_in):
    return field_in + coupling * (
        jnp.roll(field_in, 1, axis=1) + jnp.roll(field_in, -1, axis=1) - 2.0 * field_in
    )


def screen_phase(profile, bottom_row, depth_start):
    depths = depth_start + jnp.arange(profile.shape[0], dtype=jnp.int32)
    in_water = depths[None, :] < bottom_row[:, None]
    water_phase = phase_scale * (1.0 / (profile * profile) - 1.0)
    return (jnp.where(in_water, water_phase[None, :], bed_phase), in_water)


def depth_segment(field_in, pade_factors, adjoint):
    block_size = pade_factors.shape[3]
    if field_in.shape[2] % block_size == 0:
        worked = depth_apply(
            field_in.reshape(2, field_in.shape[1], field_in.shape[2] // block_size, block_size),
            pade_factors,
            adjoint,
        )
        return worked.reshape(field_in.shape)
    turned = lax.all_to_all(field_in, "line", split_axis=1, concat_axis=2, tiled=True)
    full_depth = turned.shape[2]
    worked = depth_apply(
        turned.reshape(2, turned.shape[1], full_depth // block_size, block_size),
        pade_factors,
        adjoint,
    )
    return lax.all_to_all(
        worked.reshape(turned.shape), "line", split_axis=2, concat_axis=1, tiled=True
    )


def general_local(
    checkpoint, adjoint_start, misfit, pade_factors, azimuth_inverse, bottom, base_speed, speed_step
):
    depth_rows = checkpoint.shape[3]
    depth_start = lax.axis_index("line") * depth_rows
    every_step = lax.all_gather(speed_step, "range", axis=0, tiled=True)
    running = jnp.cumsum(every_step, axis=0)
    profile = base_speed + lax.dynamic_index_in_dim(
        running, lax.axis_index("range"), 0, keepdims=False
    )
    phase_angle, in_water = screen_phase(profile, bottom[0], depth_start)
    cosine = jnp.cos(phase_angle)
    sine_term = jnp.sin(phase_angle)
    source = checkpoint[0].astype(jnp.float32)
    screened = jnp.stack(
        [cosine * source[0] - sine_term * source[1], sine_term * source[0] + cosine * source[1]]
    ).astype(jnp.bfloat16)
    depth_out = depth_segment(screened, pade_factors, False)
    numerator = numerator_map(depth_out.astype(jnp.float32)).astype(jnp.bfloat16)
    inverse = azimuth_inverse[0]
    field_end = azimuth_apply(numerator, inverse, False).astype(jnp.bfloat16)
    arrival = passed_along(adjoint_start, "range", -1)
    lam_end = (arrival[0].astype(jnp.float32) + misfit[0].astype(jnp.float32)).astype(jnp.bfloat16)
    backward = numerator_map(azimuth_apply(lam_end, inverse, True)).astype(jnp.bfloat16)
    backward = depth_segment(backward, pade_factors, True)
    cotangent = backward.astype(jnp.float32)
    adjoint_begin = jnp.stack(
        [
            cosine * cotangent[0] + sine_term * cotangent[1],
            cosine * cotangent[1] - sine_term * cotangent[0],
        ]
    ).astype(jnp.bfloat16)
    screened_f = screened.astype(jnp.float32)
    weight = jnp.where(in_water, cotangent[1] * screened_f[0] - cotangent[0] * screened_f[1], 0.0)
    grad_here = (
        jnp.sum(weight, axis=0) * (-8.0 / (profile * profile * profile)) / checkpoint.shape[2]
    )[None, :]
    all_grads = lax.all_gather(grad_here, "range", axis=0, tiled=True)
    suffix = jnp.flip(jnp.cumsum(jnp.flip(all_grads, 0), axis=0), 0)
    grad_increment = lax.dynamic_slice_in_dim(suffix, lax.axis_index("range"), 1, 0)
    return (field_end[None], adjoint_begin[None], grad_increment)


def dot_nt(left, right):
    return lax.dot_general(
        left, right, (((1,), (1,)), ((), ())), preferred_element_type=jnp.float32
    )


def dot_nn(left, right):
    return jnp.dot(left, right, preferred_element_type=jnp.float32)


def numerator_rows(field_in):
    rows = field_in.shape[0]
    return field_in + coupling * (
        pltpu.roll(field_in, 1, 0) + pltpu.roll(field_in, rows - 1, 0) - 2.0 * field_in
    )


def phase_tile(trig_ref, limit_ref, block_index, shape):
    columns = lax.broadcasted_iota(jnp.int32, shape, 1) + block_index * shape[1]
    in_water = columns < limit_ref[...]
    trig = trig_ref[...]
    cosine = jnp.where(in_water, trig[0:1], trig[2:3])
    sine_term = jnp.where(in_water, trig[1:2], trig[3:4])
    return cosine, sine_term, in_water


def screen_tile(source_ref, cosine, sine_term):
    source_r = source_ref[0].astype(jnp.float32)
    source_i = source_ref[1].astype(jnp.float32)
    screened_r = (cosine * source_r - sine_term * source_i).astype(jnp.bfloat16)
    screened_i = (sine_term * source_r + cosine * source_i).astype(jnp.bfloat16)
    return screened_r, screened_i


def forward_kernel(source_ref, trig_ref, limit_ref, pade_ref, inverse_ref, out_ref):
    block_index = pl.program_id(0)
    rows, width = source_ref.shape[1], source_ref.shape[2]
    cosine, sine_term, _ = phase_tile(trig_ref, limit_ref, block_index, (rows, width))
    cur_r, cur_i = screen_tile(source_ref, cosine, sine_term)
    for factor in range(pade_ref.shape[0]):
        pade_r = pade_ref[factor, 0]
        pade_i = pade_ref[factor, 1]
        real_part = dot_nt(cur_r, pade_r) - dot_nt(cur_i, pade_i)
        imag_part = dot_nt(cur_i, pade_r) + dot_nt(cur_r, pade_i)
        cur_r = real_part.astype(jnp.bfloat16)
        cur_i = imag_part.astype(jnp.bfloat16)
    num_r = numerator_rows(cur_r.astype(jnp.float32)).astype(jnp.bfloat16)
    num_i = numerator_rows(cur_i.astype(jnp.float32)).astype(jnp.bfloat16)
    inv_r = inverse_ref[0]
    inv_i = inverse_ref[1]
    block_width = inv_r.shape[0]
    for start in range(0, rows, block_width):
        part_r = num_r[start : start + block_width]
        part_i = num_i[start : start + block_width]
        out_ref[0, start : start + block_width, :] = (
            dot_nn(inv_r, part_r) - dot_nn(inv_i, part_i)
        ).astype(jnp.bfloat16)
        out_ref[1, start : start + block_width, :] = (
            dot_nn(inv_r, part_i) + dot_nn(inv_i, part_r)
        ).astype(jnp.bfloat16)


def make_backward_kernel(block_index):
    def backward_kernel(
        arrival_ref, misfit_ref, source_ref, trig_ref, limit_ref, pade_ref, inverse_t_ref,
        out_ref, grad_ref,
    ):
        rows, width = source_ref.shape[1], source_ref.shape[2]
        lam_r = (
            arrival_ref[0].astype(jnp.float32) + misfit_ref[0].astype(jnp.float32)
        ).astype(jnp.bfloat16)
        lam_i = (
            arrival_ref[1].astype(jnp.float32) + misfit_ref[1].astype(jnp.float32)
        ).astype(jnp.bfloat16)
        inv_r = inverse_t_ref[0]
        inv_i = inverse_t_ref[1]
        block_width = inv_r.shape[0]
        pieces_r = []
        pieces_i = []
        for start in range(0, rows, block_width):
            part_r = lam_r[start : start + block_width]
            part_i = lam_i[start : start + block_width]
            pieces_r.append(dot_nn(inv_r, part_r) + dot_nn(inv_i, part_i))
            pieces_i.append(dot_nn(inv_r, part_i) - dot_nn(inv_i, part_r))
        cur_r = numerator_rows(jnp.concatenate(pieces_r, axis=0)).astype(jnp.bfloat16)
        cur_i = numerator_rows(jnp.concatenate(pieces_i, axis=0)).astype(jnp.bfloat16)
        for factor in range(pade_ref.shape[0] - 1, -1, -1):
            pade_r = pade_ref[factor, 0]
            pade_i = pade_ref[factor, 1]
            real_part = dot_nn(cur_r, pade_r) + dot_nn(cur_i, pade_i)
            imag_part = dot_nn(cur_i, pade_r) - dot_nn(cur_r, pade_i)
            cur_r = real_part.astype(jnp.bfloat16)
            cur_i = imag_part.astype(jnp.bfloat16)
        cot_r = cur_r.astype(jnp.float32)
        cot_i = cur_i.astype(jnp.float32)
        cosine, sine_term, in_water = phase_tile(trig_ref, limit_ref, block_index, (rows, width))
        out_ref[0] = (cosine * cot_r + sine_term * cot_i).astype(jnp.bfloat16)
        out_ref[1] = (cosine * cot_i - sine_term * cot_r).astype(jnp.bfloat16)
        screened_r, screened_i = screen_tile(source_ref, cosine, sine_term)
        weight = jnp.where(
            in_water,
            cot_i * screened_r.astype(jnp.float32) - cot_r * screened_i.astype(jnp.float32),
            0.0,
        )
        grad_ref[...] = jnp.sum(weight, axis=0, keepdims=True)

    return backward_kernel


def range_scan(value, direction):
    count = lax.axis_size("range")
    total = value
    for reach in range(1, count):
        total = total + passed_along(value, "range", direction * reach)
    return total


def fused_local(
    checkpoint, adjoint_start, misfit, pade_factors, azimuth_inverse, bottom, base_speed, speed_step
):
    depth_rows = checkpoint.shape[3]
    rows = checkpoint.shape[2]
    block_size = pade_factors.shape[3]
    block_count = depth_rows // block_size
    depth_start = lax.axis_index("line") * depth_rows
    arrivals = [
        passed_along(
            adjoint_start[:, :, :, index * block_size : (index + 1) * block_size], "range", -1
        )
        for index in range(block_count)
    ]
    profile = base_speed + range_scan(speed_step, 1)[0]
    water_phase = phase_scale * (1.0 / (profile * profile) - 1.0)
    bed_row = jnp.full_like(water_phase, bed_phase)
    trig = jnp.stack(
        [jnp.cos(water_phase), jnp.sin(water_phase), jnp.cos(bed_row), jnp.sin(bed_row)]
    )
    limit = (bottom[0] - depth_start)[:, None]
    inverse = azimuth_inverse[0]
    inverse_t = jnp.swapaxes(inverse, 1, 2)
    field_spec = pl.BlockSpec((None, 2, rows, block_size), lambda b: (0, 0, 0, b))
    trig_spec = pl.BlockSpec((4, block_size), lambda b: (0, b))
    limit_spec = pl.BlockSpec((rows, 1), lambda b: (0, 0))
    pade_spec = pl.BlockSpec(pade_factors.shape, lambda b: (0, 0, 0, 0))
    inverse_spec = pl.BlockSpec(inverse.shape, lambda b: (0, 0, 0))
    field_end = pl.pallas_call(
        forward_kernel,
        grid=(block_count,),
        in_specs=[field_spec, trig_spec, limit_spec, pade_spec, inverse_spec],
        out_specs=field_spec,
        out_shape=jax.ShapeDtypeStruct(checkpoint.shape, jnp.bfloat16),
    )(checkpoint, trig, limit, pade_factors, inverse)
    field_end, arrivals[0] = lax.optimization_barrier((field_end, arrivals[0]))
    adjoint_begin = None
    grads = []
    for index in range(block_count):
        fixed = lambda b, index=index: (0, 0, 0, index)
        chunk_spec = pl.BlockSpec((None, 2, rows, block_size), lambda b: (0, 0, 0, 0))
        block_spec = pl.BlockSpec((None, 2, rows, block_size), fixed)
        in_specs = [
            chunk_spec,
            block_spec,
            block_spec,
            pl.BlockSpec((4, block_size), lambda b, index=index: (0, index)),
            limit_spec,
            pade_spec,
            inverse_spec,
        ]
        operands = [arrivals[index], misfit, checkpoint, trig, limit, pade_factors, inverse_t]
        aliases = {}
        kernel = make_backward_kernel(index)
        if adjoint_begin is not None:
            in_specs.append(pl.BlockSpec(memory_space=pl.ANY))
            operands.append(adjoint_begin)
            aliases = {len(operands) - 1: 0}
            kernel = lambda *refs, kernel=kernel: kernel(*refs[:7], *refs[8:])
        adjoint_begin, grad_part = pl.pallas_call(
            kernel,
            grid=(1,),
            in_specs=in_specs,
            out_specs=[
                block_spec,
                pl.BlockSpec((1, block_size), lambda b: (0, 0)),
            ],
            out_shape=[
                jax.ShapeDtypeStruct(checkpoint.shape, jnp.bfloat16),
                jax.ShapeDtypeStruct((1, block_size), jnp.float32),
            ],
            input_output_aliases=aliases,
        )(*operands)
        grads.append(grad_part)
    grad_sum = jnp.concatenate(grads, axis=1)
    grad_here = grad_sum * (-8.0 / (profile * profile * profile)) / rows
    count = lax.axis_size("range")
    own = lax.axis_index("range")
    senders = jnp.arange(count, dtype=jnp.int32)[:, None] <= own
    spread = jnp.where(senders, grad_here, 0.0)
    gathered = lax.all_to_all(spread, "range", split_axis=0, concat_axis=0, tiled=True)
    grad_increment = jnp.sum(gathered, axis=0, keepdims=True)
    return (field_end, adjoint_begin, grad_increment)


def local(
    checkpoint, adjoint_start, misfit, pade_factors, azimuth_inverse, bottom, base_speed, speed_step
):
    if checkpoint.shape[3] % pade_factors.shape[3] == 0:
        return fused_local(
            checkpoint, adjoint_start, misfit, pade_factors, azimuth_inverse, bottom,
            base_speed, speed_step,
        )
    return general_local(
        checkpoint, adjoint_start, misfit, pade_factors, azimuth_inverse, bottom,
        base_speed, speed_step,
    )


def solution(mesh):
    in_specs = (
        P("range", "freq", None, "line"),
        P("range", "freq", None, "line"),
        P("range", "freq", None, "line"),
        P(None, "freq", None, None),
        P("range", "freq", None, None),
        P("range", None),
        P("line"),
        P("range", "line"),
    )
    out_specs = (
        P("range", "freq", None, "line"),
        P("range", "freq", None, "line"),
        P(("freq", "range"), "line"),
    )
    return jax.shard_map(local, mesh=mesh, in_specs=in_specs, out_specs=out_specs, check_vma=False)
```

```python
import jax
import jax.numpy as jnp
from jax import lax
from jax.sharding import PartitionSpec as P
from jax.experimental import pallas as pl
from jax.experimental.pallas import tpu as pltpu

phase_scale = 4.0
bed_phase = -1.8
coupling = 0.3


def passed_along(value, axis, by):
    count = lax.axis_size(axis)
    pairs = [(i, i + by) for i in range(count) if 0 <= i + by < count]
    return lax.ppermute(value, axis, pairs)


def pair_terms(diag_one, diag_two, cross_one, cross_two, adjoint):
    if adjoint:
        return (diag_one + diag_two, cross_one - cross_two)
    return (diag_one - diag_two, cross_one + cross_two)


def depth_apply(current, pade_ops, adjoint):
    factor_count = pade_ops.shape[0]
    sequence = range(factor_count - 1, -1, -1) if adjoint else range(factor_count)
    for factor in sequence:
        contract = 1 if adjoint else 2
        product = lax.dot_general(
            current,
            pade_ops[factor],
            (((3,), (contract,)), ((), ())),
            preferred_element_type=jnp.float32,
        )
        real_part, imag_part = pair_terms(
            product[0, :, :, 0],
            product[1, :, :, 1],
            product[1, :, :, 0],
            product[0, :, :, 1],
            adjoint,
        )
        current = jnp.stack([real_part, imag_part]).astype(jnp.bfloat16)
    return current


def azimuth_apply(field_in, inverse, adjoint):
    block_width = inverse.shape[1]
    blocked = field_in.reshape(2, field_in.shape[1] // block_width, block_width, field_in.shape[2])
    contract = 1 if adjoint else 2
    product = lax.dot_general(
        inverse, blocked, (((contract,), (2,)), ((), ())), preferred_element_type=jnp.float32
    )
    real_part, imag_part = pair_terms(
        product[0, :, 0], product[1, :, 1], product[0, :, 1], product[1, :, 0], adjoint
    )
    joined = jnp.stack([real_part, imag_part])
    return joined.transpose(0, 2, 1, 3).reshape(field_in.shape)


def numerator_map(field_in):
    return field_in + coupling * (
        jnp.roll(field_in, 1, axis=1) + jnp.roll(field_in, -1, axis=1) - 2.0 * field_in
    )


def screen_phase(profile, bottom_row, depth_start):
    depths = depth_start + jnp.arange(profile.shape[0], dtype=jnp.int32)
    in_water = depths[None, :] < bottom_row[:, None]
    water_phase = phase_scale * (1.0 / (profile * profile) - 1.0)
    return (jnp.where(in_water, water_phase[None, :], bed_phase), in_water)


def depth_segment(field_in, pade_factors, adjoint):
    block_size = pade_factors.shape[3]
    if field_in.shape[2] % block_size == 0:
        worked = depth_apply(
            field_in.reshape(2, field_in.shape[1], field_in.shape[2] // block_size, block_size),
            pade_factors,
            adjoint,
        )
        return worked.reshape(field_in.shape)
    turned = lax.all_to_all(field_in, "line", split_axis=1, concat_axis=2, tiled=True)
    full_depth = turned.shape[2]
    worked = depth_apply(
        turned.reshape(2, turned.shape[1], full_depth // block_size, block_size),
        pade_factors,
        adjoint,
    )
    return lax.all_to_all(
        worked.reshape(turned.shape), "line", split_axis=2, concat_axis=1, tiled=True
    )


def general_local(
    checkpoint, adjoint_start, misfit, pade_factors, azimuth_inverse, bottom, base_speed, speed_step
):
    depth_rows = checkpoint.shape[3]
    depth_start = lax.axis_index("line") * depth_rows
    every_step = lax.all_gather(speed_step, "range", axis=0, tiled=True)
    running = jnp.cumsum(every_step, axis=0)
    profile = base_speed + lax.dynamic_index_in_dim(
        running, lax.axis_index("range"), 0, keepdims=False
    )
    phase_angle, in_water = screen_phase(profile, bottom[0], depth_start)
    cosine = jnp.cos(phase_angle)
    sine_term = jnp.sin(phase_angle)
    source = checkpoint[0].astype(jnp.float32)
    screened = jnp.stack(
        [cosine * source[0] - sine_term * source[1], sine_term * source[0] + cosine * source[1]]
    ).astype(jnp.bfloat16)
    depth_out = depth_segment(screened, pade_factors, False)
    numerator = numerator_map(depth_out.astype(jnp.float32)).astype(jnp.bfloat16)
    inverse = azimuth_inverse[0]
    field_end = azimuth_apply(numerator, inverse, False).astype(jnp.bfloat16)
    arrival = passed_along(adjoint_start, "range", -1)
    lam_end = (arrival[0].astype(jnp.float32) + misfit[0].astype(jnp.float32)).astype(jnp.bfloat16)
    backward = numerator_map(azimuth_apply(lam_end, inverse, True)).astype(jnp.bfloat16)
    backward = depth_segment(backward, pade_factors, True)
    cotangent = backward.astype(jnp.float32)
    adjoint_begin = jnp.stack(
        [
            cosine * cotangent[0] + sine_term * cotangent[1],
            cosine * cotangent[1] - sine_term * cotangent[0],
        ]
    ).astype(jnp.bfloat16)
    screened_f = screened.astype(jnp.float32)
    weight = jnp.where(in_water, cotangent[1] * screened_f[0] - cotangent[0] * screened_f[1], 0.0)
    grad_here = (
        jnp.sum(weight, axis=0) * (-8.0 / (profile * profile * profile)) / checkpoint.shape[2]
    )[None, :]
    all_grads = lax.all_gather(grad_here, "range", axis=0, tiled=True)
    suffix = jnp.flip(jnp.cumsum(jnp.flip(all_grads, 0), axis=0), 0)
    grad_increment = lax.dynamic_slice_in_dim(suffix, lax.axis_index("range"), 1, 0)
    return (field_end[None], adjoint_begin[None], grad_increment)


def dot_nt(left, right):
    return lax.dot_general(
        left, right, (((1,), (1,)), ((), ())), preferred_element_type=jnp.float32
    )


def dot_nn(left, right):
    return jnp.dot(left, right, preferred_element_type=jnp.float32)


def numerator_rows(field_in):
    rows = field_in.shape[0]
    return field_in + coupling * (
        pltpu.roll(field_in, 1, 0) + pltpu.roll(field_in, rows - 1, 0) - 2.0 * field_in
    )


def phase_tile(trig_ref, limit_ref, block_index, shape):
    columns = lax.broadcasted_iota(jnp.int32, shape, 1) + block_index * shape[1]
    in_water = columns < limit_ref[...]
    trig = trig_ref[...]
    cosine = jnp.where(in_water, trig[0:1], trig[2:3])
    sine_term = jnp.where(in_water, trig[1:2], trig[3:4])
    return cosine, sine_term, in_water


def screen_tile(source_ref, cosine, sine_term):
    source_r = source_ref[0].astype(jnp.float32)
    source_i = source_ref[1].astype(jnp.float32)
    screened_r = (cosine * source_r - sine_term * source_i).astype(jnp.bfloat16)
    screened_i = (sine_term * source_r + cosine * source_i).astype(jnp.bfloat16)
    return screened_r, screened_i


def forward_kernel(source_ref, trig_ref, limit_ref, pade_ref, inverse_ref, out_ref):
    block_index = pl.program_id(0)
    rows, width = source_ref.shape[1], source_ref.shape[2]
    cosine, sine_term, _ = phase_tile(trig_ref, limit_ref, block_index, (rows, width))
    cur_r, cur_i = screen_tile(source_ref, cosine, sine_term)
    for factor in range(pade_ref.shape[0]):
        pade_r = pade_ref[factor, 0]
        pade_i = pade_ref[factor, 1]
        real_part = dot_nt(cur_r, pade_r) - dot_nt(cur_i, pade_i)
        imag_part = dot_nt(cur_i, pade_r) + dot_nt(cur_r, pade_i)
        cur_r = real_part.astype(jnp.bfloat16)
        cur_i = imag_part.astype(jnp.bfloat16)
    num_r = numerator_rows(cur_r.astype(jnp.float32)).astype(jnp.bfloat16)
    num_i = numerator_rows(cur_i.astype(jnp.float32)).astype(jnp.bfloat16)
    inv_r = inverse_ref[0]
    inv_i = inverse_ref[1]
    block_width = inv_r.shape[0]
    for start in range(0, rows, block_width):
        part_r = num_r[start : start + block_width]
        part_i = num_i[start : start + block_width]
        out_ref[0, start : start + block_width, :] = (
            dot_nn(inv_r, part_r) - dot_nn(inv_i, part_i)
        ).astype(jnp.bfloat16)
        out_ref[1, start : start + block_width, :] = (
            dot_nn(inv_r, part_i) + dot_nn(inv_i, part_r)
        ).astype(jnp.bfloat16)


def make_backward_kernel(block_index):
    def backward_kernel(
        arrival_ref, misfit_ref, source_hbm, trig_ref, limit_hbm, pade_hbm, inverse_t_ref,
        scale_ref, out_ref, grad_ref, source_ref, limit_ref, pade_ref, copy_sems,
    ):
        rows, width = source_ref.shape[1], source_ref.shape[2]
        pade_copy = pltpu.make_async_copy(pade_hbm, pade_ref, copy_sems.at[0])
        source_copy = pltpu.make_async_copy(
            source_hbm.at[0, :, :, pl.ds(block_index * width, width)], source_ref, copy_sems.at[1]
        )
        limit_copy = pltpu.make_async_copy(limit_hbm, limit_ref, copy_sems.at[2])
        pade_copy.start()
        source_copy.start()
        limit_copy.start()
        lam_r = (
            arrival_ref[0].astype(jnp.float32) + misfit_ref[0].astype(jnp.float32)
        ).astype(jnp.bfloat16)
        lam_i = (
            arrival_ref[1].astype(jnp.float32) + misfit_ref[1].astype(jnp.float32)
        ).astype(jnp.bfloat16)
        inv_r = inverse_t_ref[0]
        inv_i = inverse_t_ref[1]
        block_width = inv_r.shape[0]
        pieces_r = []
        pieces_i = []
        for start in range(0, rows, block_width):
            part_r = lam_r[start : start + block_width]
            part_i = lam_i[start : start + block_width]
            pieces_r.append(dot_nn(inv_r, part_r) + dot_nn(inv_i, part_i))
            pieces_i.append(dot_nn(inv_r, part_i) - dot_nn(inv_i, part_r))
        cur_r = numerator_rows(jnp.concatenate(pieces_r, axis=0)).astype(jnp.bfloat16)
        cur_i = numerator_rows(jnp.concatenate(pieces_i, axis=0)).astype(jnp.bfloat16)
        pade_copy.wait()
        for factor in range(pade_ref.shape[0] - 1, -1, -1):
            pade_r = pade_ref[factor, 0]
            pade_i = pade_ref[factor, 1]
            real_part = dot_nn(cur_r, pade_r) + dot_nn(cur_i, pade_i)
            imag_part = dot_nn(cur_i, pade_r) - dot_nn(cur_r, pade_i)
            cur_r = real_part.astype(jnp.bfloat16)
            cur_i = imag_part.astype(jnp.bfloat16)
        cot_r = cur_r.astype(jnp.float32)
        cot_i = cur_i.astype(jnp.float32)
        source_copy.wait()
        limit_copy.wait()
        cosine, sine_term, in_water = phase_tile(trig_ref, limit_ref, block_index, (rows, width))
        out_ref[0] = (cosine * cot_r + sine_term * cot_i).astype(jnp.bfloat16)
        out_ref[1] = (cosine * cot_i - sine_term * cot_r).astype(jnp.bfloat16)
        screened_r, screened_i = screen_tile(source_ref, cosine, sine_term)
        weight = jnp.where(
            in_water,
            cot_i * screened_r.astype(jnp.float32) - cot_r * screened_i.astype(jnp.float32),
            0.0,
        )
        grad_ref[...] = jnp.sum(weight, axis=0, keepdims=True) * scale_ref[...] / rows

    return backward_kernel


def range_scan(value, direction):
    count = lax.axis_size("range")
    total = value
    for reach in range(1, count):
        total = total + passed_along(value, "range", direction * reach)
    return total


def fused_local(
    checkpoint, adjoint_start, misfit, pade_factors, azimuth_inverse, bottom, base_speed, speed_step
):
    depth_rows = checkpoint.shape[3]
    rows = checkpoint.shape[2]
    block_size = pade_factors.shape[3]
    block_count = depth_rows // block_size
    depth_start = lax.axis_index("line") * depth_rows
    arrivals = [
        passed_along(
            adjoint_start[:, :, :, index * block_size : (index + 1) * block_size], "range", -1
        )
        for index in range(block_count)
    ]
    profile = base_speed + range_scan(speed_step, 1)[0]
    water_phase = phase_scale * (1.0 / (profile * profile) - 1.0)
    bed_row = jnp.full_like(water_phase, bed_phase)
    trig = jnp.stack(
        [jnp.cos(water_phase), jnp.sin(water_phase), jnp.cos(bed_row), jnp.sin(bed_row)]
    )
    limit = (bottom[0] - depth_start)[:, None]
    inverse = azimuth_inverse[0]
    inverse_t = jnp.swapaxes(inverse, 1, 2)
    field_spec = pl.BlockSpec((None, 2, rows, block_size), lambda b: (0, 0, 0, b))
    trig_spec = pl.BlockSpec((4, block_size), lambda b: (0, b))
    limit_spec = pl.BlockSpec((rows, 1), lambda b: (0, 0))
    pade_spec = pl.BlockSpec(pade_factors.shape, lambda b: (0, 0, 0, 0))
    inverse_spec = pl.BlockSpec(inverse.shape, lambda b: (0, 0, 0))
    field_end = pl.pallas_call(
        forward_kernel,
        grid=(block_count,),
        in_specs=[field_spec, trig_spec, limit_spec, pade_spec, inverse_spec],
        out_specs=field_spec,
        out_shape=jax.ShapeDtypeStruct(checkpoint.shape, jnp.bfloat16),
    )(checkpoint, trig, limit, pade_factors, inverse)
    field_end, arrivals[0] = lax.optimization_barrier((field_end, arrivals[0]))
    scale = -8.0 / (profile * profile * profile)
    scale = scale[None, :]
    adjoint_begin = None
    grad_here = None
    any_spec = pl.BlockSpec(memory_space=pl.ANY)
    for index in range(block_count):
        fixed = lambda b, index=index: (0, 0, 0, index)
        row_fixed = lambda b, index=index: (0, index)
        chunk_spec = pl.BlockSpec((None, 2, rows, block_size), lambda b: (0, 0, 0, 0))
        block_spec = pl.BlockSpec((None, 2, rows, block_size), fixed)
        in_specs = [
            chunk_spec,
            block_spec,
            any_spec,
            pl.BlockSpec((4, block_size), row_fixed),
            any_spec,
            any_spec,
            inverse_spec,
            pl.BlockSpec((1, block_size), row_fixed),
        ]
        operands = [arrivals[index], misfit, checkpoint, trig, limit, pade_factors, inverse_t, scale]
        base_count = len(operands)
        aliases = {}
        kernel = make_backward_kernel(index)
        if adjoint_begin is not None:
            in_specs += [any_spec, any_spec]
            operands += [adjoint_begin, grad_here]
            aliases = {base_count: 0, base_count + 1: 1}
            kernel = lambda *refs, kernel=kernel, base_count=base_count: kernel(
                *refs[:base_count], *refs[base_count + 2 :]
            )
        adjoint_begin, grad_here = pl.pallas_call(
            kernel,
            grid=(1,),
            in_specs=in_specs,
            out_specs=[block_spec, pl.BlockSpec((1, block_size), row_fixed)],
            out_shape=[
                jax.ShapeDtypeStruct(checkpoint.shape, jnp.bfloat16),
                jax.ShapeDtypeStruct((1, depth_rows), jnp.float32),
            ],
            scratch_shapes=[
                pltpu.VMEM((2, rows, block_size), jnp.bfloat16),
                pltpu.VMEM(limit.shape, jnp.int32),
                pltpu.VMEM(pade_factors.shape, jnp.bfloat16),
                pltpu.SemaphoreType.DMA((3,)),
            ],
            input_output_aliases=aliases,
        )(*operands)
    grad_increment = range_scan(grad_here, -1)
    return (field_end, adjoint_begin, grad_increment)


def local(
    checkpoint, adjoint_start, misfit, pade_factors, azimuth_inverse, bottom, base_speed, speed_step
):
    if checkpoint.shape[3] % pade_factors.shape[3] == 0:
        return fused_local(
            checkpoint, adjoint_start, misfit, pade_factors, azimuth_inverse, bottom,
            base_speed, speed_step,
        )
    return general_local(
        checkpoint, adjoint_start, misfit, pade_factors, azimuth_inverse, bottom,
        base_speed, speed_step,
    )


def solution(mesh):
    in_specs = (
        P("range", "freq", None, "line"),
        P("range", "freq", None, "line"),
        P("range", "freq", None, "line"),
        P(None, "freq", None, None),
        P("range", "freq", None, None),
        P("range", None),
        P("line"),
        P("range", "line"),
    )
    out_specs = (
        P("range", "freq", None, "line"),
        P("range", "freq", None, "line"),
        P(("freq", "range"), "line"),
    )
    return jax.shard_map(local, mesh=mesh, in_specs=in_specs, out_specs=out_specs, check_vma=False)
```

```python
import jax
import jax.numpy as jnp
from jax import lax
from jax.sharding import PartitionSpec as P
from jax.experimental import pallas as pl
from jax.experimental.pallas import tpu as pltpu

phase_scale = 4.0
bed_phase = -1.8
coupling = 0.3


def passed_along(value, axis, by):
    count = lax.axis_size(axis)
    pairs = [(i, i + by) for i in range(count) if 0 <= i + by < count]
    return lax.ppermute(value, axis, pairs)


def pair_terms(diag_one, diag_two, cross_one, cross_two, adjoint):
    if adjoint:
        return (diag_one + diag_two, cross_one - cross_two)
    return (diag_one - diag_two, cross_one + cross_two)


def depth_apply(current, pade_ops, adjoint):
    factor_count = pade_ops.shape[0]
    sequence = range(factor_count - 1, -1, -1) if adjoint else range(factor_count)
    for factor in sequence:
        contract = 1 if adjoint else 2
        product = lax.dot_general(
            current,
            pade_ops[factor],
            (((3,), (contract,)), ((), ())),
            preferred_element_type=jnp.float32,
        )
        real_part, imag_part = pair_terms(
            product[0, :, :, 0],
            product[1, :, :, 1],
            product[1, :, :, 0],
            product[0, :, :, 1],
            adjoint,
        )
        current = jnp.stack([real_part, imag_part]).astype(jnp.bfloat16)
    return current


def azimuth_apply(field_in, inverse, adjoint):
    block_width = inverse.shape[1]
    blocked = field_in.reshape(2, field_in.shape[1] // block_width, block_width, field_in.shape[2])
    contract = 1 if adjoint else 2
    product = lax.dot_general(
        inverse, blocked, (((contract,), (2,)), ((), ())), preferred_element_type=jnp.float32
    )
    real_part, imag_part = pair_terms(
        product[0, :, 0], product[1, :, 1], product[0, :, 1], product[1, :, 0], adjoint
    )
    joined = jnp.stack([real_part, imag_part])
    return joined.transpose(0, 2, 1, 3).reshape(field_in.shape)


def numerator_map(field_in):
    return field_in + coupling * (
        jnp.roll(field_in, 1, axis=1) + jnp.roll(field_in, -1, axis=1) - 2.0 * field_in
    )


def screen_phase(profile, bottom_row, depth_start):
    depths = depth_start + jnp.arange(profile.shape[0], dtype=jnp.int32)
    in_water = depths[None, :] < bottom_row[:, None]
    water_phase = phase_scale * (1.0 / (profile * profile) - 1.0)
    return (jnp.where(in_water, water_phase[None, :], bed_phase), in_water)


def depth_segment(field_in, pade_factors, adjoint):
    block_size = pade_factors.shape[3]
    if field_in.shape[2] % block_size == 0:
        worked = depth_apply(
            field_in.reshape(2, field_in.shape[1], field_in.shape[2] // block_size, block_size),
            pade_factors,
            adjoint,
        )
        return worked.reshape(field_in.shape)
    turned = lax.all_to_all(field_in, "line", split_axis=1, concat_axis=2, tiled=True)
    full_depth = turned.shape[2]
    worked = depth_apply(
        turned.reshape(2, turned.shape[1], full_depth // block_size, block_size),
        pade_factors,
        adjoint,
    )
    return lax.all_to_all(
        worked.reshape(turned.shape), "line", split_axis=2, concat_axis=1, tiled=True
    )


def general_local(
    checkpoint, adjoint_start, misfit, pade_factors, azimuth_inverse, bottom, base_speed, speed_step
):
    depth_rows = checkpoint.shape[3]
    depth_start = lax.axis_index("line") * depth_rows
    every_step = lax.all_gather(speed_step, "range", axis=0, tiled=True)
    running = jnp.cumsum(every_step, axis=0)
    profile = base_speed + lax.dynamic_index_in_dim(
        running, lax.axis_index("range"), 0, keepdims=False
    )
    phase_angle, in_water = screen_phase(profile, bottom[0], depth_start)
    cosine = jnp.cos(phase_angle)
    sine_term = jnp.sin(phase_angle)
    source = checkpoint[0].astype(jnp.float32)
    screened = jnp.stack(
        [cosine * source[0] - sine_term * source[1], sine_term * source[0] + cosine * source[1]]
    ).astype(jnp.bfloat16)
    depth_out = depth_segment(screened, pade_factors, False)
    numerator = numerator_map(depth_out.astype(jnp.float32)).astype(jnp.bfloat16)
    inverse = azimuth_inverse[0]
    field_end = azimuth_apply(numerator, inverse, False).astype(jnp.bfloat16)
    arrival = passed_along(adjoint_start, "range", -1)
    lam_end = (arrival[0].astype(jnp.float32) + misfit[0].astype(jnp.float32)).astype(jnp.bfloat16)
    backward = numerator_map(azimuth_apply(lam_end, inverse, True)).astype(jnp.bfloat16)
    backward = depth_segment(backward, pade_factors, True)
    cotangent = backward.astype(jnp.float32)
    adjoint_begin = jnp.stack(
        [
            cosine * cotangent[0] + sine_term * cotangent[1],
            cosine * cotangent[1] - sine_term * cotangent[0],
        ]
    ).astype(jnp.bfloat16)
    screened_f = screened.astype(jnp.float32)
    weight = jnp.where(in_water, cotangent[1] * screened_f[0] - cotangent[0] * screened_f[1], 0.0)
    grad_here = (
        jnp.sum(weight, axis=0) * (-8.0 / (profile * profile * profile)) / checkpoint.shape[2]
    )[None, :]
    all_grads = lax.all_gather(grad_here, "range", axis=0, tiled=True)
    suffix = jnp.flip(jnp.cumsum(jnp.flip(all_grads, 0), axis=0), 0)
    grad_increment = lax.dynamic_slice_in_dim(suffix, lax.axis_index("range"), 1, 0)
    return (field_end[None], adjoint_begin[None], grad_increment)


def dot_nt(left, right):
    return lax.dot_general(
        left, right, (((1,), (1,)), ((), ())), preferred_element_type=jnp.float32
    )


def dot_nn(left, right):
    return jnp.dot(left, right, preferred_element_type=jnp.float32)


def numerator_rows(field_in):
    rows = field_in.shape[0]
    return field_in + coupling * (
        pltpu.roll(field_in, 1, 0) + pltpu.roll(field_in, rows - 1, 0) - 2.0 * field_in
    )


def phase_tile(trig_ref, limit_ref, block_index, shape):
    columns = lax.broadcasted_iota(jnp.int32, shape, 1) + block_index * shape[1]
    in_water = columns < limit_ref[...]
    trig = trig_ref[...]
    cosine = jnp.where(in_water, trig[0:1], trig[2:3])
    sine_term = jnp.where(in_water, trig[1:2], trig[3:4])
    return cosine, sine_term, in_water


def screen_tile(source_ref, cosine, sine_term):
    source_r = source_ref[0].astype(jnp.float32)
    source_i = source_ref[1].astype(jnp.float32)
    screened_r = (cosine * source_r - sine_term * source_i).astype(jnp.bfloat16)
    screened_i = (sine_term * source_r + cosine * source_i).astype(jnp.bfloat16)
    return screened_r, screened_i


def forward_kernel(source_ref, trig_ref, limit_ref, pade_ref, inverse_ref, out_ref):
    block_index = pl.program_id(0)
    rows, width = source_ref.shape[1], source_ref.shape[2]
    cosine, sine_term, _ = phase_tile(trig_ref, limit_ref, block_index, (rows, width))
    cur_r, cur_i = screen_tile(source_ref, cosine, sine_term)
    for factor in range(pade_ref.shape[0]):
        pade_r = pade_ref[factor, 0]
        pade_i = pade_ref[factor, 1]
        real_part = dot_nt(cur_r, pade_r) - dot_nt(cur_i, pade_i)
        imag_part = dot_nt(cur_i, pade_r) + dot_nt(cur_r, pade_i)
        cur_r = real_part.astype(jnp.bfloat16)
        cur_i = imag_part.astype(jnp.bfloat16)
    num_r = numerator_rows(cur_r.astype(jnp.float32)).astype(jnp.bfloat16)
    num_i = numerator_rows(cur_i.astype(jnp.float32)).astype(jnp.bfloat16)
    inv_r = inverse_ref[0]
    inv_i = inverse_ref[1]
    block_width = inv_r.shape[0]
    for start in range(0, rows, block_width):
        part_r = num_r[start : start + block_width]
        part_i = num_i[start : start + block_width]
        out_ref[0, start : start + block_width, :] = (
            dot_nn(inv_r, part_r) - dot_nn(inv_i, part_i)
        ).astype(jnp.bfloat16)
        out_ref[1, start : start + block_width, :] = (
            dot_nn(inv_r, part_i) + dot_nn(inv_i, part_r)
        ).astype(jnp.bfloat16)


def make_backward_kernel(block_index):
    def backward_kernel(
        arrival_ref, misfit_ref, source_ref, trig_ref, limit_ref, pade_ref, inverse_t_ref,
        out_ref, grad_ref,
    ):
        rows, width = source_ref.shape[1], source_ref.shape[2]
        lam_r = (
            arrival_ref[0].astype(jnp.float32) + misfit_ref[0].astype(jnp.float32)
        ).astype(jnp.bfloat16)
        lam_i = (
            arrival_ref[1].astype(jnp.float32) + misfit_ref[1].astype(jnp.float32)
        ).astype(jnp.bfloat16)
        inv_r = inverse_t_ref[0]
        inv_i = inverse_t_ref[1]
        block_width = inv_r.shape[0]
        pieces_r = []
        pieces_i = []
        for start in range(0, rows, block_width):
            part_r = lam_r[start : start + block_width]
            part_i = lam_i[start : start + block_width]
            pieces_r.append(dot_nn(inv_r, part_r) + dot_nn(inv_i, part_i))
            pieces_i.append(dot_nn(inv_r, part_i) - dot_nn(inv_i, part_r))
        cur_r = numerator_rows(jnp.concatenate(pieces_r, axis=0)).astype(jnp.bfloat16)
        cur_i = numerator_rows(jnp.concatenate(pieces_i, axis=0)).astype(jnp.bfloat16)
        for factor in range(pade_ref.shape[0] - 1, -1, -1):
            pade_r = pade_ref[factor, 0]
            pade_i = pade_ref[factor, 1]
            real_part = dot_nn(cur_r, pade_r) + dot_nn(cur_i, pade_i)
            imag_part = dot_nn(cur_i, pade_r) - dot_nn(cur_r, pade_i)
            cur_r = real_part.astype(jnp.bfloat16)
            cur_i = imag_part.astype(jnp.bfloat16)
        cot_r = cur_r.astype(jnp.float32)
        cot_i = cur_i.astype(jnp.float32)
        cosine, sine_term, in_water = phase_tile(trig_ref, limit_ref, block_index, (rows, width))
        out_ref[0] = (cosine * cot_r + sine_term * cot_i).astype(jnp.bfloat16)
        out_ref[1] = (cosine * cot_i - sine_term * cot_r).astype(jnp.bfloat16)
        screened_r, screened_i = screen_tile(source_ref, cosine, sine_term)
        weight = jnp.where(
            in_water,
            cot_i * screened_r.astype(jnp.float32) - cot_r * screened_i.astype(jnp.float32),
            0.0,
        )
        grad_ref[...] = jnp.sum(weight, axis=0, keepdims=True)

    return backward_kernel


def lam_rows(arrival, misfit_part):
    return (arrival.astype(jnp.float32) + misfit_part.astype(jnp.float32)).astype(jnp.bfloat16)


def azimuth_adjoint(inv_r, inv_i, part_r, part_i):
    return (
        dot_nn(inv_r, part_r) + dot_nn(inv_i, part_i),
        dot_nn(inv_r, part_i) - dot_nn(inv_i, part_r),
    )


def depth_adjoint(cur_r, cur_i, pade_ref):
    for factor in range(pade_ref.shape[0] - 1, -1, -1):
        pade_r = pade_ref[factor, 0]
        pade_i = pade_ref[factor, 1]
        real_part = dot_nn(cur_r, pade_r) + dot_nn(cur_i, pade_i)
        imag_part = dot_nn(cur_i, pade_r) - dot_nn(cur_r, pade_i)
        cur_r = real_part.astype(jnp.bfloat16)
        cur_i = imag_part.astype(jnp.bfloat16)
    return cur_r.astype(jnp.float32), cur_i.astype(jnp.float32)


def finish_rows(cot_r, cot_i, trig_ref, limit_rows, source_r, source_i, block_index):
    shape = cot_r.shape
    columns = lax.broadcasted_iota(jnp.int32, shape, 1) + block_index * shape[1]
    in_water = columns < limit_rows
    trig = trig_ref[...]
    cosine = jnp.where(in_water, trig[0:1], trig[2:3])
    sine_term = jnp.where(in_water, trig[1:2], trig[3:4])
    out_r = cosine * cot_r + sine_term * cot_i
    out_i = cosine * cot_i - sine_term * cot_r
    screened_r = (cosine * source_r - sine_term * source_i).astype(jnp.bfloat16)
    screened_i = (sine_term * source_r + cosine * source_i).astype(jnp.bfloat16)
    weight = jnp.where(
        in_water,
        cot_i * screened_r.astype(jnp.float32) - cot_r * screened_i.astype(jnp.float32),
        0.0,
    )
    return out_r, out_i, jnp.sum(weight, axis=0, keepdims=True)


HALO = 8


def make_first_half_kernel(block_index):
    def kernel(
        arrival_ref, misfit_ref, source_ref, trig_ref, limit_ref, pade_ref, inverse_t_ref,
        begin_in, begin_out, grad_ref, stage_ref, copy_sem,
    ):
        half, width = arrival_ref.shape[1], arrival_ref.shape[2]
        lam_r = lam_rows(arrival_ref[0], misfit_ref[0])
        lam_i = lam_rows(arrival_ref[1], misfit_ref[1])
        inv_r = inverse_t_ref[0]
        inv_i = inverse_t_ref[1]
        block_width = inv_r.shape[0]
        pieces_r = []
        pieces_i = []
        for start in range(0, half, block_width):
            piece_r, piece_i = azimuth_adjoint(
                inv_r, inv_i, lam_r[start : start + block_width], lam_i[start : start + block_width]
            )
            pieces_r.append(piece_r)
            pieces_i.append(piece_i)
        num_r = numerator_rows(jnp.concatenate(pieces_r, axis=0))[HALO : half - HALO]
        num_i = numerator_rows(jnp.concatenate(pieces_i, axis=0))[HALO : half - HALO]
        cot_r, cot_i = depth_adjoint(
            num_r.astype(jnp.bfloat16), num_i.astype(jnp.bfloat16), pade_ref
        )
        source_r = source_ref[0].astype(jnp.float32)[HALO : half - HALO]
        source_i = source_ref[1].astype(jnp.float32)[HALO : half - HALO]
        out_r, out_i, grad_row = finish_rows(
            cot_r, cot_i, trig_ref, limit_ref[HALO : half - HALO], source_r, source_i, block_index
        )
        stage_ref[0] = out_r.astype(jnp.bfloat16)
        stage_ref[1] = out_i.astype(jnp.bfloat16)
        copy = pltpu.make_async_copy(
            stage_ref,
            begin_out.at[0, :, pl.ds(HALO, half - 2 * HALO), pl.ds(block_index * width, width)],
            copy_sem.at[0],
        )
        copy.start()
        grad_ref[...] = grad_row
        copy.wait()

    return kernel


def make_second_half_kernel(block_index):
    def kernel(
        first_ref, arrival_ref, misfit_ref, source_ref, trig_ref, limit_ref, pade_ref,
        inverse_t_ref, begin_in, begin_out, grad_ref, main_ref, wrap_ref, copy_sem,
    ):
        half, width = arrival_ref.shape[1], arrival_ref.shape[2]
        rows = 2 * half
        inv_r = inverse_t_ref[0]
        inv_i = inverse_t_ref[1]
        block_width = inv_r.shape[0]
        edge = 2 * HALO
        lam_r = lam_rows(arrival_ref[0], misfit_ref[0, half:])
        lam_i = lam_rows(arrival_ref[1], misfit_ref[1, half:])
        top_r = lam_rows(first_ref[0, half - block_width :], misfit_ref[0, half - block_width : half])
        top_i = lam_rows(first_ref[1, half - block_width :], misfit_ref[1, half - block_width : half])
        low_r = lam_rows(first_ref[0, :block_width], misfit_ref[0, :block_width])
        low_i = lam_rows(first_ref[1, :block_width], misfit_ref[1, :block_width])
        before_r, before_i = azimuth_adjoint(
            inverse_t_ref[0, block_width - edge :], inverse_t_ref[1, block_width - edge :],
            top_r, top_i,
        )
        after_r, after_i = azimuth_adjoint(
            inverse_t_ref[0, :edge], inverse_t_ref[1, :edge], low_r, low_i
        )
        pieces_r = [before_r]
        pieces_i = [before_i]
        for start in range(0, half, block_width):
            piece_r, piece_i = azimuth_adjoint(
                inv_r, inv_i, lam_r[start : start + block_width], lam_i[start : start + block_width]
            )
            pieces_r.append(piece_r)
            pieces_i.append(piece_i)
        pieces_r.append(after_r)
        pieces_i.append(after_i)
        span = half + 2 * HALO
        num_r = numerator_rows(jnp.concatenate(pieces_r, axis=0))[HALO : HALO + span]
        num_i = numerator_rows(jnp.concatenate(pieces_i, axis=0))[HALO : HALO + span]
        cot_r, cot_i = depth_adjoint(
            num_r.astype(jnp.bfloat16), num_i.astype(jnp.bfloat16), pade_ref
        )
        full_r = source_ref[0].astype(jnp.float32)
        full_i = source_ref[1].astype(jnp.float32)
        source_r = jnp.concatenate([full_r[half - HALO :], full_r[:HALO]], axis=0)
        source_i = jnp.concatenate([full_i[half - HALO :], full_i[:HALO]], axis=0)
        limit_rows = jnp.concatenate([limit_ref[half - HALO :], limit_ref[:HALO]], axis=0)
        out_r, out_i, grad_row = finish_rows(
            cot_r, cot_i, trig_ref, limit_rows, source_r, source_i, block_index
        )
        main_ref[0] = out_r[: half + HALO].astype(jnp.bfloat16)
        main_ref[1] = out_i[: half + HALO].astype(jnp.bfloat16)
        wrap_ref[0] = out_r[half + HALO :].astype(jnp.bfloat16)
        wrap_ref[1] = out_i[half + HALO :].astype(jnp.bfloat16)
        columns = pl.ds(block_index * width, width)
        main_copy = pltpu.make_async_copy(
            main_ref, begin_out.at[0, :, pl.ds(half - HALO, half + HALO), columns], copy_sem.at[0]
        )
        wrap_copy = pltpu.make_async_copy(
            wrap_ref, begin_out.at[0, :, pl.ds(0, HALO), columns], copy_sem.at[1]
        )
        main_copy.start()
        wrap_copy.start()
        grad_ref[...] = grad_row
        main_copy.wait()
        wrap_copy.wait()

    return kernel


def range_scan(value, direction):
    count = lax.axis_size("range")
    total = value
    for reach in range(1, count):
        total = total + passed_along(value, "range", direction * reach)
    return total


def fused_local(
    checkpoint, adjoint_start, misfit, pade_factors, azimuth_inverse, bottom, base_speed, speed_step
):
    depth_rows = checkpoint.shape[3]
    rows = checkpoint.shape[2]
    block_size = pade_factors.shape[3]
    block_count = depth_rows // block_size
    depth_start = lax.axis_index("line") * depth_rows
    half = rows // 2
    last = block_count - 1
    arrivals = [
        passed_along(
            adjoint_start[:, :, :, index * block_size : (index + 1) * block_size], "range", -1
        )
        for index in range(last)
    ]
    last_columns = adjoint_start[:, :, :, last * block_size :]
    halves = [
        passed_along(last_columns[:, :, :half], "range", -1),
        passed_along(last_columns[:, :, half:], "range", -1),
    ]
    profile = base_speed + range_scan(speed_step, 1)[0]
    water_phase = phase_scale * (1.0 / (profile * profile) - 1.0)
    bed_row = jnp.full_like(water_phase, bed_phase)
    trig = jnp.stack(
        [jnp.cos(water_phase), jnp.sin(water_phase), jnp.cos(bed_row), jnp.sin(bed_row)]
    )
    limit = (bottom[0] - depth_start)[:, None]
    inverse = azimuth_inverse[0]
    inverse_t = jnp.swapaxes(inverse, 1, 2)
    field_spec = pl.BlockSpec((None, 2, rows, block_size), lambda b: (0, 0, 0, b))
    trig_spec = pl.BlockSpec((4, block_size), lambda b: (0, b))
    limit_spec = pl.BlockSpec((rows, 1), lambda b: (0, 0))
    pade_spec = pl.BlockSpec(pade_factors.shape, lambda b: (0, 0, 0, 0))
    inverse_spec = pl.BlockSpec(inverse.shape, lambda b: (0, 0, 0))
    field_end = pl.pallas_call(
        forward_kernel,
        grid=(block_count,),
        in_specs=[field_spec, trig_spec, limit_spec, pade_spec, inverse_spec],
        out_specs=field_spec,
        out_shape=jax.ShapeDtypeStruct(checkpoint.shape, jnp.bfloat16),
    )(checkpoint, trig, limit, pade_factors, inverse)
    field_end, arrivals[0] = lax.optimization_barrier((field_end, arrivals[0]))
    adjoint_begin = None
    grads = []
    for index in range(last):
        fixed = lambda b, index=index: (0, 0, 0, index)
        chunk_spec = pl.BlockSpec((None, 2, rows, block_size), lambda b: (0, 0, 0, 0))
        block_spec = pl.BlockSpec((None, 2, rows, block_size), fixed)
        in_specs = [
            chunk_spec,
            block_spec,
            block_spec,
            pl.BlockSpec((4, block_size), lambda b, index=index: (0, index)),
            limit_spec,
            pade_spec,
            inverse_spec,
        ]
        operands = [arrivals[index], misfit, checkpoint, trig, limit, pade_factors, inverse_t]
        aliases = {}
        kernel = make_backward_kernel(index)
        if adjoint_begin is not None:
            in_specs.append(pl.BlockSpec(memory_space=pl.ANY))
            operands.append(adjoint_begin)
            aliases = {len(operands) - 1: 0}
            kernel = lambda *refs, kernel=kernel: kernel(*refs[:7], *refs[8:])
        adjoint_begin, grad_part = pl.pallas_call(
            kernel,
            grid=(1,),
            in_specs=in_specs,
            out_specs=[
                block_spec,
                pl.BlockSpec((1, block_size), lambda b: (0, 0)),
            ],
            out_shape=[
                jax.ShapeDtypeStruct(checkpoint.shape, jnp.bfloat16),
                jax.ShapeDtypeStruct((1, block_size), jnp.float32),
            ],
            input_output_aliases=aliases,
        )(*operands)
        grads.append(grad_part)
    any_spec = pl.BlockSpec(memory_space=pl.ANY)
    fixed_last = lambda b: (0, 0, 0, last)
    half_spec = pl.BlockSpec((None, 2, half, block_size), lambda b: (0, 0, 0, 0))
    trig_last = pl.BlockSpec((4, block_size), lambda b: (0, last))
    grad_spec = pl.BlockSpec((1, block_size), lambda b: (0, 0))
    begin_shape = jax.ShapeDtypeStruct(checkpoint.shape, jnp.bfloat16)
    grad_shape = jax.ShapeDtypeStruct((1, block_size), jnp.float32)
    adjoint_begin, grad_first = pl.pallas_call(
        make_first_half_kernel(last),
        grid=(1,),
        in_specs=[
            half_spec,
            pl.BlockSpec((None, 2, half, block_size), fixed_last),
            pl.BlockSpec((None, 2, half, block_size), fixed_last),
            trig_last,
            limit_spec,
            pade_spec,
            inverse_spec,
            any_spec,
        ],
        out_specs=[any_spec, grad_spec],
        out_shape=[begin_shape, grad_shape],
        scratch_shapes=[
            pltpu.VMEM((2, half - 2 * HALO, block_size), jnp.bfloat16),
            pltpu.SemaphoreType.DMA((1,)),
        ],
        input_output_aliases={7: 0},
    )(halves[0], misfit, checkpoint, trig, limit, pade_factors, inverse_t, adjoint_begin)
    full_last = pl.BlockSpec((None, 2, rows, block_size), fixed_last)
    adjoint_begin, grad_second = pl.pallas_call(
        make_second_half_kernel(last),
        grid=(1,),
        in_specs=[
            half_spec,
            half_spec,
            full_last,
            full_last,
            trig_last,
            limit_spec,
            pade_spec,
            inverse_spec,
            any_spec,
        ],
        out_specs=[any_spec, grad_spec],
        out_shape=[begin_shape, grad_shape],
        scratch_shapes=[
            pltpu.VMEM((2, half + HALO, block_size), jnp.bfloat16),
            pltpu.VMEM((2, HALO, block_size), jnp.bfloat16),
            pltpu.SemaphoreType.DMA((2,)),
        ],
        input_output_aliases={8: 0},
    )(
        halves[0], halves[1], misfit, checkpoint, trig, limit, pade_factors, inverse_t,
        adjoint_begin,
    )
    grads.append(grad_first + grad_second)
    grad_sum = jnp.concatenate(grads, axis=1)
    grad_here = grad_sum * (-8.0 / (profile * profile * profile)) / rows
    grad_increment = range_scan(grad_here, -1)
    return (field_end, adjoint_begin, grad_increment)


def local(
    checkpoint, adjoint_start, misfit, pade_factors, azimuth_inverse, bottom, base_speed, speed_step
):
    if (
        checkpoint.shape[3] % pade_factors.shape[3] == 0
        and checkpoint.shape[3] >= 2 * pade_factors.shape[3]
        and checkpoint.shape[2] % (2 * azimuth_inverse.shape[2]) == 0
    ):
        return fused_local(
            checkpoint, adjoint_start, misfit, pade_factors, azimuth_inverse, bottom,
            base_speed, speed_step,
        )
    return general_local(
        checkpoint, adjoint_start, misfit, pade_factors, azimuth_inverse, bottom,
        base_speed, speed_step,
    )


def solution(mesh):
    in_specs = (
        P("range", "freq", None, "line"),
        P("range", "freq", None, "line"),
        P("range", "freq", None, "line"),
        P(None, "freq", None, None),
        P("range", "freq", None, None),
        P("range", None),
        P("line"),
        P("range", "line"),
    )
    out_specs = (
        P("range", "freq", None, "line"),
        P("range", "freq", None, "line"),
        P(("freq", "range"), "line"),
    )
    return jax.shard_map(local, mesh=mesh, in_specs=in_specs, out_specs=out_specs, check_vma=False)
```

```python
import jax
import jax.numpy as jnp
from jax import lax
from jax.sharding import PartitionSpec as P
from jax.experimental import pallas as pl
from jax.experimental.pallas import tpu as pltpu

phase_scale = 4.0
bed_phase = -1.8
coupling = 0.3


def passed_along(value, axis, by):
    count = lax.axis_size(axis)
    pairs = [(i, i + by) for i in range(count) if 0 <= i + by < count]
    return lax.ppermute(value, axis, pairs)


def pair_terms(diag_one, diag_two, cross_one, cross_two, adjoint):
    if adjoint:
        return (diag_one + diag_two, cross_one - cross_two)
    return (diag_one - diag_two, cross_one + cross_two)


def depth_apply(current, pade_ops, adjoint):
    factor_count = pade_ops.shape[0]
    sequence = range(factor_count - 1, -1, -1) if adjoint else range(factor_count)
    for factor in sequence:
        contract = 1 if adjoint else 2
        product = lax.dot_general(
            current,
            pade_ops[factor],
            (((3,), (contract,)), ((), ())),
            preferred_element_type=jnp.float32,
        )
        real_part, imag_part = pair_terms(
            product[0, :, :, 0],
            product[1, :, :, 1],
            product[1, :, :, 0],
            product[0, :, :, 1],
            adjoint,
        )
        current = jnp.stack([real_part, imag_part]).astype(jnp.bfloat16)
    return current


def azimuth_apply(field_in, inverse, adjoint):
    block_width = inverse.shape[1]
    blocked = field_in.reshape(2, field_in.shape[1] // block_width, block_width, field_in.shape[2])
    contract = 1 if adjoint else 2
    product = lax.dot_general(
        inverse, blocked, (((contract,), (2,)), ((), ())), preferred_element_type=jnp.float32
    )
    real_part, imag_part = pair_terms(
        product[0, :, 0], product[1, :, 1], product[0, :, 1], product[1, :, 0], adjoint
    )
    joined = jnp.stack([real_part, imag_part])
    return joined.transpose(0, 2, 1, 3).reshape(field_in.shape)


def numerator_map(field_in):
    return field_in + coupling * (
        jnp.roll(field_in, 1, axis=1) + jnp.roll(field_in, -1, axis=1) - 2.0 * field_in
    )


def screen_phase(profile, bottom_row, depth_start):
    depths = depth_start + jnp.arange(profile.shape[0], dtype=jnp.int32)
    in_water = depths[None, :] < bottom_row[:, None]
    water_phase = phase_scale * (1.0 / (profile * profile) - 1.0)
    return (jnp.where(in_water, water_phase[None, :], bed_phase), in_water)


def depth_segment(field_in, pade_factors, adjoint):
    block_size = pade_factors.shape[3]
    if field_in.shape[2] % block_size == 0:
        worked = depth_apply(
            field_in.reshape(2, field_in.shape[1], field_in.shape[2] // block_size, block_size),
            pade_factors,
            adjoint,
        )
        return worked.reshape(field_in.shape)
    turned = lax.all_to_all(field_in, "line", split_axis=1, concat_axis=2, tiled=True)
    full_depth = turned.shape[2]
    worked = depth_apply(
        turned.reshape(2, turned.shape[1], full_depth // block_size, block_size),
        pade_factors,
        adjoint,
    )
    return lax.all_to_all(
        worked.reshape(turned.shape), "line", split_axis=2, concat_axis=1, tiled=True
    )


def general_local(
    checkpoint, adjoint_start, misfit, pade_factors, azimuth_inverse, bottom, base_speed, speed_step
):
    depth_rows = checkpoint.shape[3]
    depth_start = lax.axis_index("line") * depth_rows
    every_step = lax.all_gather(speed_step, "range", axis=0, tiled=True)
    running = jnp.cumsum(every_step, axis=0)
    profile = base_speed + lax.dynamic_index_in_dim(
        running, lax.axis_index("range"), 0, keepdims=False
    )
    phase_angle, in_water = screen_phase(profile, bottom[0], depth_start)
    cosine = jnp.cos(phase_angle)
    sine_term = jnp.sin(phase_angle)
    source = checkpoint[0].astype(jnp.float32)
    screened = jnp.stack(
        [cosine * source[0] - sine_term * source[1], sine_term * source[0] + cosine * source[1]]
    ).astype(jnp.bfloat16)
    depth_out = depth_segment(screened, pade_factors, False)
    numerator = numerator_map(depth_out.astype(jnp.float32)).astype(jnp.bfloat16)
    inverse = azimuth_inverse[0]
    field_end = azimuth_apply(numerator, inverse, False).astype(jnp.bfloat16)
    arrival = passed_along(adjoint_start, "range", -1)
    lam_end = (arrival[0].astype(jnp.float32) + misfit[0].astype(jnp.float32)).astype(jnp.bfloat16)
    backward = numerator_map(azimuth_apply(lam_end, inverse, True)).astype(jnp.bfloat16)
    backward = depth_segment(backward, pade_factors, True)
    cotangent = backward.astype(jnp.float32)
    adjoint_begin = jnp.stack(
        [
            cosine * cotangent[0] + sine_term * cotangent[1],
            cosine * cotangent[1] - sine_term * cotangent[0],
        ]
    ).astype(jnp.bfloat16)
    screened_f = screened.astype(jnp.float32)
    weight = jnp.where(in_water, cotangent[1] * screened_f[0] - cotangent[0] * screened_f[1], 0.0)
    grad_here = (
        jnp.sum(weight, axis=0) * (-8.0 / (profile * profile * profile)) / checkpoint.shape[2]
    )[None, :]
    all_grads = lax.all_gather(grad_here, "range", axis=0, tiled=True)
    suffix = jnp.flip(jnp.cumsum(jnp.flip(all_grads, 0), axis=0), 0)
    grad_increment = lax.dynamic_slice_in_dim(suffix, lax.axis_index("range"), 1, 0)
    return (field_end[None], adjoint_begin[None], grad_increment)


def dot_nt(left, right):
    return lax.dot_general(
        left, right, (((1,), (1,)), ((), ())), preferred_element_type=jnp.float32
    )


def dot_nn(left, right):
    return jnp.dot(left, right, preferred_element_type=jnp.float32)


def numerator_rows(field_in):
    rows = field_in.shape[0]
    return field_in + coupling * (
        pltpu.roll(field_in, 1, 0) + pltpu.roll(field_in, rows - 1, 0) - 2.0 * field_in
    )


def phase_tile(trig_ref, limit_ref, block_index, shape):
    columns = lax.broadcasted_iota(jnp.int32, shape, 1) + block_index * shape[1]
    in_water = columns < limit_ref[...]
    trig = trig_ref[...]
    cosine = jnp.where(in_water, trig[0:1], trig[2:3])
    sine_term = jnp.where(in_water, trig[1:2], trig[3:4])
    return cosine, sine_term, in_water


def screen_tile(source_ref, cosine, sine_term):
    source_r = source_ref[0].astype(jnp.float32)
    source_i = source_ref[1].astype(jnp.float32)
    screened_r = (cosine * source_r - sine_term * source_i).astype(jnp.bfloat16)
    screened_i = (sine_term * source_r + cosine * source_i).astype(jnp.bfloat16)
    return screened_r, screened_i


def forward_kernel(source_ref, trig_ref, limit_ref, pade_ref, inverse_ref, out_ref):
    block_index = pl.program_id(0)
    rows, width = source_ref.shape[1], source_ref.shape[2]
    cosine, sine_term, _ = phase_tile(trig_ref, limit_ref, block_index, (rows, width))
    cur_r, cur_i = screen_tile(source_ref, cosine, sine_term)
    for factor in range(pade_ref.shape[0]):
        pade_r = pade_ref[factor, 0]
        pade_i = pade_ref[factor, 1]
        real_part = dot_nt(cur_r, pade_r) - dot_nt(cur_i, pade_i)
        imag_part = dot_nt(cur_i, pade_r) + dot_nt(cur_r, pade_i)
        cur_r = real_part.astype(jnp.bfloat16)
        cur_i = imag_part.astype(jnp.bfloat16)
    num_r = numerator_rows(cur_r.astype(jnp.float32)).astype(jnp.bfloat16)
    num_i = numerator_rows(cur_i.astype(jnp.float32)).astype(jnp.bfloat16)
    inv_r = inverse_ref[0]
    inv_i = inverse_ref[1]
    block_width = inv_r.shape[0]
    for start in range(0, rows, block_width):
        part_r = num_r[start : start + block_width]
        part_i = num_i[start : start + block_width]
        out_ref[0, start : start + block_width, :] = (
            dot_nn(inv_r, part_r) - dot_nn(inv_i, part_i)
        ).astype(jnp.bfloat16)
        out_ref[1, start : start + block_width, :] = (
            dot_nn(inv_r, part_i) + dot_nn(inv_i, part_r)
        ).astype(jnp.bfloat16)


def make_backward_kernel(block_index):
    def backward_kernel(
        arrival_ref, misfit_ref, source_ref, trig_ref, limit_ref, pade_ref, inverse_t_ref,
        out_ref, grad_ref,
    ):
        rows, width = source_ref.shape[1], source_ref.shape[2]
        lam_r = (
            arrival_ref[0].astype(jnp.float32) + misfit_ref[0].astype(jnp.float32)
        ).astype(jnp.bfloat16)
        lam_i = (
            arrival_ref[1].astype(jnp.float32) + misfit_ref[1].astype(jnp.float32)
        ).astype(jnp.bfloat16)
        inv_r = inverse_t_ref[0]
        inv_i = inverse_t_ref[1]
        block_width = inv_r.shape[0]
        pieces_r = []
        pieces_i = []
        for start in range(0, rows, block_width):
            part_r = lam_r[start : start + block_width]
            part_i = lam_i[start : start + block_width]
            pieces_r.append(dot_nn(inv_r, part_r) + dot_nn(inv_i, part_i))
            pieces_i.append(dot_nn(inv_r, part_i) - dot_nn(inv_i, part_r))
        cur_r = numerator_rows(jnp.concatenate(pieces_r, axis=0)).astype(jnp.bfloat16)
        cur_i = numerator_rows(jnp.concatenate(pieces_i, axis=0)).astype(jnp.bfloat16)
        for factor in range(pade_ref.shape[0] - 1, -1, -1):
            pade_r = pade_ref[factor, 0]
            pade_i = pade_ref[factor, 1]
            real_part = dot_nn(cur_r, pade_r) + dot_nn(cur_i, pade_i)
            imag_part = dot_nn(cur_i, pade_r) - dot_nn(cur_r, pade_i)
            cur_r = real_part.astype(jnp.bfloat16)
            cur_i = imag_part.astype(jnp.bfloat16)
        cot_r = cur_r.astype(jnp.float32)
        cot_i = cur_i.astype(jnp.float32)
        cosine, sine_term, in_water = phase_tile(trig_ref, limit_ref, block_index, (rows, width))
        out_ref[0] = (cosine * cot_r + sine_term * cot_i).astype(jnp.bfloat16)
        out_ref[1] = (cosine * cot_i - sine_term * cot_r).astype(jnp.bfloat16)
        screened_r, screened_i = screen_tile(source_ref, cosine, sine_term)
        weight = jnp.where(
            in_water,
            cot_i * screened_r.astype(jnp.float32) - cot_r * screened_i.astype(jnp.float32),
            0.0,
        )
        grad_ref[...] = jnp.sum(weight, axis=0, keepdims=True)

    return backward_kernel


def lam_rows(arrival, misfit_part):
    return (arrival.astype(jnp.float32) + misfit_part.astype(jnp.float32)).astype(jnp.bfloat16)


def azimuth_adjoint(inv_r, inv_i, part_r, part_i):
    return (
        dot_nn(inv_r, part_r) + dot_nn(inv_i, part_i),
        dot_nn(inv_r, part_i) - dot_nn(inv_i, part_r),
    )


def depth_adjoint(cur_r, cur_i, pade_ref):
    for factor in range(pade_ref.shape[0] - 1, -1, -1):
        pade_r = pade_ref[factor, 0]
        pade_i = pade_ref[factor, 1]
        real_part = dot_nn(cur_r, pade_r) + dot_nn(cur_i, pade_i)
        imag_part = dot_nn(cur_i, pade_r) - dot_nn(cur_r, pade_i)
        cur_r = real_part.astype(jnp.bfloat16)
        cur_i = imag_part.astype(jnp.bfloat16)
    return cur_r.astype(jnp.float32), cur_i.astype(jnp.float32)


def finish_rows(cot_r, cot_i, trig_ref, limit_rows, source_r, source_i, block_index):
    shape = cot_r.shape
    columns = lax.broadcasted_iota(jnp.int32, shape, 1) + block_index * shape[1]
    in_water = columns < limit_rows
    trig = trig_ref[...]
    cosine = jnp.where(in_water, trig[0:1], trig[2:3])
    sine_term = jnp.where(in_water, trig[1:2], trig[3:4])
    out_r = cosine * cot_r + sine_term * cot_i
    out_i = cosine * cot_i - sine_term * cot_r
    screened_r = (cosine * source_r - sine_term * source_i).astype(jnp.bfloat16)
    screened_i = (sine_term * source_r + cosine * source_i).astype(jnp.bfloat16)
    weight = jnp.where(
        in_water,
        cot_i * screened_r.astype(jnp.float32) - cot_r * screened_i.astype(jnp.float32),
        0.0,
    )
    return out_r, out_i, jnp.sum(weight, axis=0, keepdims=True)


HALO = 8


def make_first_half_kernel(block_index):
    def kernel(
        arrival_ref, misfit_ref, source_ref, trig_ref, limit_ref, pade_ref, inverse_t_ref,
        begin_in, begin_out, grad_ref, stage_ref, copy_sem,
    ):
        half, width = arrival_ref.shape[1], arrival_ref.shape[2]
        lam_r = lam_rows(arrival_ref[0], misfit_ref[0])
        lam_i = lam_rows(arrival_ref[1], misfit_ref[1])
        inv_r = inverse_t_ref[0]
        inv_i = inverse_t_ref[1]
        block_width = inv_r.shape[0]
        pieces_r = []
        pieces_i = []
        for start in range(0, half, block_width):
            piece_r, piece_i = azimuth_adjoint(
                inv_r, inv_i, lam_r[start : start + block_width], lam_i[start : start + block_width]
            )
            pieces_r.append(piece_r)
            pieces_i.append(piece_i)
        num_r = numerator_rows(jnp.concatenate(pieces_r, axis=0))[HALO : half - HALO]
        num_i = numerator_rows(jnp.concatenate(pieces_i, axis=0))[HALO : half - HALO]
        cot_r, cot_i = depth_adjoint(
            num_r.astype(jnp.bfloat16), num_i.astype(jnp.bfloat16), pade_ref
        )
        source_r = source_ref[0].astype(jnp.float32)[HALO : half - HALO]
        source_i = source_ref[1].astype(jnp.float32)[HALO : half - HALO]
        out_r, out_i, grad_row = finish_rows(
            cot_r, cot_i, trig_ref, limit_ref[HALO : half - HALO], source_r, source_i, block_index
        )
        stage_ref[0] = out_r.astype(jnp.bfloat16)
        stage_ref[1] = out_i.astype(jnp.bfloat16)
        copy = pltpu.make_async_copy(
            stage_ref,
            begin_out.at[0, :, pl.ds(HALO, half - 2 * HALO), pl.ds(block_index * width, width)],
            copy_sem.at[0],
        )
        copy.start()
        grad_ref[...] = grad_row
        copy.wait()

    return kernel


def make_second_half_kernel(block_index):
    def kernel(
        first_ref, arrival_ref, misfit_ref, source_ref, trig_ref, limit_ref, pade_ref,
        inverse_t_ref, begin_in, begin_out, grad_ref, main_ref, wrap_ref, copy_sem,
    ):
        half, width = arrival_ref.shape[1], arrival_ref.shape[2]
        inv_r = inverse_t_ref[0]
        inv_i = inverse_t_ref[1]
        block_width = inv_r.shape[0]
        edge = 2 * HALO
        lam_r = lam_rows(arrival_ref[0], misfit_ref[0, half:])
        lam_i = lam_rows(arrival_ref[1], misfit_ref[1, half:])
        top_r = lam_rows(first_ref[0, half - block_width :], misfit_ref[0, half - block_width : half])
        top_i = lam_rows(first_ref[1, half - block_width :], misfit_ref[1, half - block_width : half])
        low_r = lam_rows(first_ref[0, :block_width], misfit_ref[0, :block_width])
        low_i = lam_rows(first_ref[1, :block_width], misfit_ref[1, :block_width])
        before_r, before_i = azimuth_adjoint(
            inverse_t_ref[0, block_width - edge :], inverse_t_ref[1, block_width - edge :],
            top_r, top_i,
        )
        after_r, after_i = azimuth_adjoint(
            inverse_t_ref[0, :edge], inverse_t_ref[1, :edge], low_r, low_i
        )
        pieces_r = [before_r]
        pieces_i = [before_i]
        for start in range(0, half, block_width):
            piece_r, piece_i = azimuth_adjoint(
                inv_r, inv_i, lam_r[start : start + block_width], lam_i[start : start + block_width]
            )
            pieces_r.append(piece_r)
            pieces_i.append(piece_i)
        pieces_r.append(after_r)
        pieces_i.append(after_i)
        span = half + 2 * HALO
        num_r = numerator_rows(jnp.concatenate(pieces_r, axis=0))[HALO : HALO + span]
        num_i = numerator_rows(jnp.concatenate(pieces_i, axis=0))[HALO : HALO + span]
        cot_r, cot_i = depth_adjoint(
            num_r.astype(jnp.bfloat16), num_i.astype(jnp.bfloat16), pade_ref
        )
        full_r = source_ref[0].astype(jnp.float32)
        full_i = source_ref[1].astype(jnp.float32)
        source_r = jnp.concatenate([full_r[half - HALO :], full_r[:HALO]], axis=0)
        source_i = jnp.concatenate([full_i[half - HALO :], full_i[:HALO]], axis=0)
        limit_rows = jnp.concatenate([limit_ref[half - HALO :], limit_ref[:HALO]], axis=0)
        out_r, out_i, grad_row = finish_rows(
            cot_r, cot_i, trig_ref, limit_rows, source_r, source_i, block_index
        )
        main_ref[0] = out_r[: half + HALO].astype(jnp.bfloat16)
        main_ref[1] = out_i[: half + HALO].astype(jnp.bfloat16)
        wrap_ref[0] = out_r[half + HALO :].astype(jnp.bfloat16)
        wrap_ref[1] = out_i[half + HALO :].astype(jnp.bfloat16)
        columns = pl.ds(block_index * width, width)
        main_copy = pltpu.make_async_copy(
            main_ref, begin_out.at[0, :, pl.ds(half - HALO, half + HALO), columns], copy_sem.at[0]
        )
        wrap_copy = pltpu.make_async_copy(
            wrap_ref, begin_out.at[0, :, pl.ds(0, HALO), columns], copy_sem.at[1]
        )
        main_copy.start()
        wrap_copy.start()
        grad_ref[...] = grad_row
        main_copy.wait()
        wrap_copy.wait()

    return kernel


def range_scan(value, direction):
    count = lax.axis_size("range")
    total = value
    for reach in range(1, count):
        total = total + passed_along(value, "range", direction * reach)
    return total


def fused_local(
    checkpoint, adjoint_start, misfit, pade_factors, azimuth_inverse, bottom, base_speed, speed_step
):
    depth_rows = checkpoint.shape[3]
    rows = checkpoint.shape[2]
    block_size = pade_factors.shape[3]
    block_count = depth_rows // block_size
    depth_start = lax.axis_index("line") * depth_rows
    half = rows // 2
    last = block_count - 1
    arrivals = [
        passed_along(
            adjoint_start[:, :, :, index * block_size : (index + 1) * block_size], "range", -1
        )
        for index in range(last)
    ]
    last_columns = adjoint_start[:, :, :, last * block_size :]
    first_half = passed_along(last_columns[:, :, :half], "range", -1)
    second_half = passed_along(last_columns[:, :, half:], "range", -1)
    halves = [first_half, second_half]
    profile = base_speed + range_scan(speed_step, 1)[0]
    water_phase = phase_scale * (1.0 / (profile * profile) - 1.0)
    bed_row = jnp.full_like(water_phase, bed_phase)
    trig = jnp.stack(
        [jnp.cos(water_phase), jnp.sin(water_phase), jnp.cos(bed_row), jnp.sin(bed_row)]
    )
    limit = (bottom[0] - depth_start)[:, None]
    inverse = azimuth_inverse[0]
    inverse_t = jnp.swapaxes(inverse, 1, 2)
    field_spec = pl.BlockSpec((None, 2, rows, block_size), lambda b: (0, 0, 0, b))
    trig_spec = pl.BlockSpec((4, block_size), lambda b: (0, b))
    limit_spec = pl.BlockSpec((rows, 1), lambda b: (0, 0))
    pade_spec = pl.BlockSpec(pade_factors.shape, lambda b: (0, 0, 0, 0))
    inverse_spec = pl.BlockSpec(inverse.shape, lambda b: (0, 0, 0))
    field_end = pl.pallas_call(
        forward_kernel,
        grid=(block_count,),
        in_specs=[field_spec, trig_spec, limit_spec, pade_spec, inverse_spec],
        out_specs=field_spec,
        out_shape=jax.ShapeDtypeStruct(checkpoint.shape, jnp.bfloat16),
    )(checkpoint, trig, limit, pade_factors, inverse)
    field_end, arrivals[0] = lax.optimization_barrier((field_end, arrivals[0]))
    adjoint_begin = None
    grads = []
    for index in range(last):
        fixed = lambda b, index=index: (0, 0, 0, index)
        chunk_spec = pl.BlockSpec((None, 2, rows, block_size), lambda b: (0, 0, 0, 0))
        block_spec = pl.BlockSpec((None, 2, rows, block_size), fixed)
        in_specs = [
            chunk_spec,
            block_spec,
            block_spec,
            pl.BlockSpec((4, block_size), lambda b, index=index: (0, index)),
            limit_spec,
            pade_spec,
            inverse_spec,
        ]
        operands = [arrivals[index], misfit, checkpoint, trig, limit, pade_factors, inverse_t]
        aliases = {}
        kernel = make_backward_kernel(index)
        if adjoint_begin is not None:
            in_specs.append(pl.BlockSpec(memory_space=pl.ANY))
            operands.append(adjoint_begin)
            aliases = {len(operands) - 1: 0}
            kernel = lambda *refs, kernel=kernel: kernel(*refs[:7], *refs[8:])
        adjoint_begin, grad_part = pl.pallas_call(
            kernel,
            grid=(1,),
            in_specs=in_specs,
            out_specs=[
                block_spec,
                pl.BlockSpec((1, block_size), lambda b: (0, 0)),
            ],
            out_shape=[
                jax.ShapeDtypeStruct(checkpoint.shape, jnp.bfloat16),
                jax.ShapeDtypeStruct((1, block_size), jnp.float32),
            ],
            input_output_aliases=aliases,
        )(*operands)
        grads.append(grad_part)
    any_spec = pl.BlockSpec(memory_space=pl.ANY)
    fixed_last = lambda b: (0, 0, 0, last)
    half_spec = pl.BlockSpec((None, 2, half, block_size), lambda b: (0, 0, 0, 0))
    trig_last = pl.BlockSpec((4, block_size), lambda b: (0, last))
    grad_spec = pl.BlockSpec((1, block_size), lambda b: (0, 0))
    begin_shape = jax.ShapeDtypeStruct(checkpoint.shape, jnp.bfloat16)
    grad_shape = jax.ShapeDtypeStruct((1, block_size), jnp.float32)
    adjoint_begin, grad_first = pl.pallas_call(
        make_first_half_kernel(last),
        grid=(1,),
        in_specs=[
            half_spec,
            pl.BlockSpec((None, 2, half, block_size), fixed_last),
            pl.BlockSpec((None, 2, half, block_size), fixed_last),
            trig_last,
            limit_spec,
            pade_spec,
            inverse_spec,
            any_spec,
        ],
        out_specs=[any_spec, grad_spec],
        out_shape=[begin_shape, grad_shape],
        scratch_shapes=[
            pltpu.VMEM((2, half - 2 * HALO, block_size), jnp.bfloat16),
            pltpu.SemaphoreType.DMA((1,)),
        ],
        input_output_aliases={7: 0},
    )(halves[0], misfit, checkpoint, trig, limit, pade_factors, inverse_t, adjoint_begin)
    full_last = pl.BlockSpec((None, 2, rows, block_size), fixed_last)
    adjoint_begin, grad_second = pl.pallas_call(
        make_second_half_kernel(last),
        grid=(1,),
        in_specs=[
            half_spec,
            half_spec,
            full_last,
            full_last,
            trig_last,
            limit_spec,
            pade_spec,
            inverse_spec,
            any_spec,
        ],
        out_specs=[any_spec, grad_spec],
        out_shape=[begin_shape, grad_shape],
        scratch_shapes=[
            pltpu.VMEM((2, half + HALO, block_size), jnp.bfloat16),
            pltpu.VMEM((2, HALO, block_size), jnp.bfloat16),
            pltpu.SemaphoreType.DMA((2,)),
        ],
        input_output_aliases={8: 0},
    )(
        halves[0], halves[1], misfit, checkpoint, trig, limit, pade_factors, inverse_t,
        adjoint_begin,
    )
    grads.append(grad_first + grad_second)
    grad_sum = jnp.concatenate(grads, axis=1)
    grad_here = grad_sum * (-8.0 / (profile * profile * profile)) / rows
    grad_increment = range_scan(grad_here, -1)
    return (field_end, adjoint_begin, grad_increment)


def local(
    checkpoint, adjoint_start, misfit, pade_factors, azimuth_inverse, bottom, base_speed, speed_step
):
    if (
        checkpoint.shape[3] % pade_factors.shape[3] == 0
        and checkpoint.shape[3] >= 2 * pade_factors.shape[3]
        and checkpoint.shape[2] % (2 * azimuth_inverse.shape[2]) == 0
    ):
        return fused_local(
            checkpoint, adjoint_start, misfit, pade_factors, azimuth_inverse, bottom,
            base_speed, speed_step,
        )
    return general_local(
        checkpoint, adjoint_start, misfit, pade_factors, azimuth_inverse, bottom,
        base_speed, speed_step,
    )


def solution(mesh):
    in_specs = (
        P("range", "freq", None, "line"),
        P("range", "freq", None, "line"),
        P("range", "freq", None, "line"),
        P(None, "freq", None, None),
        P("range", "freq", None, None),
        P("range", None),
        P("line"),
        P("range", "line"),
    )
    out_specs = (
        P("range", "freq", None, "line"),
        P("range", "freq", None, "line"),
        P(("freq", "range"), "line"),
    )
    return jax.shard_map(local, mesh=mesh, in_specs=in_specs, out_specs=out_specs, check_vma=False)
```

```python
import jax
import jax.numpy as jnp
from jax import lax
from jax.sharding import PartitionSpec as P
from jax.experimental import pallas as pl
from jax.experimental.pallas import tpu as pltpu

phase_scale = 4.0
bed_phase = -1.8
coupling = 0.3


def passed_along(value, axis, by):
    count = lax.axis_size(axis)
    pairs = [(i, i + by) for i in range(count) if 0 <= i + by < count]
    return lax.ppermute(value, axis, pairs)


def pair_terms(diag_one, diag_two, cross_one, cross_two, adjoint):
    if adjoint:
        return (diag_one + diag_two, cross_one - cross_two)
    return (diag_one - diag_two, cross_one + cross_two)


def depth_apply(current, pade_ops, adjoint):
    factor_count = pade_ops.shape[0]
    sequence = range(factor_count - 1, -1, -1) if adjoint else range(factor_count)
    for factor in sequence:
        contract = 1 if adjoint else 2
        product = lax.dot_general(
            current,
            pade_ops[factor],
            (((3,), (contract,)), ((), ())),
            preferred_element_type=jnp.float32,
        )
        real_part, imag_part = pair_terms(
            product[0, :, :, 0],
            product[1, :, :, 1],
            product[1, :, :, 0],
            product[0, :, :, 1],
            adjoint,
        )
        current = jnp.stack([real_part, imag_part]).astype(jnp.bfloat16)
    return current


def azimuth_apply(field_in, inverse, adjoint):
    block_width = inverse.shape[1]
    blocked = field_in.reshape(2, field_in.shape[1] // block_width, block_width, field_in.shape[2])
    contract = 1 if adjoint else 2
    product = lax.dot_general(
        inverse, blocked, (((contract,), (2,)), ((), ())), preferred_element_type=jnp.float32
    )
    real_part, imag_part = pair_terms(
        product[0, :, 0], product[1, :, 1], product[0, :, 1], product[1, :, 0], adjoint
    )
    joined = jnp.stack([real_part, imag_part])
    return joined.transpose(0, 2, 1, 3).reshape(field_in.shape)


def numerator_map(field_in):
    return field_in + coupling * (
        jnp.roll(field_in, 1, axis=1) + jnp.roll(field_in, -1, axis=1) - 2.0 * field_in
    )


def screen_phase(profile, bottom_row, depth_start):
    depths = depth_start + jnp.arange(profile.shape[0], dtype=jnp.int32)
    in_water = depths[None, :] < bottom_row[:, None]
    water_phase = phase_scale * (1.0 / (profile * profile) - 1.0)
    return (jnp.where(in_water, water_phase[None, :], bed_phase), in_water)


def depth_segment(field_in, pade_factors, adjoint):
    block_size = pade_factors.shape[3]
    if field_in.shape[2] % block_size == 0:
        worked = depth_apply(
            field_in.reshape(2, field_in.shape[1], field_in.shape[2] // block_size, block_size),
            pade_factors,
            adjoint,
        )
        return worked.reshape(field_in.shape)
    turned = lax.all_to_all(field_in, "line", split_axis=1, concat_axis=2, tiled=True)
    full_depth = turned.shape[2]
    worked = depth_apply(
        turned.reshape(2, turned.shape[1], full_depth // block_size, block_size),
        pade_factors,
        adjoint,
    )
    return lax.all_to_all(
        worked.reshape(turned.shape), "line", split_axis=2, concat_axis=1, tiled=True
    )


def general_local(
    checkpoint, adjoint_start, misfit, pade_factors, azimuth_inverse, bottom, base_speed, speed_step
):
    depth_rows = checkpoint.shape[3]
    depth_start = lax.axis_index("line") * depth_rows
    every_step = lax.all_gather(speed_step, "range", axis=0, tiled=True)
    running = jnp.cumsum(every_step, axis=0)
    profile = base_speed + lax.dynamic_index_in_dim(
        running, lax.axis_index("range"), 0, keepdims=False
    )
    phase_angle, in_water = screen_phase(profile, bottom[0], depth_start)
    cosine = jnp.cos(phase_angle)
    sine_term = jnp.sin(phase_angle)
    source = checkpoint[0].astype(jnp.float32)
    screened = jnp.stack(
        [cosine * source[0] - sine_term * source[1], sine_term * source[0] + cosine * source[1]]
    ).astype(jnp.bfloat16)
    depth_out = depth_segment(screened, pade_factors, False)
    numerator = numerator_map(depth_out.astype(jnp.float32)).astype(jnp.bfloat16)
    inverse = azimuth_inverse[0]
    field_end = azimuth_apply(numerator, inverse, False).astype(jnp.bfloat16)
    arrival = passed_along(adjoint_start, "range", -1)
    lam_end = (arrival[0].astype(jnp.float32) + misfit[0].astype(jnp.float32)).astype(jnp.bfloat16)
    backward = numerator_map(azimuth_apply(lam_end, inverse, True)).astype(jnp.bfloat16)
    backward = depth_segment(backward, pade_factors, True)
    cotangent = backward.astype(jnp.float32)
    adjoint_begin = jnp.stack(
        [
            cosine * cotangent[0] + sine_term * cotangent[1],
            cosine * cotangent[1] - sine_term * cotangent[0],
        ]
    ).astype(jnp.bfloat16)
    screened_f = screened.astype(jnp.float32)
    weight = jnp.where(in_water, cotangent[1] * screened_f[0] - cotangent[0] * screened_f[1], 0.0)
    grad_here = (
        jnp.sum(weight, axis=0) * (-8.0 / (profile * profile * profile)) / checkpoint.shape[2]
    )[None, :]
    all_grads = lax.all_gather(grad_here, "range", axis=0, tiled=True)
    suffix = jnp.flip(jnp.cumsum(jnp.flip(all_grads, 0), axis=0), 0)
    grad_increment = lax.dynamic_slice_in_dim(suffix, lax.axis_index("range"), 1, 0)
    return (field_end[None], adjoint_begin[None], grad_increment)


def dot_nt(left, right):
    return lax.dot_general(
        left, right, (((1,), (1,)), ((), ())), preferred_element_type=jnp.float32
    )


def dot_nn(left, right):
    return jnp.dot(left, right, preferred_element_type=jnp.float32)


def numerator_rows(field_in):
    rows = field_in.shape[0]
    return field_in + coupling * (
        pltpu.roll(field_in, 1, 0) + pltpu.roll(field_in, rows - 1, 0) - 2.0 * field_in
    )


def phase_tile(trig_ref, limit_ref, block_index, shape):
    columns = lax.broadcasted_iota(jnp.int32, shape, 1) + block_index * shape[1]
    in_water = columns < limit_ref[...]
    trig = trig_ref[...]
    cosine = jnp.where(in_water, trig[0:1], trig[2:3])
    sine_term = jnp.where(in_water, trig[1:2], trig[3:4])
    return cosine, sine_term, in_water


def screen_tile(source_ref, cosine, sine_term):
    source_r = source_ref[0].astype(jnp.float32)
    source_i = source_ref[1].astype(jnp.float32)
    screened_r = (cosine * source_r - sine_term * source_i).astype(jnp.bfloat16)
    screened_i = (sine_term * source_r + cosine * source_i).astype(jnp.bfloat16)
    return screened_r, screened_i


def forward_kernel(source_ref, trig_ref, limit_ref, pade_ref, inverse_ref, out_ref):
    block_index = pl.program_id(0)
    rows, width = source_ref.shape[1], source_ref.shape[2]
    cosine, sine_term, _ = phase_tile(trig_ref, limit_ref, block_index, (rows, width))
    cur_r, cur_i = screen_tile(source_ref, cosine, sine_term)
    for factor in range(pade_ref.shape[0]):
        pade_r = pade_ref[factor, 0]
        pade_i = pade_ref[factor, 1]
        real_part = dot_nt(cur_r, pade_r) - dot_nt(cur_i, pade_i)
        imag_part = dot_nt(cur_i, pade_r) + dot_nt(cur_r, pade_i)
        cur_r = real_part.astype(jnp.bfloat16)
        cur_i = imag_part.astype(jnp.bfloat16)
    num_r = numerator_rows(cur_r.astype(jnp.float32)).astype(jnp.bfloat16)
    num_i = numerator_rows(cur_i.astype(jnp.float32)).astype(jnp.bfloat16)
    inv_r = inverse_ref[0]
    inv_i = inverse_ref[1]
    block_width = inv_r.shape[0]
    for start in range(0, rows, block_width):
        part_r = num_r[start : start + block_width]
        part_i = num_i[start : start + block_width]
        out_ref[0, start : start + block_width, :] = (
            dot_nn(inv_r, part_r) - dot_nn(inv_i, part_i)
        ).astype(jnp.bfloat16)
        out_ref[1, start : start + block_width, :] = (
            dot_nn(inv_r, part_i) + dot_nn(inv_i, part_r)
        ).astype(jnp.bfloat16)


def make_backward_kernel(block_index):
    def backward_kernel(
        arrival_ref, misfit_ref, source_ref, trig_ref, limit_ref, pade_ref, inverse_t_ref,
        out_ref, grad_ref,
    ):
        rows, width = source_ref.shape[1], source_ref.shape[2]
        lam_r = (
            arrival_ref[0].astype(jnp.float32) + misfit_ref[0].astype(jnp.float32)
        ).astype(jnp.bfloat16)
        lam_i = (
            arrival_ref[1].astype(jnp.float32) + misfit_ref[1].astype(jnp.float32)
        ).astype(jnp.bfloat16)
        inv_r = inverse_t_ref[0]
        inv_i = inverse_t_ref[1]
        block_width = inv_r.shape[0]
        pieces_r = []
        pieces_i = []
        for start in range(0, rows, block_width):
            part_r = lam_r[start : start + block_width]
            part_i = lam_i[start : start + block_width]
            pieces_r.append(dot_nn(inv_r, part_r) + dot_nn(inv_i, part_i))
            pieces_i.append(dot_nn(inv_r, part_i) - dot_nn(inv_i, part_r))
        cur_r = numerator_rows(jnp.concatenate(pieces_r, axis=0)).astype(jnp.bfloat16)
        cur_i = numerator_rows(jnp.concatenate(pieces_i, axis=0)).astype(jnp.bfloat16)
        for factor in range(pade_ref.shape[0] - 1, -1, -1):
            pade_r = pade_ref[factor, 0]
            pade_i = pade_ref[factor, 1]
            real_part = dot_nn(cur_r, pade_r) + dot_nn(cur_i, pade_i)
            imag_part = dot_nn(cur_i, pade_r) - dot_nn(cur_r, pade_i)
            cur_r = real_part.astype(jnp.bfloat16)
            cur_i = imag_part.astype(jnp.bfloat16)
        cot_r = cur_r.astype(jnp.float32)
        cot_i = cur_i.astype(jnp.float32)
        cosine, sine_term, in_water = phase_tile(trig_ref, limit_ref, block_index, (rows, width))
        out_ref[0] = (cosine * cot_r + sine_term * cot_i).astype(jnp.bfloat16)
        out_ref[1] = (cosine * cot_i - sine_term * cot_r).astype(jnp.bfloat16)
        screened_r, screened_i = screen_tile(source_ref, cosine, sine_term)
        weight = jnp.where(
            in_water,
            cot_i * screened_r.astype(jnp.float32) - cot_r * screened_i.astype(jnp.float32),
            0.0,
        )
        grad_ref[...] = jnp.sum(weight, axis=0, keepdims=True)

    return backward_kernel


def lam_rows(arrival, misfit_part):
    return (arrival.astype(jnp.float32) + misfit_part.astype(jnp.float32)).astype(jnp.bfloat16)


def azimuth_adjoint(inv_r, inv_i, part_r, part_i):
    return (
        dot_nn(inv_r, part_r) + dot_nn(inv_i, part_i),
        dot_nn(inv_r, part_i) - dot_nn(inv_i, part_r),
    )


def depth_adjoint(cur_r, cur_i, pade_ref):
    for factor in range(pade_ref.shape[0] - 1, -1, -1):
        pade_r = pade_ref[factor, 0]
        pade_i = pade_ref[factor, 1]
        real_part = dot_nn(cur_r, pade_r) + dot_nn(cur_i, pade_i)
        imag_part = dot_nn(cur_i, pade_r) - dot_nn(cur_r, pade_i)
        cur_r = real_part.astype(jnp.bfloat16)
        cur_i = imag_part.astype(jnp.bfloat16)
    return cur_r.astype(jnp.float32), cur_i.astype(jnp.float32)


def finish_rows(cot_r, cot_i, trig_ref, limit_rows, source_r, source_i, block_index):
    shape = cot_r.shape
    columns = lax.broadcasted_iota(jnp.int32, shape, 1) + block_index * shape[1]
    in_water = columns < limit_rows
    trig = trig_ref[...]
    cosine = jnp.where(in_water, trig[0:1], trig[2:3])
    sine_term = jnp.where(in_water, trig[1:2], trig[3:4])
    out_r = cosine * cot_r + sine_term * cot_i
    out_i = cosine * cot_i - sine_term * cot_r
    screened_r = (cosine * source_r - sine_term * source_i).astype(jnp.bfloat16)
    screened_i = (sine_term * source_r + cosine * source_i).astype(jnp.bfloat16)
    weight = jnp.where(
        in_water,
        cot_i * screened_r.astype(jnp.float32) - cot_r * screened_i.astype(jnp.float32),
        0.0,
    )
    return out_r, out_i, jnp.sum(weight, axis=0, keepdims=True)


HALO = 8


def make_first_half_kernel(block_index):
    def kernel(
        arrival_ref, misfit_ref, source_ref, trig_ref, limit_ref, pade_ref, inverse_t_ref,
        begin_in, begin_out, grad_ref, stage_ref, copy_sem,
    ):
        half, width = arrival_ref.shape[1], arrival_ref.shape[2]
        lam_r = lam_rows(arrival_ref[0], misfit_ref[0])
        lam_i = lam_rows(arrival_ref[1], misfit_ref[1])
        inv_r = inverse_t_ref[0]
        inv_i = inverse_t_ref[1]
        block_width = inv_r.shape[0]
        pieces_r = []
        pieces_i = []
        for start in range(0, half, block_width):
            piece_r, piece_i = azimuth_adjoint(
                inv_r, inv_i, lam_r[start : start + block_width], lam_i[start : start + block_width]
            )
            pieces_r.append(piece_r)
            pieces_i.append(piece_i)
        num_r = numerator_rows(jnp.concatenate(pieces_r, axis=0))[HALO : half - HALO]
        num_i = numerator_rows(jnp.concatenate(pieces_i, axis=0))[HALO : half - HALO]
        cot_r, cot_i = depth_adjoint(
            num_r.astype(jnp.bfloat16), num_i.astype(jnp.bfloat16), pade_ref
        )
        source_r = source_ref[0].astype(jnp.float32)[HALO : half - HALO]
        source_i = source_ref[1].astype(jnp.float32)[HALO : half - HALO]
        out_r, out_i, grad_row = finish_rows(
            cot_r, cot_i, trig_ref, limit_ref[HALO : half - HALO], source_r, source_i, block_index
        )
        stage_ref[0] = out_r.astype(jnp.bfloat16)
        stage_ref[1] = out_i.astype(jnp.bfloat16)
        copy = pltpu.make_async_copy(
            stage_ref,
            begin_out.at[0, :, pl.ds(HALO, half - 2 * HALO), pl.ds(block_index * width, width)],
            copy_sem.at[0],
        )
        copy.start()
        grad_ref[...] = grad_row
        copy.wait()

    return kernel


def make_second_half_kernel(block_index):
    def kernel(
        first_ref, arrival_ref, misfit_ref, source_ref, trig_ref, limit_ref, pade_ref,
        inverse_t_ref, begin_in, whole_grad_ref, first_grad_ref, scale_ref,
        begin_out, grad_ref, main_ref, wrap_ref, copy_sem,
    ):
        half, width = arrival_ref.shape[1], arrival_ref.shape[2]
        rows = 2 * half
        inv_r = inverse_t_ref[0]
        inv_i = inverse_t_ref[1]
        block_width = inv_r.shape[0]
        edge = 2 * HALO
        lam_r = lam_rows(arrival_ref[0], misfit_ref[0, half:])
        lam_i = lam_rows(arrival_ref[1], misfit_ref[1, half:])
        top_r = lam_rows(first_ref[0, half - block_width :], misfit_ref[0, half - block_width : half])
        top_i = lam_rows(first_ref[1, half - block_width :], misfit_ref[1, half - block_width : half])
        low_r = lam_rows(first_ref[0, :block_width], misfit_ref[0, :block_width])
        low_i = lam_rows(first_ref[1, :block_width], misfit_ref[1, :block_width])
        before_r, before_i = azimuth_adjoint(
            inverse_t_ref[0, block_width - edge :], inverse_t_ref[1, block_width - edge :],
            top_r, top_i,
        )
        after_r, after_i = azimuth_adjoint(
            inverse_t_ref[0, :edge], inverse_t_ref[1, :edge], low_r, low_i
        )
        pieces_r = [before_r]
        pieces_i = [before_i]
        for start in range(0, half, block_width):
            piece_r, piece_i = azimuth_adjoint(
                inv_r, inv_i, lam_r[start : start + block_width], lam_i[start : start + block_width]
            )
            pieces_r.append(piece_r)
            pieces_i.append(piece_i)
        pieces_r.append(after_r)
        pieces_i.append(after_i)
        span = half + 2 * HALO
        num_r = numerator_rows(jnp.concatenate(pieces_r, axis=0))[HALO : HALO + span]
        num_i = numerator_rows(jnp.concatenate(pieces_i, axis=0))[HALO : HALO + span]
        cot_r, cot_i = depth_adjoint(
            num_r.astype(jnp.bfloat16), num_i.astype(jnp.bfloat16), pade_ref
        )
        full_r = source_ref[0].astype(jnp.float32)
        full_i = source_ref[1].astype(jnp.float32)
        source_r = jnp.concatenate([full_r[half - HALO :], full_r[:HALO]], axis=0)
        source_i = jnp.concatenate([full_i[half - HALO :], full_i[:HALO]], axis=0)
        limit_rows = jnp.concatenate([limit_ref[half - HALO :], limit_ref[:HALO]], axis=0)
        out_r, out_i, grad_row = finish_rows(
            cot_r, cot_i, trig_ref, limit_rows, source_r, source_i, block_index
        )
        main_ref[0] = out_r[: half + HALO].astype(jnp.bfloat16)
        main_ref[1] = out_i[: half + HALO].astype(jnp.bfloat16)
        wrap_ref[0] = out_r[half + HALO :].astype(jnp.bfloat16)
        wrap_ref[1] = out_i[half + HALO :].astype(jnp.bfloat16)
        columns = pl.ds(block_index * width, width)
        main_copy = pltpu.make_async_copy(
            main_ref, begin_out.at[0, :, pl.ds(half - HALO, half + HALO), columns], copy_sem.at[0]
        )
        wrap_copy = pltpu.make_async_copy(
            wrap_ref, begin_out.at[0, :, pl.ds(0, HALO), columns], copy_sem.at[1]
        )
        main_copy.start()
        wrap_copy.start()
        scale = scale_ref[...]
        grad_ref[:, : block_index * width] = (
            whole_grad_ref[...] * scale[:, : block_index * width] / rows
        )
        grad_ref[:, block_index * width :] = (
            (first_grad_ref[...] + grad_row) * scale[:, block_index * width :] / rows
        )
        main_copy.wait()
        wrap_copy.wait()

    return kernel


def range_scan(value, direction):
    count = lax.axis_size("range")
    total = value
    for reach in range(1, count):
        total = total + passed_along(value, "range", direction * reach)
    return total


def fused_local(
    checkpoint, adjoint_start, misfit, pade_factors, azimuth_inverse, bottom, base_speed, speed_step
):
    depth_rows = checkpoint.shape[3]
    rows = checkpoint.shape[2]
    block_size = pade_factors.shape[3]
    block_count = depth_rows // block_size
    depth_start = lax.axis_index("line") * depth_rows
    half = rows // 2
    last = block_count - 1
    arrivals = [
        passed_along(
            adjoint_start[:, :, :, index * block_size : (index + 1) * block_size], "range", -1
        )
        for index in range(last)
    ]
    last_columns = adjoint_start[:, :, :, last * block_size :]
    first_half = passed_along(last_columns[:, :, :half], "range", -1)
    second_half = passed_along(last_columns[:, :, half:], "range", -1)
    halves = [first_half, second_half]
    profile = base_speed + range_scan(speed_step, 1)[0]
    water_phase = phase_scale * (1.0 / (profile * profile) - 1.0)
    bed_row = jnp.full_like(water_phase, bed_phase)
    trig = jnp.stack(
        [jnp.cos(water_phase), jnp.sin(water_phase), jnp.cos(bed_row), jnp.sin(bed_row)]
    )
    limit = (bottom[0] - depth_start)[:, None]
    inverse = azimuth_inverse[0]
    inverse_t = jnp.swapaxes(inverse, 1, 2)
    field_spec = pl.BlockSpec((None, 2, rows, block_size), lambda b: (0, 0, 0, b))
    trig_spec = pl.BlockSpec((4, block_size), lambda b: (0, b))
    limit_spec = pl.BlockSpec((rows, 1), lambda b: (0, 0))
    pade_spec = pl.BlockSpec(pade_factors.shape, lambda b: (0, 0, 0, 0))
    inverse_spec = pl.BlockSpec(inverse.shape, lambda b: (0, 0, 0))
    field_end = pl.pallas_call(
        forward_kernel,
        grid=(block_count,),
        in_specs=[field_spec, trig_spec, limit_spec, pade_spec, inverse_spec],
        out_specs=field_spec,
        out_shape=jax.ShapeDtypeStruct(checkpoint.shape, jnp.bfloat16),
    )(checkpoint, trig, limit, pade_factors, inverse)
    field_end, arrivals[0] = lax.optimization_barrier((field_end, arrivals[0]))
    adjoint_begin = None
    grads = []
    for index in range(last):
        fixed = lambda b, index=index: (0, 0, 0, index)
        chunk_spec = pl.BlockSpec((None, 2, rows, block_size), lambda b: (0, 0, 0, 0))
        block_spec = pl.BlockSpec((None, 2, rows, block_size), fixed)
        in_specs = [
            chunk_spec,
            block_spec,
            block_spec,
            pl.BlockSpec((4, block_size), lambda b, index=index: (0, index)),
            limit_spec,
            pade_spec,
            inverse_spec,
        ]
        operands = [arrivals[index], misfit, checkpoint, trig, limit, pade_factors, inverse_t]
        aliases = {}
        kernel = make_backward_kernel(index)
        if adjoint_begin is not None:
            in_specs.append(pl.BlockSpec(memory_space=pl.ANY))
            operands.append(adjoint_begin)
            aliases = {len(operands) - 1: 0}
            kernel = lambda *refs, kernel=kernel: kernel(*refs[:7], *refs[8:])
        adjoint_begin, grad_part = pl.pallas_call(
            kernel,
            grid=(1,),
            in_specs=in_specs,
            out_specs=[
                block_spec,
                pl.BlockSpec((1, block_size), lambda b: (0, 0)),
            ],
            out_shape=[
                jax.ShapeDtypeStruct(checkpoint.shape, jnp.bfloat16),
                jax.ShapeDtypeStruct((1, block_size), jnp.float32),
            ],
            input_output_aliases=aliases,
        )(*operands)
        grads.append(grad_part)
    any_spec = pl.BlockSpec(memory_space=pl.ANY)
    fixed_last = lambda b: (0, 0, 0, last)
    half_spec = pl.BlockSpec((None, 2, half, block_size), lambda b: (0, 0, 0, 0))
    trig_last = pl.BlockSpec((4, block_size), lambda b: (0, last))
    grad_spec = pl.BlockSpec((1, block_size), lambda b: (0, 0))
    begin_shape = jax.ShapeDtypeStruct(checkpoint.shape, jnp.bfloat16)
    grad_shape = jax.ShapeDtypeStruct((1, block_size), jnp.float32)
    adjoint_begin, grad_first = pl.pallas_call(
        make_first_half_kernel(last),
        grid=(1,),
        in_specs=[
            half_spec,
            pl.BlockSpec((None, 2, half, block_size), fixed_last),
            pl.BlockSpec((None, 2, half, block_size), fixed_last),
            trig_last,
            limit_spec,
            pade_spec,
            inverse_spec,
            any_spec,
        ],
        out_specs=[any_spec, grad_spec],
        out_shape=[begin_shape, grad_shape],
        scratch_shapes=[
            pltpu.VMEM((2, half - 2 * HALO, block_size), jnp.bfloat16),
            pltpu.SemaphoreType.DMA((1,)),
        ],
        input_output_aliases={7: 0},
    )(halves[0], misfit, checkpoint, trig, limit, pade_factors, inverse_t, adjoint_begin)
    full_last = pl.BlockSpec((None, 2, rows, block_size), fixed_last)
    scale = (-8.0 / (profile * profile * profile))[None, :]
    whole_row = pl.BlockSpec((1, depth_rows), lambda b: (0, 0))
    adjoint_begin, grad_here = pl.pallas_call(
        make_second_half_kernel(last),
        grid=(1,),
        in_specs=[
            half_spec,
            half_spec,
            full_last,
            full_last,
            trig_last,
            limit_spec,
            pade_spec,
            inverse_spec,
            any_spec,
            pl.BlockSpec((1, last * block_size), lambda b: (0, 0)),
            grad_spec,
            whole_row,
        ],
        out_specs=[any_spec, whole_row],
        out_shape=[begin_shape, jax.ShapeDtypeStruct((1, depth_rows), jnp.float32)],
        scratch_shapes=[
            pltpu.VMEM((2, half + HALO, block_size), jnp.bfloat16),
            pltpu.VMEM((2, HALO, block_size), jnp.bfloat16),
            pltpu.SemaphoreType.DMA((2,)),
        ],
        input_output_aliases={8: 0},
    )(
        halves[0], halves[1], misfit, checkpoint, trig, limit, pade_factors, inverse_t,
        adjoint_begin, grads[0], grad_first, scale,
    )
    grad_increment = range_scan(grad_here, -1)
    return (field_end, adjoint_begin, grad_increment)


def local(
    checkpoint, adjoint_start, misfit, pade_factors, azimuth_inverse, bottom, base_speed, speed_step
):
    if (
        checkpoint.shape[3] % pade_factors.shape[3] == 0
        and checkpoint.shape[3] >= 2 * pade_factors.shape[3]
        and checkpoint.shape[2] % (2 * azimuth_inverse.shape[2]) == 0
    ):
        return fused_local(
            checkpoint, adjoint_start, misfit, pade_factors, azimuth_inverse, bottom,
            base_speed, speed_step,
        )
    return general_local(
        checkpoint, adjoint_start, misfit, pade_factors, azimuth_inverse, bottom,
        base_speed, speed_step,
    )


def solution(mesh):
    in_specs = (
        P("range", "freq", None, "line"),
        P("range", "freq", None, "line"),
        P("range", "freq", None, "line"),
        P(None, "freq", None, None),
        P("range", "freq", None, None),
        P("range", None),
        P("line"),
        P("range", "line"),
    )
    out_specs = (
        P("range", "freq", None, "line"),
        P("range", "freq", None, "line"),
        P(("freq", "range"), "line"),
    )
    return jax.shard_map(local, mesh=mesh, in_specs=in_specs, out_specs=out_specs, check_vma=False)
```

```python
import jax
import jax.numpy as jnp
from jax import lax
from jax.sharding import PartitionSpec as P
from jax.experimental import pallas as pl
from jax.experimental.pallas import tpu as pltpu

phase_scale = 4.0
bed_phase = -1.8
coupling = 0.3


def passed_along(value, axis, by):
    count = lax.axis_size(axis)
    pairs = [(i, i + by) for i in range(count) if 0 <= i + by < count]
    return lax.ppermute(value, axis, pairs)


def pair_terms(diag_one, diag_two, cross_one, cross_two, adjoint):
    if adjoint:
        return (diag_one + diag_two, cross_one - cross_two)
    return (diag_one - diag_two, cross_one + cross_two)


def depth_apply(current, pade_ops, adjoint):
    factor_count = pade_ops.shape[0]
    sequence = range(factor_count - 1, -1, -1) if adjoint else range(factor_count)
    for factor in sequence:
        contract = 1 if adjoint else 2
        product = lax.dot_general(
            current,
            pade_ops[factor],
            (((3,), (contract,)), ((), ())),
            preferred_element_type=jnp.float32,
        )
        real_part, imag_part = pair_terms(
            product[0, :, :, 0],
            product[1, :, :, 1],
            product[1, :, :, 0],
            product[0, :, :, 1],
            adjoint,
        )
        current = jnp.stack([real_part, imag_part]).astype(jnp.bfloat16)
    return current


def azimuth_apply(field_in, inverse, adjoint):
    block_width = inverse.shape[1]
    blocked = field_in.reshape(2, field_in.shape[1] // block_width, block_width, field_in.shape[2])
    contract = 1 if adjoint else 2
    product = lax.dot_general(
        inverse, blocked, (((contract,), (2,)), ((), ())), preferred_element_type=jnp.float32
    )
    real_part, imag_part = pair_terms(
        product[0, :, 0], product[1, :, 1], product[0, :, 1], product[1, :, 0], adjoint
    )
    joined = jnp.stack([real_part, imag_part])
    return joined.transpose(0, 2, 1, 3).reshape(field_in.shape)


def numerator_map(field_in):
    return field_in + coupling * (
        jnp.roll(field_in, 1, axis=1) + jnp.roll(field_in, -1, axis=1) - 2.0 * field_in
    )


def screen_phase(profile, bottom_row, depth_start):
    depths = depth_start + jnp.arange(profile.shape[0], dtype=jnp.int32)
    in_water = depths[None, :] < bottom_row[:, None]
    water_phase = phase_scale * (1.0 / (profile * profile) - 1.0)
    return (jnp.where(in_water, water_phase[None, :], bed_phase), in_water)


def depth_segment(field_in, pade_factors, adjoint):
    block_size = pade_factors.shape[3]
    if field_in.shape[2] % block_size == 0:
        worked = depth_apply(
            field_in.reshape(2, field_in.shape[1], field_in.shape[2] // block_size, block_size),
            pade_factors,
            adjoint,
        )
        return worked.reshape(field_in.shape)
    turned = lax.all_to_all(field_in, "line", split_axis=1, concat_axis=2, tiled=True)
    full_depth = turned.shape[2]
    worked = depth_apply(
        turned.reshape(2, turned.shape[1], full_depth // block_size, block_size),
        pade_factors,
        adjoint,
    )
    return lax.all_to_all(
        worked.reshape(turned.shape), "line", split_axis=2, concat_axis=1, tiled=True
    )


def general_local(
    checkpoint, adjoint_start, misfit, pade_factors, azimuth_inverse, bottom, base_speed, speed_step
):
    depth_rows = checkpoint.shape[3]
    depth_start = lax.axis_index("line") * depth_rows
    every_step = lax.all_gather(speed_step, "range", axis=0, tiled=True)
    running = jnp.cumsum(every_step, axis=0)
    profile = base_speed + lax.dynamic_index_in_dim(
        running, lax.axis_index("range"), 0, keepdims=False
    )
    phase_angle, in_water = screen_phase(profile, bottom[0], depth_start)
    cosine = jnp.cos(phase_angle)
    sine_term = jnp.sin(phase_angle)
    source = checkpoint[0].astype(jnp.float32)
    screened = jnp.stack(
        [cosine * source[0] - sine_term * source[1], sine_term * source[0] + cosine * source[1]]
    ).astype(jnp.bfloat16)
    depth_out = depth_segment(screened, pade_factors, False)
    numerator = numerator_map(depth_out.astype(jnp.float32)).astype(jnp.bfloat16)
    inverse = azimuth_inverse[0]
    field_end = azimuth_apply(numerator, inverse, False).astype(jnp.bfloat16)
    arrival = passed_along(adjoint_start, "range", -1)
    lam_end = (arrival[0].astype(jnp.float32) + misfit[0].astype(jnp.float32)).astype(jnp.bfloat16)
    backward = numerator_map(azimuth_apply(lam_end, inverse, True)).astype(jnp.bfloat16)
    backward = depth_segment(backward, pade_factors, True)
    cotangent = backward.astype(jnp.float32)
    adjoint_begin = jnp.stack(
        [
            cosine * cotangent[0] + sine_term * cotangent[1],
            cosine * cotangent[1] - sine_term * cotangent[0],
        ]
    ).astype(jnp.bfloat16)
    screened_f = screened.astype(jnp.float32)
    weight = jnp.where(in_water, cotangent[1] * screened_f[0] - cotangent[0] * screened_f[1], 0.0)
    grad_here = (
        jnp.sum(weight, axis=0) * (-8.0 / (profile * profile * profile)) / checkpoint.shape[2]
    )[None, :]
    all_grads = lax.all_gather(grad_here, "range", axis=0, tiled=True)
    suffix = jnp.flip(jnp.cumsum(jnp.flip(all_grads, 0), axis=0), 0)
    grad_increment = lax.dynamic_slice_in_dim(suffix, lax.axis_index("range"), 1, 0)
    return (field_end[None], adjoint_begin[None], grad_increment)


def dot_nt(left, right):
    return lax.dot_general(
        left, right, (((1,), (1,)), ((), ())), preferred_element_type=jnp.float32
    )


def dot_nn(left, right):
    return jnp.dot(left, right, preferred_element_type=jnp.float32)


def numerator_rows(field_in):
    rows = field_in.shape[0]
    return field_in + coupling * (
        pltpu.roll(field_in, 1, 0) + pltpu.roll(field_in, rows - 1, 0) - 2.0 * field_in
    )


def phase_tile(trig_ref, limit_ref, block_index, shape):
    columns = lax.broadcasted_iota(jnp.int32, shape, 1) + block_index * shape[1]
    in_water = columns < limit_ref[...]
    trig = trig_ref[...]
    cosine = jnp.where(in_water, trig[0:1], trig[2:3])
    sine_term = jnp.where(in_water, trig[1:2], trig[3:4])
    return cosine, sine_term, in_water


def screen_tile(source_ref, cosine, sine_term):
    source_r = source_ref[0].astype(jnp.float32)
    source_i = source_ref[1].astype(jnp.float32)
    screened_r = (cosine * source_r - sine_term * source_i).astype(jnp.bfloat16)
    screened_i = (sine_term * source_r + cosine * source_i).astype(jnp.bfloat16)
    return screened_r, screened_i


def forward_kernel(source_ref, trig_ref, limit_ref, pade_ref, inverse_ref, out_ref):
    block_index = pl.program_id(0)
    rows, width = source_ref.shape[1], source_ref.shape[2]
    cosine, sine_term, _ = phase_tile(trig_ref, limit_ref, block_index, (rows, width))
    cur_r, cur_i = screen_tile(source_ref, cosine, sine_term)
    for factor in range(pade_ref.shape[0]):
        pade_r = pade_ref[factor, 0]
        pade_i = pade_ref[factor, 1]
        real_part = dot_nt(cur_r, pade_r) - dot_nt(cur_i, pade_i)
        imag_part = dot_nt(cur_i, pade_r) + dot_nt(cur_r, pade_i)
        cur_r = real_part.astype(jnp.bfloat16)
        cur_i = imag_part.astype(jnp.bfloat16)
    num_r = numerator_rows(cur_r.astype(jnp.float32)).astype(jnp.bfloat16)
    num_i = numerator_rows(cur_i.astype(jnp.float32)).astype(jnp.bfloat16)
    inv_r = inverse_ref[0]
    inv_i = inverse_ref[1]
    block_width = inv_r.shape[0]
    for start in range(0, rows, block_width):
        part_r = num_r[start : start + block_width]
        part_i = num_i[start : start + block_width]
        out_ref[0, start : start + block_width, :] = (
            dot_nn(inv_r, part_r) - dot_nn(inv_i, part_i)
        ).astype(jnp.bfloat16)
        out_ref[1, start : start + block_width, :] = (
            dot_nn(inv_r, part_i) + dot_nn(inv_i, part_r)
        ).astype(jnp.bfloat16)


def make_backward_kernel(block_index):
    def backward_kernel(
        arrival_ref, misfit_ref, source_ref, trig_ref, limit_ref, pade_ref, inverse_t_ref,
        out_ref, grad_ref,
    ):
        rows, width = source_ref.shape[1], source_ref.shape[2]
        lam_r = (
            arrival_ref[0].astype(jnp.float32) + misfit_ref[0].astype(jnp.float32)
        ).astype(jnp.bfloat16)
        lam_i = (
            arrival_ref[1].astype(jnp.float32) + misfit_ref[1].astype(jnp.float32)
        ).astype(jnp.bfloat16)
        inv_r = inverse_t_ref[0]
        inv_i = inverse_t_ref[1]
        block_width = inv_r.shape[0]
        pieces_r = []
        pieces_i = []
        for start in range(0, rows, block_width):
            part_r = lam_r[start : start + block_width]
            part_i = lam_i[start : start + block_width]
            pieces_r.append(dot_nn(inv_r, part_r) + dot_nn(inv_i, part_i))
            pieces_i.append(dot_nn(inv_r, part_i) - dot_nn(inv_i, part_r))
        cur_r = numerator_rows(jnp.concatenate(pieces_r, axis=0)).astype(jnp.bfloat16)
        cur_i = numerator_rows(jnp.concatenate(pieces_i, axis=0)).astype(jnp.bfloat16)
        for factor in range(pade_ref.shape[0] - 1, -1, -1):
            pade_r = pade_ref[factor, 0]
            pade_i = pade_ref[factor, 1]
            real_part = dot_nn(cur_r, pade_r) + dot_nn(cur_i, pade_i)
            imag_part = dot_nn(cur_i, pade_r) - dot_nn(cur_r, pade_i)
            cur_r = real_part.astype(jnp.bfloat16)
            cur_i = imag_part.astype(jnp.bfloat16)
        cot_r = cur_r.astype(jnp.float32)
        cot_i = cur_i.astype(jnp.float32)
        cosine, sine_term, in_water = phase_tile(trig_ref, limit_ref, block_index, (rows, width))
        out_ref[0] = (cosine * cot_r + sine_term * cot_i).astype(jnp.bfloat16)
        out_ref[1] = (cosine * cot_i - sine_term * cot_r).astype(jnp.bfloat16)
        screened_r, screened_i = screen_tile(source_ref, cosine, sine_term)
        weight = jnp.where(
            in_water,
            cot_i * screened_r.astype(jnp.float32) - cot_r * screened_i.astype(jnp.float32),
            0.0,
        )
        grad_ref[...] = jnp.sum(weight, axis=0, keepdims=True)

    return backward_kernel


def lam_rows(arrival, misfit_part):
    return (arrival.astype(jnp.float32) + misfit_part.astype(jnp.float32)).astype(jnp.bfloat16)


def azimuth_adjoint(inv_r, inv_i, part_r, part_i):
    return (
        dot_nn(inv_r, part_r) + dot_nn(inv_i, part_i),
        dot_nn(inv_r, part_i) - dot_nn(inv_i, part_r),
    )


def depth_adjoint(cur_r, cur_i, pade_ref):
    for factor in range(pade_ref.shape[0] - 1, -1, -1):
        pade_r = pade_ref[factor, 0]
        pade_i = pade_ref[factor, 1]
        real_part = dot_nn(cur_r, pade_r) + dot_nn(cur_i, pade_i)
        imag_part = dot_nn(cur_i, pade_r) - dot_nn(cur_r, pade_i)
        cur_r = real_part.astype(jnp.bfloat16)
        cur_i = imag_part.astype(jnp.bfloat16)
    return cur_r.astype(jnp.float32), cur_i.astype(jnp.float32)


def finish_rows(cot_r, cot_i, trig_ref, limit_rows, source_r, source_i, block_index):
    shape = cot_r.shape
    columns = lax.broadcasted_iota(jnp.int32, shape, 1) + block_index * shape[1]
    in_water = columns < limit_rows
    trig = trig_ref[...]
    cosine = jnp.where(in_water, trig[0:1], trig[2:3])
    sine_term = jnp.where(in_water, trig[1:2], trig[3:4])
    out_r = cosine * cot_r + sine_term * cot_i
    out_i = cosine * cot_i - sine_term * cot_r
    screened_r = (cosine * source_r - sine_term * source_i).astype(jnp.bfloat16)
    screened_i = (sine_term * source_r + cosine * source_i).astype(jnp.bfloat16)
    weight = jnp.where(
        in_water,
        cot_i * screened_r.astype(jnp.float32) - cot_r * screened_i.astype(jnp.float32),
        0.0,
    )
    return out_r, out_i, jnp.sum(weight, axis=0, keepdims=True)


HALO = 8


def make_first_half_kernel(block_index):
    def kernel(
        arrival_ref, misfit_ref, source_ref, trig_ref, limit_ref, pade_ref, inverse_t_ref,
        begin_in, begin_out, grad_ref, stage_ref, copy_sem,
    ):
        half, width = arrival_ref.shape[1], arrival_ref.shape[2]
        lam_r = lam_rows(arrival_ref[0], misfit_ref[0, :half])
        lam_i = lam_rows(arrival_ref[1], misfit_ref[1, :half])
        inv_r = inverse_t_ref[0]
        inv_i = inverse_t_ref[1]
        block_width = inv_r.shape[0]
        pieces_r = []
        pieces_i = []
        for start in range(0, half, block_width):
            piece_r, piece_i = azimuth_adjoint(
                inv_r, inv_i, lam_r[start : start + block_width], lam_i[start : start + block_width]
            )
            pieces_r.append(piece_r)
            pieces_i.append(piece_i)
        num_r = numerator_rows(jnp.concatenate(pieces_r, axis=0))[HALO : half - HALO]
        num_i = numerator_rows(jnp.concatenate(pieces_i, axis=0))[HALO : half - HALO]
        cot_r, cot_i = depth_adjoint(
            num_r.astype(jnp.bfloat16), num_i.astype(jnp.bfloat16), pade_ref
        )
        source_r = source_ref[0, :half].astype(jnp.float32)[HALO : half - HALO]
        source_i = source_ref[1, :half].astype(jnp.float32)[HALO : half - HALO]
        out_r, out_i, grad_row = finish_rows(
            cot_r, cot_i, trig_ref, limit_ref[HALO : half - HALO], source_r, source_i, block_index
        )
        stage_ref[0] = out_r.astype(jnp.bfloat16)
        stage_ref[1] = out_i.astype(jnp.bfloat16)
        copy = pltpu.make_async_copy(
            stage_ref,
            begin_out.at[0, :, pl.ds(HALO, half - 2 * HALO), pl.ds(block_index * width, width)],
            copy_sem.at[0],
        )
        copy.start()
        grad_ref[...] = grad_row
        copy.wait()

    return kernel


def make_second_half_kernel(block_index):
    def kernel(
        first_ref, arrival_ref, misfit_ref, source_ref, trig_ref, limit_ref, pade_ref,
        inverse_t_ref, begin_in, begin_out, grad_ref, main_ref, wrap_ref, copy_sem,
    ):
        half, width = first_ref.shape[1], arrival_ref.shape[2]
        tail = arrival_ref.shape[1]
        inv_r = inverse_t_ref[0]
        inv_i = inverse_t_ref[1]
        block_width = inv_r.shape[0]
        edge = 2 * HALO
        lam_r = lam_rows(arrival_ref[0], misfit_ref[0, half:])
        lam_i = lam_rows(arrival_ref[1], misfit_ref[1, half:])
        top_r = lam_rows(first_ref[0, half - block_width :], misfit_ref[0, half - block_width : half])
        top_i = lam_rows(first_ref[1, half - block_width :], misfit_ref[1, half - block_width : half])
        low_r = lam_rows(first_ref[0, :block_width], misfit_ref[0, :block_width])
        low_i = lam_rows(first_ref[1, :block_width], misfit_ref[1, :block_width])
        before_r, before_i = azimuth_adjoint(
            inverse_t_ref[0, block_width - edge :], inverse_t_ref[1, block_width - edge :],
            top_r, top_i,
        )
        after_r, after_i = azimuth_adjoint(
            inverse_t_ref[0, :edge], inverse_t_ref[1, :edge], low_r, low_i
        )
        pieces_r = [before_r]
        pieces_i = [before_i]
        for start in range(0, tail, block_width):
            piece_r, piece_i = azimuth_adjoint(
                inv_r, inv_i, lam_r[start : start + block_width], lam_i[start : start + block_width]
            )
            pieces_r.append(piece_r)
            pieces_i.append(piece_i)
        pieces_r.append(after_r)
        pieces_i.append(after_i)
        span = tail + 2 * HALO
        num_r = numerator_rows(jnp.concatenate(pieces_r, axis=0))[HALO : HALO + span]
        num_i = numerator_rows(jnp.concatenate(pieces_i, axis=0))[HALO : HALO + span]
        cot_r, cot_i = depth_adjoint(
            num_r.astype(jnp.bfloat16), num_i.astype(jnp.bfloat16), pade_ref
        )
        full_r = source_ref[0].astype(jnp.float32)
        full_i = source_ref[1].astype(jnp.float32)
        source_r = jnp.concatenate([full_r[half - HALO :], full_r[:HALO]], axis=0)
        source_i = jnp.concatenate([full_i[half - HALO :], full_i[:HALO]], axis=0)
        limit_rows = jnp.concatenate([limit_ref[half - HALO :], limit_ref[:HALO]], axis=0)
        out_r, out_i, grad_row = finish_rows(
            cot_r, cot_i, trig_ref, limit_rows, source_r, source_i, block_index
        )
        main_ref[0] = out_r[: tail + HALO].astype(jnp.bfloat16)
        main_ref[1] = out_i[: tail + HALO].astype(jnp.bfloat16)
        wrap_ref[0] = out_r[tail + HALO :].astype(jnp.bfloat16)
        wrap_ref[1] = out_i[tail + HALO :].astype(jnp.bfloat16)
        columns = pl.ds(block_index * width, width)
        main_copy = pltpu.make_async_copy(
            main_ref, begin_out.at[0, :, pl.ds(half - HALO, tail + HALO), columns], copy_sem.at[0]
        )
        wrap_copy = pltpu.make_async_copy(
            wrap_ref, begin_out.at[0, :, pl.ds(0, HALO), columns], copy_sem.at[1]
        )
        main_copy.start()
        wrap_copy.start()
        grad_ref[...] = grad_row
        main_copy.wait()
        wrap_copy.wait()

    return kernel


def range_scan(value, direction):
    count = lax.axis_size("range")
    total = value
    for reach in range(1, count):
        total = total + passed_along(value, "range", direction * reach)
    return total


def fused_local(
    checkpoint, adjoint_start, misfit, pade_factors, azimuth_inverse, bottom, base_speed, speed_step
):
    depth_rows = checkpoint.shape[3]
    rows = checkpoint.shape[2]
    block_size = pade_factors.shape[3]
    block_count = depth_rows // block_size
    depth_start = lax.axis_index("line") * depth_rows
    half = rows - azimuth_inverse.shape[2]
    tail = rows - half
    last = block_count - 1
    arrivals = [
        passed_along(
            adjoint_start[:, :, :, index * block_size : (index + 1) * block_size], "range", -1
        )
        for index in range(last)
    ]
    last_columns = adjoint_start[:, :, :, last * block_size :]
    first_half = passed_along(last_columns[:, :, :half], "range", -1)
    second_half = passed_along(last_columns[:, :, half:], "range", -1)
    halves = [first_half, second_half]
    profile = base_speed + range_scan(speed_step, 1)[0]
    water_phase = phase_scale * (1.0 / (profile * profile) - 1.0)
    bed_row = jnp.full_like(water_phase, bed_phase)
    trig = jnp.stack(
        [jnp.cos(water_phase), jnp.sin(water_phase), jnp.cos(bed_row), jnp.sin(bed_row)]
    )
    limit = (bottom[0] - depth_start)[:, None]
    inverse = azimuth_inverse[0]
    inverse_t = jnp.swapaxes(inverse, 1, 2)
    field_spec = pl.BlockSpec((None, 2, rows, block_size), lambda b: (0, 0, 0, b))
    trig_spec = pl.BlockSpec((4, block_size), lambda b: (0, b))
    limit_spec = pl.BlockSpec((rows, 1), lambda b: (0, 0))
    pade_spec = pl.BlockSpec(pade_factors.shape, lambda b: (0, 0, 0, 0))
    inverse_spec = pl.BlockSpec(inverse.shape, lambda b: (0, 0, 0))
    field_end = pl.pallas_call(
        forward_kernel,
        grid=(block_count,),
        in_specs=[field_spec, trig_spec, limit_spec, pade_spec, inverse_spec],
        out_specs=field_spec,
        out_shape=jax.ShapeDtypeStruct(checkpoint.shape, jnp.bfloat16),
    )(checkpoint, trig, limit, pade_factors, inverse)
    field_end, arrivals[0] = lax.optimization_barrier((field_end, arrivals[0]))
    adjoint_begin = None
    grads = []
    for index in range(last):
        fixed = lambda b, index=index: (0, 0, 0, index)
        chunk_spec = pl.BlockSpec((None, 2, rows, block_size), lambda b: (0, 0, 0, 0))
        block_spec = pl.BlockSpec((None, 2, rows, block_size), fixed)
        in_specs = [
            chunk_spec,
            block_spec,
            block_spec,
            pl.BlockSpec((4, block_size), lambda b, index=index: (0, index)),
            limit_spec,
            pade_spec,
            inverse_spec,
        ]
        operands = [arrivals[index], misfit, checkpoint, trig, limit, pade_factors, inverse_t]
        aliases = {}
        kernel = make_backward_kernel(index)
        if adjoint_begin is not None:
            in_specs.append(pl.BlockSpec(memory_space=pl.ANY))
            operands.append(adjoint_begin)
            aliases = {len(operands) - 1: 0}
            kernel = lambda *refs, kernel=kernel: kernel(*refs[:7], *refs[8:])
        adjoint_begin, grad_part = pl.pallas_call(
            kernel,
            grid=(1,),
            in_specs=in_specs,
            out_specs=[
                block_spec,
                pl.BlockSpec((1, block_size), lambda b: (0, 0)),
            ],
            out_shape=[
                jax.ShapeDtypeStruct(checkpoint.shape, jnp.bfloat16),
                jax.ShapeDtypeStruct((1, block_size), jnp.float32),
            ],
            input_output_aliases=aliases,
        )(*operands)
        grads.append(grad_part)
    any_spec = pl.BlockSpec(memory_space=pl.ANY)
    fixed_last = lambda b: (0, 0, 0, last)
    half_spec = pl.BlockSpec((None, 2, half, block_size), lambda b: (0, 0, 0, 0))
    tail_spec = pl.BlockSpec((None, 2, tail, block_size), lambda b: (0, 0, 0, 0))
    trig_last = pl.BlockSpec((4, block_size), lambda b: (0, last))
    grad_spec = pl.BlockSpec((1, block_size), lambda b: (0, 0))
    begin_shape = jax.ShapeDtypeStruct(checkpoint.shape, jnp.bfloat16)
    grad_shape = jax.ShapeDtypeStruct((1, block_size), jnp.float32)
    adjoint_begin, grad_first = pl.pallas_call(
        make_first_half_kernel(last),
        grid=(1,),
        in_specs=[
            half_spec,
            pl.BlockSpec((None, 2, rows, block_size), fixed_last),
            pl.BlockSpec((None, 2, rows, block_size), fixed_last),
            trig_last,
            limit_spec,
            pade_spec,
            inverse_spec,
            any_spec,
        ],
        out_specs=[any_spec, grad_spec],
        out_shape=[begin_shape, grad_shape],
        scratch_shapes=[
            pltpu.VMEM((2, half - 2 * HALO, block_size), jnp.bfloat16),
            pltpu.SemaphoreType.DMA((1,)),
        ],
        input_output_aliases={7: 0},
    )(halves[0], misfit, checkpoint, trig, limit, pade_factors, inverse_t, adjoint_begin)
    full_last = pl.BlockSpec((None, 2, rows, block_size), fixed_last)
    adjoint_begin, grad_second = pl.pallas_call(
        make_second_half_kernel(last),
        grid=(1,),
        in_specs=[
            half_spec,
            tail_spec,
            full_last,
            full_last,
            trig_last,
            limit_spec,
            pade_spec,
            inverse_spec,
            any_spec,
        ],
        out_specs=[any_spec, grad_spec],
        out_shape=[begin_shape, grad_shape],
        scratch_shapes=[
            pltpu.VMEM((2, tail + HALO, block_size), jnp.bfloat16),
            pltpu.VMEM((2, HALO, block_size), jnp.bfloat16),
            pltpu.SemaphoreType.DMA((2,)),
        ],
        input_output_aliases={8: 0},
    )(
        halves[0], halves[1], misfit, checkpoint, trig, limit, pade_factors, inverse_t,
        adjoint_begin,
    )
    grads.append(grad_first + grad_second)
    grad_sum = jnp.concatenate(grads, axis=1)
    grad_here = grad_sum * (-8.0 / (profile * profile * profile)) / rows
    grad_increment = range_scan(grad_here, -1)
    return (field_end, adjoint_begin, grad_increment)


def local(
    checkpoint, adjoint_start, misfit, pade_factors, azimuth_inverse, bottom, base_speed, speed_step
):
    if (
        checkpoint.shape[3] % pade_factors.shape[3] == 0
        and checkpoint.shape[3] >= 2 * pade_factors.shape[3]
        and checkpoint.shape[2] % (2 * azimuth_inverse.shape[2]) == 0
    ):
        return fused_local(
            checkpoint, adjoint_start, misfit, pade_factors, azimuth_inverse, bottom,
            base_speed, speed_step,
        )
    return general_local(
        checkpoint, adjoint_start, misfit, pade_factors, azimuth_inverse, bottom,
        base_speed, speed_step,
    )


def solution(mesh):
    in_specs = (
        P("range", "freq", None, "line"),
        P("range", "freq", None, "line"),
        P("range", "freq", None, "line"),
        P(None, "freq", None, None),
        P("range", "freq", None, None),
        P("range", None),
        P("line"),
        P("range", "line"),
    )
    out_specs = (
        P("range", "freq", None, "line"),
        P("range", "freq", None, "line"),
        P(("freq", "range"), "line"),
    )
    return jax.shard_map(local, mesh=mesh, in_specs=in_specs, out_specs=out_specs, check_vma=False)
```

```python
import jax
import jax.numpy as jnp
from jax import lax
from jax.sharding import PartitionSpec as P
from jax.experimental import pallas as pl
from jax.experimental.pallas import tpu as pltpu

phase_scale = 4.0
bed_phase = -1.8
coupling = 0.3


def passed_along(value, axis, by):
    count = lax.axis_size(axis)
    pairs = [(i, i + by) for i in range(count) if 0 <= i + by < count]
    return lax.ppermute(value, axis, pairs)


def pair_terms(diag_one, diag_two, cross_one, cross_two, adjoint):
    if adjoint:
        return (diag_one + diag_two, cross_one - cross_two)
    return (diag_one - diag_two, cross_one + cross_two)


def depth_apply(current, pade_ops, adjoint):
    factor_count = pade_ops.shape[0]
    sequence = range(factor_count - 1, -1, -1) if adjoint else range(factor_count)
    for factor in sequence:
        contract = 1 if adjoint else 2
        product = lax.dot_general(
            current,
            pade_ops[factor],
            (((3,), (contract,)), ((), ())),
            preferred_element_type=jnp.float32,
        )
        real_part, imag_part = pair_terms(
            product[0, :, :, 0],
            product[1, :, :, 1],
            product[1, :, :, 0],
            product[0, :, :, 1],
            adjoint,
        )
        current = jnp.stack([real_part, imag_part]).astype(jnp.bfloat16)
    return current


def azimuth_apply(field_in, inverse, adjoint):
    block_width = inverse.shape[1]
    blocked = field_in.reshape(2, field_in.shape[1] // block_width, block_width, field_in.shape[2])
    contract = 1 if adjoint else 2
    product = lax.dot_general(
        inverse, blocked, (((contract,), (2,)), ((), ())), preferred_element_type=jnp.float32
    )
    real_part, imag_part = pair_terms(
        product[0, :, 0], product[1, :, 1], product[0, :, 1], product[1, :, 0], adjoint
    )
    joined = jnp.stack([real_part, imag_part])
    return joined.transpose(0, 2, 1, 3).reshape(field_in.shape)


def numerator_map(field_in):
    return field_in + coupling * (
        jnp.roll(field_in, 1, axis=1) + jnp.roll(field_in, -1, axis=1) - 2.0 * field_in
    )


def screen_phase(profile, bottom_row, depth_start):
    depths = depth_start + jnp.arange(profile.shape[0], dtype=jnp.int32)
    in_water = depths[None, :] < bottom_row[:, None]
    water_phase = phase_scale * (1.0 / (profile * profile) - 1.0)
    return (jnp.where(in_water, water_phase[None, :], bed_phase), in_water)


def depth_segment(field_in, pade_factors, adjoint):
    block_size = pade_factors.shape[3]
    if field_in.shape[2] % block_size == 0:
        worked = depth_apply(
            field_in.reshape(2, field_in.shape[1], field_in.shape[2] // block_size, block_size),
            pade_factors,
            adjoint,
        )
        return worked.reshape(field_in.shape)
    turned = lax.all_to_all(field_in, "line", split_axis=1, concat_axis=2, tiled=True)
    full_depth = turned.shape[2]
    worked = depth_apply(
        turned.reshape(2, turned.shape[1], full_depth // block_size, block_size),
        pade_factors,
        adjoint,
    )
    return lax.all_to_all(
        worked.reshape(turned.shape), "line", split_axis=2, concat_axis=1, tiled=True
    )


def general_local(
    checkpoint, adjoint_start, misfit, pade_factors, azimuth_inverse, bottom, base_speed, speed_step
):
    depth_rows = checkpoint.shape[3]
    depth_start = lax.axis_index("line") * depth_rows
    every_step = lax.all_gather(speed_step, "range", axis=0, tiled=True)
    running = jnp.cumsum(every_step, axis=0)
    profile = base_speed + lax.dynamic_index_in_dim(
        running, lax.axis_index("range"), 0, keepdims=False
    )
    phase_angle, in_water = screen_phase(profile, bottom[0], depth_start)
    cosine = jnp.cos(phase_angle)
    sine_term = jnp.sin(phase_angle)
    source = checkpoint[0].astype(jnp.float32)
    screened = jnp.stack(
        [cosine * source[0] - sine_term * source[1], sine_term * source[0] + cosine * source[1]]
    ).astype(jnp.bfloat16)
    depth_out = depth_segment(screened, pade_factors, False)
    numerator = numerator_map(depth_out.astype(jnp.float32)).astype(jnp.bfloat16)
    inverse = azimuth_inverse[0]
    field_end = azimuth_apply(numerator, inverse, False).astype(jnp.bfloat16)
    arrival = passed_along(adjoint_start, "range", -1)
    lam_end = (arrival[0].astype(jnp.float32) + misfit[0].astype(jnp.float32)).astype(jnp.bfloat16)
    backward = numerator_map(azimuth_apply(lam_end, inverse, True)).astype(jnp.bfloat16)
    backward = depth_segment(backward, pade_factors, True)
    cotangent = backward.astype(jnp.float32)
    adjoint_begin = jnp.stack(
        [
            cosine * cotangent[0] + sine_term * cotangent[1],
            cosine * cotangent[1] - sine_term * cotangent[0],
        ]
    ).astype(jnp.bfloat16)
    screened_f = screened.astype(jnp.float32)
    weight = jnp.where(in_water, cotangent[1] * screened_f[0] - cotangent[0] * screened_f[1], 0.0)
    grad_here = (
        jnp.sum(weight, axis=0) * (-8.0 / (profile * profile * profile)) / checkpoint.shape[2]
    )[None, :]
    all_grads = lax.all_gather(grad_here, "range", axis=0, tiled=True)
    suffix = jnp.flip(jnp.cumsum(jnp.flip(all_grads, 0), axis=0), 0)
    grad_increment = lax.dynamic_slice_in_dim(suffix, lax.axis_index("range"), 1, 0)
    return (field_end[None], adjoint_begin[None], grad_increment)


def dot_nt(left, right):
    return lax.dot_general(
        left, right, (((1,), (1,)), ((), ())), preferred_element_type=jnp.float32
    )


def dot_nn(left, right):
    return jnp.dot(left, right, preferred_element_type=jnp.float32)


def numerator_rows(field_in):
    rows = field_in.shape[0]
    return field_in + coupling * (
        pltpu.roll(field_in, 1, 0) + pltpu.roll(field_in, rows - 1, 0) - 2.0 * field_in
    )


def phase_tile(trig_ref, limit_ref, block_index, shape):
    columns = lax.broadcasted_iota(jnp.int32, shape, 1) + block_index * shape[1]
    in_water = columns < limit_ref[...]
    trig = trig_ref[...]
    cosine = jnp.where(in_water, trig[0:1], trig[2:3])
    sine_term = jnp.where(in_water, trig[1:2], trig[3:4])
    return cosine, sine_term, in_water


def screen_tile(source_ref, cosine, sine_term):
    source_r = source_ref[0].astype(jnp.float32)
    source_i = source_ref[1].astype(jnp.float32)
    screened_r = (cosine * source_r - sine_term * source_i).astype(jnp.bfloat16)
    screened_i = (sine_term * source_r + cosine * source_i).astype(jnp.bfloat16)
    return screened_r, screened_i


def forward_kernel(source_ref, trig_ref, limit_ref, pade_ref, inverse_ref, out_ref):
    block_index = pl.program_id(0)
    rows, width = source_ref.shape[1], source_ref.shape[2]
    cosine, sine_term, _ = phase_tile(trig_ref, limit_ref, block_index, (rows, width))
    cur_r, cur_i = screen_tile(source_ref, cosine, sine_term)
    for factor in range(pade_ref.shape[0]):
        pade_r = pade_ref[factor, 0]
        pade_i = pade_ref[factor, 1]
        real_part = dot_nt(cur_r, pade_r) - dot_nt(cur_i, pade_i)
        imag_part = dot_nt(cur_i, pade_r) + dot_nt(cur_r, pade_i)
        cur_r = real_part.astype(jnp.bfloat16)
        cur_i = imag_part.astype(jnp.bfloat16)
    num_r = numerator_rows(cur_r.astype(jnp.float32)).astype(jnp.bfloat16)
    num_i = numerator_rows(cur_i.astype(jnp.float32)).astype(jnp.bfloat16)
    inv_r = inverse_ref[0]
    inv_i = inverse_ref[1]
    block_width = inv_r.shape[0]
    for start in range(0, rows, block_width):
        part_r = num_r[start : start + block_width]
        part_i = num_i[start : start + block_width]
        out_ref[0, start : start + block_width, :] = (
            dot_nn(inv_r, part_r) - dot_nn(inv_i, part_i)
        ).astype(jnp.bfloat16)
        out_ref[1, start : start + block_width, :] = (
            dot_nn(inv_r, part_i) + dot_nn(inv_i, part_r)
        ).astype(jnp.bfloat16)


def make_backward_kernel(block_index):
    def backward_kernel(
        arrival_ref, misfit_ref, source_ref, trig_ref, limit_ref, pade_ref, inverse_t_ref,
        out_ref, grad_ref,
    ):
        rows, width = source_ref.shape[1], source_ref.shape[2]
        lam_r = (
            arrival_ref[0].astype(jnp.float32) + misfit_ref[0].astype(jnp.float32)
        ).astype(jnp.bfloat16)
        lam_i = (
            arrival_ref[1].astype(jnp.float32) + misfit_ref[1].astype(jnp.float32)
        ).astype(jnp.bfloat16)
        inv_r = inverse_t_ref[0]
        inv_i = inverse_t_ref[1]
        block_width = inv_r.shape[0]
        pieces_r = []
        pieces_i = []
        for start in range(0, rows, block_width):
            part_r = lam_r[start : start + block_width]
            part_i = lam_i[start : start + block_width]
            pieces_r.append(dot_nn(inv_r, part_r) + dot_nn(inv_i, part_i))
            pieces_i.append(dot_nn(inv_r, part_i) - dot_nn(inv_i, part_r))
        cur_r = numerator_rows(jnp.concatenate(pieces_r, axis=0)).astype(jnp.bfloat16)
        cur_i = numerator_rows(jnp.concatenate(pieces_i, axis=0)).astype(jnp.bfloat16)
        for factor in range(pade_ref.shape[0] - 1, -1, -1):
            pade_r = pade_ref[factor, 0]
            pade_i = pade_ref[factor, 1]
            real_part = dot_nn(cur_r, pade_r) + dot_nn(cur_i, pade_i)
            imag_part = dot_nn(cur_i, pade_r) - dot_nn(cur_r, pade_i)
            cur_r = real_part.astype(jnp.bfloat16)
            cur_i = imag_part.astype(jnp.bfloat16)
        cot_r = cur_r.astype(jnp.float32)
        cot_i = cur_i.astype(jnp.float32)
        cosine, sine_term, in_water = phase_tile(trig_ref, limit_ref, block_index, (rows, width))
        out_ref[0] = (cosine * cot_r + sine_term * cot_i).astype(jnp.bfloat16)
        out_ref[1] = (cosine * cot_i - sine_term * cot_r).astype(jnp.bfloat16)
        screened_r, screened_i = screen_tile(source_ref, cosine, sine_term)
        weight = jnp.where(
            in_water,
            cot_i * screened_r.astype(jnp.float32) - cot_r * screened_i.astype(jnp.float32),
            0.0,
        )
        grad_ref[...] = jnp.sum(weight, axis=0, keepdims=True)

    return backward_kernel


def lam_rows(arrival, misfit_part):
    return (arrival.astype(jnp.float32) + misfit_part.astype(jnp.float32)).astype(jnp.bfloat16)


def azimuth_adjoint(inv_r, inv_i, part_r, part_i):
    return (
        dot_nn(inv_r, part_r) + dot_nn(inv_i, part_i),
        dot_nn(inv_r, part_i) - dot_nn(inv_i, part_r),
    )


def depth_adjoint(cur_r, cur_i, pade_ref):
    for factor in range(pade_ref.shape[0] - 1, -1, -1):
        pade_r = pade_ref[factor, 0]
        pade_i = pade_ref[factor, 1]
        real_part = dot_nn(cur_r, pade_r) + dot_nn(cur_i, pade_i)
        imag_part = dot_nn(cur_i, pade_r) - dot_nn(cur_r, pade_i)
        cur_r = real_part.astype(jnp.bfloat16)
        cur_i = imag_part.astype(jnp.bfloat16)
    return cur_r.astype(jnp.float32), cur_i.astype(jnp.float32)


def finish_rows(cot_r, cot_i, trig_ref, limit_rows, source_r, source_i, block_index):
    shape = cot_r.shape
    columns = lax.broadcasted_iota(jnp.int32, shape, 1) + block_index * shape[1]
    in_water = columns < limit_rows
    trig = trig_ref[...]
    cosine = jnp.where(in_water, trig[0:1], trig[2:3])
    sine_term = jnp.where(in_water, trig[1:2], trig[3:4])
    out_r = cosine * cot_r + sine_term * cot_i
    out_i = cosine * cot_i - sine_term * cot_r
    screened_r = (cosine * source_r - sine_term * source_i).astype(jnp.bfloat16)
    screened_i = (sine_term * source_r + cosine * source_i).astype(jnp.bfloat16)
    weight = jnp.where(
        in_water,
        cot_i * screened_r.astype(jnp.float32) - cot_r * screened_i.astype(jnp.float32),
        0.0,
    )
    return out_r, out_i, jnp.sum(weight, axis=0, keepdims=True)


HALO = 8


def make_first_half_kernel(block_index):
    def kernel(
        arrival_ref, misfit_ref, source_ref, trig_ref, limit_ref, pade_ref, inverse_t_ref,
        begin_in, begin_out, grad_ref, halo_ref, stage_ref, copy_sem,
    ):
        half, width = arrival_ref.shape[1], arrival_ref.shape[2]
        lam_r = lam_rows(arrival_ref[0], misfit_ref[0])
        lam_i = lam_rows(arrival_ref[1], misfit_ref[1])
        inv_r = inverse_t_ref[0]
        inv_i = inverse_t_ref[1]
        block_width = inv_r.shape[0]
        pieces_r = []
        pieces_i = []
        for start in range(0, half, block_width):
            piece_r, piece_i = azimuth_adjoint(
                inv_r, inv_i, lam_r[start : start + block_width], lam_i[start : start + block_width]
            )
            pieces_r.append(piece_r)
            pieces_i.append(piece_i)
        whole_r = jnp.concatenate(pieces_r, axis=0)
        whole_i = jnp.concatenate(pieces_i, axis=0)
        edge = 2 * HALO
        halo_ref[0] = whole_r[half - edge :]
        halo_ref[1] = whole_i[half - edge :]
        halo_ref[2] = whole_r[:edge]
        halo_ref[3] = whole_i[:edge]
        num_r = numerator_rows(whole_r)[HALO : half - HALO]
        num_i = numerator_rows(whole_i)[HALO : half - HALO]
        cot_r, cot_i = depth_adjoint(
            num_r.astype(jnp.bfloat16), num_i.astype(jnp.bfloat16), pade_ref
        )
        source_r = source_ref[0].astype(jnp.float32)[HALO : half - HALO]
        source_i = source_ref[1].astype(jnp.float32)[HALO : half - HALO]
        out_r, out_i, grad_row = finish_rows(
            cot_r, cot_i, trig_ref, limit_ref[HALO : half - HALO], source_r, source_i, block_index
        )
        stage_ref[0] = out_r.astype(jnp.bfloat16)
        stage_ref[1] = out_i.astype(jnp.bfloat16)
        copy = pltpu.make_async_copy(
            stage_ref,
            begin_out.at[0, :, pl.ds(HALO, half - 2 * HALO), pl.ds(block_index * width, width)],
            copy_sem.at[0],
        )
        copy.start()
        grad_ref[...] = grad_row
        copy.wait()

    return kernel


def make_second_half_kernel(block_index):
    def kernel(
        halo_ref, arrival_ref, misfit_ref, source_hbm, trig_ref, limit_hbm, pade_hbm,
        inverse_t_ref, begin_in, begin_out, grad_ref, pade_ref, source_main, source_wrap,
        limit_main, limit_wrap, main_ref, wrap_ref, copy_sem,
    ):
        tail, width = arrival_ref.shape[1], arrival_ref.shape[2]
        half = source_hbm.shape[2] - tail
        columns = pl.ds(block_index * width, width)
        loads = [
            pltpu.make_async_copy(pade_hbm, pade_ref, copy_sem.at[0]),
            pltpu.make_async_copy(
                source_hbm.at[0, :, pl.ds(half - HALO, tail + HALO), columns],
                source_main,
                copy_sem.at[1],
            ),
            pltpu.make_async_copy(
                source_hbm.at[0, :, pl.ds(0, HALO), columns], source_wrap, copy_sem.at[2]
            ),
            pltpu.make_async_copy(
                limit_hbm.at[pl.ds(half - HALO, tail + HALO)], limit_main, copy_sem.at[3]
            ),
            pltpu.make_async_copy(limit_hbm.at[pl.ds(0, HALO)], limit_wrap, copy_sem.at[4]),
        ]
        for load in loads:
            load.start()
        inv_r = inverse_t_ref[0]
        inv_i = inverse_t_ref[1]
        block_width = inv_r.shape[0]
        lam_r = lam_rows(arrival_ref[0], misfit_ref[0])
        lam_i = lam_rows(arrival_ref[1], misfit_ref[1])
        pieces_r = [halo_ref[0]]
        pieces_i = [halo_ref[1]]
        for start in range(0, tail, block_width):
            piece_r, piece_i = azimuth_adjoint(
                inv_r, inv_i, lam_r[start : start + block_width], lam_i[start : start + block_width]
            )
            pieces_r.append(piece_r)
            pieces_i.append(piece_i)
        pieces_r.append(halo_ref[2])
        pieces_i.append(halo_ref[3])
        span = tail + 2 * HALO
        num_r = numerator_rows(jnp.concatenate(pieces_r, axis=0))[HALO : HALO + span]
        num_i = numerator_rows(jnp.concatenate(pieces_i, axis=0))[HALO : HALO + span]
        loads[0].wait()
        cot_r, cot_i = depth_adjoint(
            num_r.astype(jnp.bfloat16), num_i.astype(jnp.bfloat16), pade_ref
        )
        for load in loads[1:]:
            load.wait()
        source_r = jnp.concatenate(
            [source_main[0].astype(jnp.float32), source_wrap[0].astype(jnp.float32)], axis=0
        )
        source_i = jnp.concatenate(
            [source_main[1].astype(jnp.float32), source_wrap[1].astype(jnp.float32)], axis=0
        )
        limit_rows = jnp.concatenate([limit_main[...], limit_wrap[...]], axis=0)
        out_r, out_i, grad_row = finish_rows(
            cot_r, cot_i, trig_ref, limit_rows, source_r, source_i, block_index
        )
        main_ref[0] = out_r[: tail + HALO].astype(jnp.bfloat16)
        main_ref[1] = out_i[: tail + HALO].astype(jnp.bfloat16)
        wrap_ref[0] = out_r[tail + HALO :].astype(jnp.bfloat16)
        wrap_ref[1] = out_i[tail + HALO :].astype(jnp.bfloat16)
        main_copy = pltpu.make_async_copy(
            main_ref, begin_out.at[0, :, pl.ds(half - HALO, tail + HALO), columns], copy_sem.at[5]
        )
        wrap_copy = pltpu.make_async_copy(
            wrap_ref, begin_out.at[0, :, pl.ds(0, HALO), columns], copy_sem.at[6]
        )
        main_copy.start()
        wrap_copy.start()
        grad_ref[...] = grad_row
        main_copy.wait()
        wrap_copy.wait()

    return kernel


def range_scan(value, direction):
    count = lax.axis_size("range")
    total = value
    for reach in range(1, count):
        total = total + passed_along(value, "range", direction * reach)
    return total


def fused_local(
    checkpoint, adjoint_start, misfit, pade_factors, azimuth_inverse, bottom, base_speed, speed_step
):
    depth_rows = checkpoint.shape[3]
    rows = checkpoint.shape[2]
    block_size = pade_factors.shape[3]
    block_count = depth_rows // block_size
    depth_start = lax.axis_index("line") * depth_rows
    half = rows // 2
    last = block_count - 1
    arrivals = [
        passed_along(
            adjoint_start[:, :, :, index * block_size : (index + 1) * block_size], "range", -1
        )
        for index in range(last)
    ]
    last_columns = adjoint_start[:, :, :, last * block_size :]
    first_half = passed_along(last_columns[:, :, :half], "range", -1)
    second_half = passed_along(last_columns[:, :, half:], "range", -1)
    halves = [first_half, second_half]
    profile = base_speed + range_scan(speed_step, 1)[0]
    water_phase = phase_scale * (1.0 / (profile * profile) - 1.0)
    bed_row = jnp.full_like(water_phase, bed_phase)
    trig = jnp.stack(
        [jnp.cos(water_phase), jnp.sin(water_phase), jnp.cos(bed_row), jnp.sin(bed_row)]
    )
    limit = (bottom[0] - depth_start)[:, None]
    inverse = azimuth_inverse[0]
    inverse_t = jnp.swapaxes(inverse, 1, 2)
    field_spec = pl.BlockSpec((None, 2, rows, block_size), lambda b: (0, 0, 0, b))
    trig_spec = pl.BlockSpec((4, block_size), lambda b: (0, b))
    limit_spec = pl.BlockSpec((rows, 1), lambda b: (0, 0))
    pade_spec = pl.BlockSpec(pade_factors.shape, lambda b: (0, 0, 0, 0))
    inverse_spec = pl.BlockSpec(inverse.shape, lambda b: (0, 0, 0))
    field_end = pl.pallas_call(
        forward_kernel,
        grid=(block_count,),
        in_specs=[field_spec, trig_spec, limit_spec, pade_spec, inverse_spec],
        out_specs=field_spec,
        out_shape=jax.ShapeDtypeStruct(checkpoint.shape, jnp.bfloat16),
    )(checkpoint, trig, limit, pade_factors, inverse)
    field_end, arrivals[0] = lax.optimization_barrier((field_end, arrivals[0]))
    adjoint_begin = None
    grads = []
    for index in range(last):
        fixed = lambda b, index=index: (0, 0, 0, index)
        chunk_spec = pl.BlockSpec((None, 2, rows, block_size), lambda b: (0, 0, 0, 0))
        block_spec = pl.BlockSpec((None, 2, rows, block_size), fixed)
        in_specs = [
            chunk_spec,
            block_spec,
            block_spec,
            pl.BlockSpec((4, block_size), lambda b, index=index: (0, index)),
            limit_spec,
            pade_spec,
            inverse_spec,
        ]
        operands = [arrivals[index], misfit, checkpoint, trig, limit, pade_factors, inverse_t]
        aliases = {}
        kernel = make_backward_kernel(index)
        if adjoint_begin is not None:
            in_specs.append(pl.BlockSpec(memory_space=pl.ANY))
            operands.append(adjoint_begin)
            aliases = {len(operands) - 1: 0}
            kernel = lambda *refs, kernel=kernel: kernel(*refs[:7], *refs[8:])
        adjoint_begin, grad_part = pl.pallas_call(
            kernel,
            grid=(1,),
            in_specs=in_specs,
            out_specs=[
                block_spec,
                pl.BlockSpec((1, block_size), lambda b: (0, 0)),
            ],
            out_shape=[
                jax.ShapeDtypeStruct(checkpoint.shape, jnp.bfloat16),
                jax.ShapeDtypeStruct((1, block_size), jnp.float32),
            ],
            input_output_aliases=aliases,
        )(*operands)
        grads.append(grad_part)
    any_spec = pl.BlockSpec(memory_space=pl.ANY)
    fixed_last = lambda b: (0, 0, 0, last)
    half_spec = pl.BlockSpec((None, 2, half, block_size), lambda b: (0, 0, 0, 0))
    trig_last = pl.BlockSpec((4, block_size), lambda b: (0, last))
    grad_spec = pl.BlockSpec((1, block_size), lambda b: (0, 0))
    begin_shape = jax.ShapeDtypeStruct(checkpoint.shape, jnp.bfloat16)
    grad_shape = jax.ShapeDtypeStruct((1, block_size), jnp.float32)
    edge = 2 * HALO
    adjoint_begin, grad_first, halo = pl.pallas_call(
        make_first_half_kernel(last),
        grid=(1,),
        in_specs=[
            half_spec,
            pl.BlockSpec((None, 2, half, block_size), fixed_last),
            pl.BlockSpec((None, 2, half, block_size), fixed_last),
            trig_last,
            limit_spec,
            pade_spec,
            inverse_spec,
            any_spec,
        ],
        out_specs=[any_spec, grad_spec, pl.BlockSpec((4, edge, block_size), lambda b: (0, 0, 0))],
        out_shape=[
            begin_shape, grad_shape, jax.ShapeDtypeStruct((4, edge, block_size), jnp.float32)
        ],
        scratch_shapes=[
            pltpu.VMEM((2, half - 2 * HALO, block_size), jnp.bfloat16),
            pltpu.SemaphoreType.DMA((1,)),
        ],
        input_output_aliases={7: 0},
    )(halves[0], misfit, checkpoint, trig, limit, pade_factors, inverse_t, adjoint_begin)
    tail = rows - half
    adjoint_begin, grad_second = pl.pallas_call(
        make_second_half_kernel(last),
        grid=(1,),
        in_specs=[
            pl.BlockSpec((4, edge, block_size), lambda b: (0, 0, 0)),
            pl.BlockSpec((None, 2, tail, block_size), lambda b: (0, 0, 0, 0)),
            pl.BlockSpec((None, 2, tail, block_size), lambda b: (0, 0, 1, last)),
            any_spec,
            trig_last,
            any_spec,
            any_spec,
            inverse_spec,
            any_spec,
        ],
        out_specs=[any_spec, grad_spec],
        out_shape=[begin_shape, grad_shape],
        scratch_shapes=[
            pltpu.VMEM(pade_factors.shape, jnp.bfloat16),
            pltpu.VMEM((2, tail + HALO, block_size), jnp.bfloat16),
            pltpu.VMEM((2, HALO, block_size), jnp.bfloat16),
            pltpu.VMEM((tail + HALO, 1), jnp.int32),
            pltpu.VMEM((HALO, 1), jnp.int32),
            pltpu.VMEM((2, tail + HALO, block_size), jnp.bfloat16),
            pltpu.VMEM((2, HALO, block_size), jnp.bfloat16),
            pltpu.SemaphoreType.DMA((7,)),
        ],
        input_output_aliases={8: 0},
    )(
        halo, halves[1], misfit, checkpoint, trig, limit, pade_factors, inverse_t,
        adjoint_begin,
    )
    grads.append(grad_first + grad_second)
    grad_sum = jnp.concatenate(grads, axis=1)
    grad_here = grad_sum * (-8.0 / (profile * profile * profile)) / rows
    grad_increment = range_scan(grad_here, -1)
    return (field_end, adjoint_begin, grad_increment)


def local(
    checkpoint, adjoint_start, misfit, pade_factors, azimuth_inverse, bottom, base_speed, speed_step
):
    if (
        checkpoint.shape[3] % pade_factors.shape[3] == 0
        and checkpoint.shape[3] >= 2 * pade_factors.shape[3]
        and checkpoint.shape[2] % (2 * azimuth_inverse.shape[2]) == 0
    ):
        return fused_local(
            checkpoint, adjoint_start, misfit, pade_factors, azimuth_inverse, bottom,
            base_speed, speed_step,
        )
    return general_local(
        checkpoint, adjoint_start, misfit, pade_factors, azimuth_inverse, bottom,
        base_speed, speed_step,
    )


def solution(mesh):
    in_specs = (
        P("range", "freq", None, "line"),
        P("range", "freq", None, "line"),
        P("range", "freq", None, "line"),
        P(None, "freq", None, None),
        P("range", "freq", None, None),
        P("range", None),
        P("line"),
        P("range", "line"),
    )
    out_specs = (
        P("range", "freq", None, "line"),
        P("range", "freq", None, "line"),
        P(("freq", "range"), "line"),
    )
    return jax.shard_map(local, mesh=mesh, in_specs=in_specs, out_specs=out_specs, check_vma=False)
```

```python
import jax
import jax.numpy as jnp
from jax import lax
from jax.sharding import PartitionSpec as P
from jax.experimental import pallas as pl
from jax.experimental.pallas import tpu as pltpu

phase_scale = 4.0
bed_phase = -1.8
coupling = 0.3


def passed_along(value, axis, by):
    count = lax.axis_size(axis)
    pairs = [(i, i + by) for i in range(count) if 0 <= i + by < count]
    return lax.ppermute(value, axis, pairs)


def pair_terms(diag_one, diag_two, cross_one, cross_two, adjoint):
    if adjoint:
        return (diag_one + diag_two, cross_one - cross_two)
    return (diag_one - diag_two, cross_one + cross_two)


def depth_apply(current, pade_ops, adjoint):
    factor_count = pade_ops.shape[0]
    sequence = range(factor_count - 1, -1, -1) if adjoint else range(factor_count)
    for factor in sequence:
        contract = 1 if adjoint else 2
        product = lax.dot_general(
            current,
            pade_ops[factor],
            (((3,), (contract,)), ((), ())),
            preferred_element_type=jnp.float32,
        )
        real_part, imag_part = pair_terms(
            product[0, :, :, 0],
            product[1, :, :, 1],
            product[1, :, :, 0],
            product[0, :, :, 1],
            adjoint,
        )
        current = jnp.stack([real_part, imag_part]).astype(jnp.bfloat16)
    return current


def azimuth_apply(field_in, inverse, adjoint):
    block_width = inverse.shape[1]
    blocked = field_in.reshape(2, field_in.shape[1] // block_width, block_width, field_in.shape[2])
    contract = 1 if adjoint else 2
    product = lax.dot_general(
        inverse, blocked, (((contract,), (2,)), ((), ())), preferred_element_type=jnp.float32
    )
    real_part, imag_part = pair_terms(
        product[0, :, 0], product[1, :, 1], product[0, :, 1], product[1, :, 0], adjoint
    )
    joined = jnp.stack([real_part, imag_part])
    return joined.transpose(0, 2, 1, 3).reshape(field_in.shape)


def numerator_map(field_in):
    return field_in + coupling * (
        jnp.roll(field_in, 1, axis=1) + jnp.roll(field_in, -1, axis=1) - 2.0 * field_in
    )


def screen_phase(profile, bottom_row, depth_start):
    depths = depth_start + jnp.arange(profile.shape[0], dtype=jnp.int32)
    in_water = depths[None, :] < bottom_row[:, None]
    water_phase = phase_scale * (1.0 / (profile * profile) - 1.0)
    return (jnp.where(in_water, water_phase[None, :], bed_phase), in_water)


def depth_segment(field_in, pade_factors, adjoint):
    block_size = pade_factors.shape[3]
    if field_in.shape[2] % block_size == 0:
        worked = depth_apply(
            field_in.reshape(2, field_in.shape[1], field_in.shape[2] // block_size, block_size),
            pade_factors,
            adjoint,
        )
        return worked.reshape(field_in.shape)
    turned = lax.all_to_all(field_in, "line", split_axis=1, concat_axis=2, tiled=True)
    full_depth = turned.shape[2]
    worked = depth_apply(
        turned.reshape(2, turned.shape[1], full_depth // block_size, block_size),
        pade_factors,
        adjoint,
    )
    return lax.all_to_all(
        worked.reshape(turned.shape), "line", split_axis=2, concat_axis=1, tiled=True
    )


def general_local(
    checkpoint, adjoint_start, misfit, pade_factors, azimuth_inverse, bottom, base_speed, speed_step
):
    depth_rows = checkpoint.shape[3]
    depth_start = lax.axis_index("line") * depth_rows
    every_step = lax.all_gather(speed_step, "range", axis=0, tiled=True)
    running = jnp.cumsum(every_step, axis=0)
    profile = base_speed + lax.dynamic_index_in_dim(
        running, lax.axis_index("range"), 0, keepdims=False
    )
    phase_angle, in_water = screen_phase(profile, bottom[0], depth_start)
    cosine = jnp.cos(phase_angle)
    sine_term = jnp.sin(phase_angle)
    source = checkpoint[0].astype(jnp.float32)
    screened = jnp.stack(
        [cosine * source[0] - sine_term * source[1], sine_term * source[0] + cosine * source[1]]
    ).astype(jnp.bfloat16)
    depth_out = depth_segment(screened, pade_factors, False)
    numerator = numerator_map(depth_out.astype(jnp.float32)).astype(jnp.bfloat16)
    inverse = azimuth_inverse[0]
    field_end = azimuth_apply(numerator, inverse, False).astype(jnp.bfloat16)
    arrival = passed_along(adjoint_start, "range", -1)
    lam_end = (arrival[0].astype(jnp.float32) + misfit[0].astype(jnp.float32)).astype(jnp.bfloat16)
    backward = numerator_map(azimuth_apply(lam_end, inverse, True)).astype(jnp.bfloat16)
    backward = depth_segment(backward, pade_factors, True)
    cotangent = backward.astype(jnp.float32)
    adjoint_begin = jnp.stack(
        [
            cosine * cotangent[0] + sine_term * cotangent[1],
            cosine * cotangent[1] - sine_term * cotangent[0],
        ]
    ).astype(jnp.bfloat16)
    screened_f = screened.astype(jnp.float32)
    weight = jnp.where(in_water, cotangent[1] * screened_f[0] - cotangent[0] * screened_f[1], 0.0)
    grad_here = (
        jnp.sum(weight, axis=0) * (-8.0 / (profile * profile * profile)) / checkpoint.shape[2]
    )[None, :]
    all_grads = lax.all_gather(grad_here, "range", axis=0, tiled=True)
    suffix = jnp.flip(jnp.cumsum(jnp.flip(all_grads, 0), axis=0), 0)
    grad_increment = lax.dynamic_slice_in_dim(suffix, lax.axis_index("range"), 1, 0)
    return (field_end[None], adjoint_begin[None], grad_increment)


def dot_nt(left, right):
    return lax.dot_general(
        left, right, (((1,), (1,)), ((), ())), preferred_element_type=jnp.float32
    )


def dot_nn(left, right):
    return jnp.dot(left, right, preferred_element_type=jnp.float32)


def numerator_rows(field_in):
    rows = field_in.shape[0]
    return field_in + coupling * (
        pltpu.roll(field_in, 1, 0) + pltpu.roll(field_in, rows - 1, 0) - 2.0 * field_in
    )


def phase_tile(trig_ref, limit_ref, block_index, shape):
    columns = lax.broadcasted_iota(jnp.int32, shape, 1) + block_index * shape[1]
    in_water = columns < limit_ref[...]
    trig = trig_ref[...]
    cosine = jnp.where(in_water, trig[0:1], trig[2:3])
    sine_term = jnp.where(in_water, trig[1:2], trig[3:4])
    return cosine, sine_term, in_water


def screen_tile(source_ref, cosine, sine_term):
    source_r = source_ref[0].astype(jnp.float32)
    source_i = source_ref[1].astype(jnp.float32)
    screened_r = (cosine * source_r - sine_term * source_i).astype(jnp.bfloat16)
    screened_i = (sine_term * source_r + cosine * source_i).astype(jnp.bfloat16)
    return screened_r, screened_i


def forward_kernel(source_ref, trig_ref, limit_ref, pade_ref, inverse_ref, out_ref):
    block_index = pl.program_id(0)
    rows, width = source_ref.shape[1], source_ref.shape[2]
    cosine, sine_term, _ = phase_tile(trig_ref, limit_ref, block_index, (rows, width))
    cur_r, cur_i = screen_tile(source_ref, cosine, sine_term)
    for factor in range(pade_ref.shape[0]):
        pade_r = pade_ref[factor, 0]
        pade_i = pade_ref[factor, 1]
        real_part = dot_nt(cur_r, pade_r) - dot_nt(cur_i, pade_i)
        imag_part = dot_nt(cur_i, pade_r) + dot_nt(cur_r, pade_i)
        cur_r = real_part.astype(jnp.bfloat16)
        cur_i = imag_part.astype(jnp.bfloat16)
    num_r = numerator_rows(cur_r.astype(jnp.float32)).astype(jnp.bfloat16)
    num_i = numerator_rows(cur_i.astype(jnp.float32)).astype(jnp.bfloat16)
    inv_r = inverse_ref[0]
    inv_i = inverse_ref[1]
    block_width = inv_r.shape[0]
    for start in range(0, rows, block_width):
        part_r = num_r[start : start + block_width]
        part_i = num_i[start : start + block_width]
        out_ref[0, start : start + block_width, :] = (
            dot_nn(inv_r, part_r) - dot_nn(inv_i, part_i)
        ).astype(jnp.bfloat16)
        out_ref[1, start : start + block_width, :] = (
            dot_nn(inv_r, part_i) + dot_nn(inv_i, part_r)
        ).astype(jnp.bfloat16)


def make_backward_kernel(block_index):
    def backward_kernel(
        arrival_ref, misfit_ref, source_ref, trig_ref, limit_ref, pade_ref, inverse_t_ref,
        out_ref, grad_ref,
    ):
        rows, width = source_ref.shape[1], source_ref.shape[2]
        lam_r = (
            arrival_ref[0].astype(jnp.float32) + misfit_ref[0].astype(jnp.float32)
        ).astype(jnp.bfloat16)
        lam_i = (
            arrival_ref[1].astype(jnp.float32) + misfit_ref[1].astype(jnp.float32)
        ).astype(jnp.bfloat16)
        inv_r = inverse_t_ref[0]
        inv_i = inverse_t_ref[1]
        block_width = inv_r.shape[0]
        pieces_r = []
        pieces_i = []
        for start in range(0, rows, block_width):
            part_r = lam_r[start : start + block_width]
            part_i = lam_i[start : start + block_width]
            pieces_r.append(dot_nn(inv_r, part_r) + dot_nn(inv_i, part_i))
            pieces_i.append(dot_nn(inv_r, part_i) - dot_nn(inv_i, part_r))
        cur_r = numerator_rows(jnp.concatenate(pieces_r, axis=0)).astype(jnp.bfloat16)
        cur_i = numerator_rows(jnp.concatenate(pieces_i, axis=0)).astype(jnp.bfloat16)
        for factor in range(pade_ref.shape[0] - 1, -1, -1):
            pade_r = pade_ref[factor, 0]
            pade_i = pade_ref[factor, 1]
            real_part = dot_nn(cur_r, pade_r) + dot_nn(cur_i, pade_i)
            imag_part = dot_nn(cur_i, pade_r) - dot_nn(cur_r, pade_i)
            cur_r = real_part.astype(jnp.bfloat16)
            cur_i = imag_part.astype(jnp.bfloat16)
        cot_r = cur_r.astype(jnp.float32)
        cot_i = cur_i.astype(jnp.float32)
        cosine, sine_term, in_water = phase_tile(trig_ref, limit_ref, block_index, (rows, width))
        out_ref[0] = (cosine * cot_r + sine_term * cot_i).astype(jnp.bfloat16)
        out_ref[1] = (cosine * cot_i - sine_term * cot_r).astype(jnp.bfloat16)
        screened_r, screened_i = screen_tile(source_ref, cosine, sine_term)
        weight = jnp.where(
            in_water,
            cot_i * screened_r.astype(jnp.float32) - cot_r * screened_i.astype(jnp.float32),
            0.0,
        )
        grad_ref[...] = jnp.sum(weight, axis=0, keepdims=True)

    return backward_kernel


def lam_rows(arrival, misfit_part):
    return (arrival.astype(jnp.float32) + misfit_part.astype(jnp.float32)).astype(jnp.bfloat16)


def azimuth_adjoint(inv_r, inv_i, part_r, part_i):
    return (
        dot_nn(inv_r, part_r) + dot_nn(inv_i, part_i),
        dot_nn(inv_r, part_i) - dot_nn(inv_i, part_r),
    )


def depth_adjoint(cur_r, cur_i, pade_ref):
    for factor in range(pade_ref.shape[0] - 1, -1, -1):
        pade_r = pade_ref[factor, 0]
        pade_i = pade_ref[factor, 1]
        real_part = dot_nn(cur_r, pade_r) + dot_nn(cur_i, pade_i)
        imag_part = dot_nn(cur_i, pade_r) - dot_nn(cur_r, pade_i)
        cur_r = real_part.astype(jnp.bfloat16)
        cur_i = imag_part.astype(jnp.bfloat16)
    return cur_r.astype(jnp.float32), cur_i.astype(jnp.float32)


def finish_rows(cot_r, cot_i, trig_ref, limit_rows, source_r, source_i, block_index):
    shape = cot_r.shape
    columns = lax.broadcasted_iota(jnp.int32, shape, 1) + block_index * shape[1]
    in_water = columns < limit_rows
    trig = trig_ref[...]
    cosine = jnp.where(in_water, trig[0:1], trig[2:3])
    sine_term = jnp.where(in_water, trig[1:2], trig[3:4])
    out_r = cosine * cot_r + sine_term * cot_i
    out_i = cosine * cot_i - sine_term * cot_r
    screened_r = (cosine * source_r - sine_term * source_i).astype(jnp.bfloat16)
    screened_i = (sine_term * source_r + cosine * source_i).astype(jnp.bfloat16)
    weight = jnp.where(
        in_water,
        cot_i * screened_r.astype(jnp.float32) - cot_r * screened_i.astype(jnp.float32),
        0.0,
    )
    return out_r, out_i, jnp.sum(weight, axis=0, keepdims=True)


HALO = 8


def make_first_half_kernel(block_index):
    def kernel(
        arrival_ref, misfit_ref, source_ref, trig_ref, limit_ref, pade_ref, inverse_t_ref,
        begin_in, begin_out, grad_ref, halo_ref, stage_ref, copy_sem,
    ):
        half, width = arrival_ref.shape[1], arrival_ref.shape[2]
        lam_r = lam_rows(arrival_ref[0], misfit_ref[0])
        lam_i = lam_rows(arrival_ref[1], misfit_ref[1])
        inv_r = inverse_t_ref[0]
        inv_i = inverse_t_ref[1]
        block_width = inv_r.shape[0]
        pieces_r = []
        pieces_i = []
        for start in range(0, half, block_width):
            piece_r, piece_i = azimuth_adjoint(
                inv_r, inv_i, lam_r[start : start + block_width], lam_i[start : start + block_width]
            )
            pieces_r.append(piece_r)
            pieces_i.append(piece_i)
        whole_r = jnp.concatenate(pieces_r, axis=0)
        whole_i = jnp.concatenate(pieces_i, axis=0)
        edge = 2 * HALO
        halo_ref[0] = whole_r[half - edge :]
        halo_ref[1] = whole_i[half - edge :]
        halo_ref[2] = whole_r[:edge]
        halo_ref[3] = whole_i[:edge]
        num_r = numerator_rows(whole_r)[HALO : half - HALO]
        num_i = numerator_rows(whole_i)[HALO : half - HALO]
        cot_r, cot_i = depth_adjoint(
            num_r.astype(jnp.bfloat16), num_i.astype(jnp.bfloat16), pade_ref
        )
        source_r = source_ref[0].astype(jnp.float32)[HALO : half - HALO]
        source_i = source_ref[1].astype(jnp.float32)[HALO : half - HALO]
        out_r, out_i, grad_row = finish_rows(
            cot_r, cot_i, trig_ref, limit_ref[HALO : half - HALO], source_r, source_i, block_index
        )
        stage_ref[0] = out_r.astype(jnp.bfloat16)
        stage_ref[1] = out_i.astype(jnp.bfloat16)
        copy = pltpu.make_async_copy(
            stage_ref,
            begin_out.at[0, :, pl.ds(HALO, half - 2 * HALO), pl.ds(block_index * width, width)],
            copy_sem.at[0],
        )
        copy.start()
        grad_ref[...] = grad_row
        copy.wait()

    return kernel


def make_second_half_kernel(block_index):
    def kernel(
        halo_ref, arrival_ref, misfit_ref, source_hbm, trig_ref, limit_hbm, pade_hbm,
        inverse_t_ref, begin_in, begin_out, grad_ref, pade_ref, source_main, source_wrap,
        limit_main, limit_wrap, main_ref, wrap_ref, copy_sem,
    ):
        tail, width = arrival_ref.shape[1], arrival_ref.shape[2]
        half = source_hbm.shape[2] - tail
        columns = pl.ds(block_index * width, width)
        factor_count = pade_ref.shape[0]
        pade_loads = [
            pltpu.make_async_copy(pade_hbm.at[factor], pade_ref.at[factor], copy_sem.at[7 + factor])
            for factor in range(factor_count - 1, -1, -1)
        ]
        for load in pade_loads:
            load.start()
        loads = [
            pltpu.make_async_copy(
                source_hbm.at[0, :, pl.ds(half - HALO, tail + HALO), columns],
                source_main,
                copy_sem.at[1],
            ),
            pltpu.make_async_copy(
                source_hbm.at[0, :, pl.ds(0, HALO), columns], source_wrap, copy_sem.at[2]
            ),
            pltpu.make_async_copy(
                limit_hbm.at[pl.ds(half - HALO, tail + HALO)], limit_main, copy_sem.at[3]
            ),
            pltpu.make_async_copy(limit_hbm.at[pl.ds(0, HALO)], limit_wrap, copy_sem.at[4]),
        ]
        for load in loads:
            load.start()
        inv_r = inverse_t_ref[0]
        inv_i = inverse_t_ref[1]
        block_width = inv_r.shape[0]
        lam_r = lam_rows(arrival_ref[0], misfit_ref[0])
        lam_i = lam_rows(arrival_ref[1], misfit_ref[1])
        pieces_r = [halo_ref[0]]
        pieces_i = [halo_ref[1]]
        for start in range(0, tail, block_width):
            piece_r, piece_i = azimuth_adjoint(
                inv_r, inv_i, lam_r[start : start + block_width], lam_i[start : start + block_width]
            )
            pieces_r.append(piece_r)
            pieces_i.append(piece_i)
        pieces_r.append(halo_ref[2])
        pieces_i.append(halo_ref[3])
        span = tail + 2 * HALO
        num_r = numerator_rows(jnp.concatenate(pieces_r, axis=0))[HALO : HALO + span]
        num_i = numerator_rows(jnp.concatenate(pieces_i, axis=0))[HALO : HALO + span]
        cur_r = num_r.astype(jnp.bfloat16)
        cur_i = num_i.astype(jnp.bfloat16)
        for load, factor in zip(pade_loads, range(factor_count - 1, -1, -1)):
            load.wait()
            pade_r = pade_ref[factor, 0]
            pade_i = pade_ref[factor, 1]
            real_part = dot_nn(cur_r, pade_r) + dot_nn(cur_i, pade_i)
            imag_part = dot_nn(cur_i, pade_r) - dot_nn(cur_r, pade_i)
            cur_r = real_part.astype(jnp.bfloat16)
            cur_i = imag_part.astype(jnp.bfloat16)
        cot_r = cur_r.astype(jnp.float32)
        cot_i = cur_i.astype(jnp.float32)
        for load in loads:
            load.wait()
        source_r = jnp.concatenate(
            [source_main[0].astype(jnp.float32), source_wrap[0].astype(jnp.float32)], axis=0
        )
        source_i = jnp.concatenate(
            [source_main[1].astype(jnp.float32), source_wrap[1].astype(jnp.float32)], axis=0
        )
        limit_rows = jnp.concatenate([limit_main[...], limit_wrap[...]], axis=0)
        out_r, out_i, grad_row = finish_rows(
            cot_r, cot_i, trig_ref, limit_rows, source_r, source_i, block_index
        )
        main_ref[0] = out_r[: tail + HALO].astype(jnp.bfloat16)
        main_ref[1] = out_i[: tail + HALO].astype(jnp.bfloat16)
        wrap_ref[0] = out_r[tail + HALO :].astype(jnp.bfloat16)
        wrap_ref[1] = out_i[tail + HALO :].astype(jnp.bfloat16)
        main_copy = pltpu.make_async_copy(
            main_ref, begin_out.at[0, :, pl.ds(half - HALO, tail + HALO), columns], copy_sem.at[5]
        )
        wrap_copy = pltpu.make_async_copy(
            wrap_ref, begin_out.at[0, :, pl.ds(0, HALO), columns], copy_sem.at[6]
        )
        main_copy.start()
        wrap_copy.start()
        grad_ref[...] = grad_row
        main_copy.wait()
        wrap_copy.wait()

    return kernel


def range_scan(value, direction):
    count = lax.axis_size("range")
    total = value
    for reach in range(1, count):
        total = total + passed_along(value, "range", direction * reach)
    return total


def fused_local(
    checkpoint, adjoint_start, misfit, pade_factors, azimuth_inverse, bottom, base_speed, speed_step
):
    depth_rows = checkpoint.shape[3]
    rows = checkpoint.shape[2]
    block_size = pade_factors.shape[3]
    block_count = depth_rows // block_size
    depth_start = lax.axis_index("line") * depth_rows
    half = rows // 2
    last = block_count - 1
    arrivals = [
        passed_along(
            adjoint_start[:, :, :, index * block_size : (index + 1) * block_size], "range", -1
        )
        for index in range(last)
    ]
    last_columns = adjoint_start[:, :, :, last * block_size :]
    first_half = passed_along(last_columns[:, :, :half], "range", -1)
    second_half = passed_along(last_columns[:, :, half:], "range", -1)
    halves = [first_half, second_half]
    profile = base_speed + range_scan(speed_step, 1)[0]
    water_phase = phase_scale * (1.0 / (profile * profile) - 1.0)
    bed_row = jnp.full_like(water_phase, bed_phase)
    trig = jnp.stack(
        [jnp.cos(water_phase), jnp.sin(water_phase), jnp.cos(bed_row), jnp.sin(bed_row)]
    )
    limit = (bottom[0] - depth_start)[:, None]
    inverse = azimuth_inverse[0]
    inverse_t = jnp.swapaxes(inverse, 1, 2)
    field_spec = pl.BlockSpec((None, 2, rows, block_size), lambda b: (0, 0, 0, b))
    trig_spec = pl.BlockSpec((4, block_size), lambda b: (0, b))
    limit_spec = pl.BlockSpec((rows, 1), lambda b: (0, 0))
    pade_spec = pl.BlockSpec(pade_factors.shape, lambda b: (0, 0, 0, 0))
    inverse_spec = pl.BlockSpec(inverse.shape, lambda b: (0, 0, 0))
    field_end = pl.pallas_call(
        forward_kernel,
        grid=(block_count,),
        in_specs=[field_spec, trig_spec, limit_spec, pade_spec, inverse_spec],
        out_specs=field_spec,
        out_shape=jax.ShapeDtypeStruct(checkpoint.shape, jnp.bfloat16),
    )(checkpoint, trig, limit, pade_factors, inverse)
    field_end, arrivals[0] = lax.optimization_barrier((field_end, arrivals[0]))
    adjoint_begin = None
    grads = []
    for index in range(last):
        fixed = lambda b, index=index: (0, 0, 0, index)
        chunk_spec = pl.BlockSpec((None, 2, rows, block_size), lambda b: (0, 0, 0, 0))
        block_spec = pl.BlockSpec((None, 2, rows, block_size), fixed)
        in_specs = [
            chunk_spec,
            block_spec,
            block_spec,
            pl.BlockSpec((4, block_size), lambda b, index=index: (0, index)),
            limit_spec,
            pade_spec,
            inverse_spec,
        ]
        operands = [arrivals[index], misfit, checkpoint, trig, limit, pade_factors, inverse_t]
        aliases = {}
        kernel = make_backward_kernel(index)
        if adjoint_begin is not None:
            in_specs.append(pl.BlockSpec(memory_space=pl.ANY))
            operands.append(adjoint_begin)
            aliases = {len(operands) - 1: 0}
            kernel = lambda *refs, kernel=kernel: kernel(*refs[:7], *refs[8:])
        adjoint_begin, grad_part = pl.pallas_call(
            kernel,
            grid=(1,),
            in_specs=in_specs,
            out_specs=[
                block_spec,
                pl.BlockSpec((1, block_size), lambda b: (0, 0)),
            ],
            out_shape=[
                jax.ShapeDtypeStruct(checkpoint.shape, jnp.bfloat16),
                jax.ShapeDtypeStruct((1, block_size), jnp.float32),
            ],
            input_output_aliases=aliases,
        )(*operands)
        grads.append(grad_part)
    any_spec = pl.BlockSpec(memory_space=pl.ANY)
    fixed_last = lambda b: (0, 0, 0, last)
    half_spec = pl.BlockSpec((None, 2, half, block_size), lambda b: (0, 0, 0, 0))
    trig_last = pl.BlockSpec((4, block_size), lambda b: (0, last))
    grad_spec = pl.BlockSpec((1, block_size), lambda b: (0, 0))
    begin_shape = jax.ShapeDtypeStruct(checkpoint.shape, jnp.bfloat16)
    grad_shape = jax.ShapeDtypeStruct((1, block_size), jnp.float32)
    edge = 2 * HALO
    adjoint_begin, grad_first, halo = pl.pallas_call(
        make_first_half_kernel(last),
        grid=(1,),
        in_specs=[
            half_spec,
            pl.BlockSpec((None, 2, half, block_size), fixed_last),
            pl.BlockSpec((None, 2, half, block_size), fixed_last),
            trig_last,
            limit_spec,
            pade_spec,
            inverse_spec,
            any_spec,
        ],
        out_specs=[any_spec, grad_spec, pl.BlockSpec((4, edge, block_size), lambda b: (0, 0, 0))],
        out_shape=[
            begin_shape, grad_shape, jax.ShapeDtypeStruct((4, edge, block_size), jnp.float32)
        ],
        scratch_shapes=[
            pltpu.VMEM((2, half - 2 * HALO, block_size), jnp.bfloat16),
            pltpu.SemaphoreType.DMA((1,)),
        ],
        input_output_aliases={7: 0},
    )(halves[0], misfit, checkpoint, trig, limit, pade_factors, inverse_t, adjoint_begin)
    tail = rows - half
    adjoint_begin, grad_second = pl.pallas_call(
        make_second_half_kernel(last),
        grid=(1,),
        in_specs=[
            pl.BlockSpec((4, edge, block_size), lambda b: (0, 0, 0)),
            pl.BlockSpec((None, 2, tail, block_size), lambda b: (0, 0, 0, 0)),
            pl.BlockSpec((None, 2, tail, block_size), lambda b: (0, 0, 1, last)),
            any_spec,
            trig_last,
            any_spec,
            any_spec,
            inverse_spec,
            any_spec,
        ],
        out_specs=[any_spec, grad_spec],
        out_shape=[begin_shape, grad_shape],
        scratch_shapes=[
            pltpu.VMEM(pade_factors.shape, jnp.bfloat16),
            pltpu.VMEM((2, tail + HALO, block_size), jnp.bfloat16),
            pltpu.VMEM((2, HALO, block_size), jnp.bfloat16),
            pltpu.VMEM((tail + HALO, 1), jnp.int32),
            pltpu.VMEM((HALO, 1), jnp.int32),
            pltpu.VMEM((2, tail + HALO, block_size), jnp.bfloat16),
            pltpu.VMEM((2, HALO, block_size), jnp.bfloat16),
            pltpu.SemaphoreType.DMA((7 + pade_factors.shape[0],)),
        ],
        input_output_aliases={8: 0},
    )(
        halo, halves[1], misfit, checkpoint, trig, limit, pade_factors, inverse_t,
        adjoint_begin,
    )
    grads.append(grad_first + grad_second)
    grad_sum = jnp.concatenate(grads, axis=1)
    grad_here = grad_sum * (-8.0 / (profile * profile * profile)) / rows
    grad_increment = range_scan(grad_here, -1)
    return (field_end, adjoint_begin, grad_increment)


def local(
    checkpoint, adjoint_start, misfit, pade_factors, azimuth_inverse, bottom, base_speed, speed_step
):
    if (
        checkpoint.shape[3] % pade_factors.shape[3] == 0
        and checkpoint.shape[3] >= 2 * pade_factors.shape[3]
        and checkpoint.shape[2] % (2 * azimuth_inverse.shape[2]) == 0
    ):
        return fused_local(
            checkpoint, adjoint_start, misfit, pade_factors, azimuth_inverse, bottom,
            base_speed, speed_step,
        )
    return general_local(
        checkpoint, adjoint_start, misfit, pade_factors, azimuth_inverse, bottom,
        base_speed, speed_step,
    )


def solution(mesh):
    in_specs = (
        P("range", "freq", None, "line"),
        P("range", "freq", None, "line"),
        P("range", "freq", None, "line"),
        P(None, "freq", None, None),
        P("range", "freq", None, None),
        P("range", None),
        P("line"),
        P("range", "line"),
    )
    out_specs = (
        P("range", "freq", None, "line"),
        P("range", "freq", None, "line"),
        P(("freq", "range"), "line"),
    )
    return jax.shard_map(local, mesh=mesh, in_specs=in_specs, out_specs=out_specs, check_vma=False)
```

```python
import jax
import jax.numpy as jnp
from jax import lax
from jax.sharding import PartitionSpec as P
from jax.experimental import pallas as pl
from jax.experimental.pallas import tpu as pltpu

phase_scale = 4.0
bed_phase = -1.8
coupling = 0.3


def passed_along(value, axis, by):
    count = lax.axis_size(axis)
    pairs = [(i, i + by) for i in range(count) if 0 <= i + by < count]
    return lax.ppermute(value, axis, pairs)


def pair_terms(diag_one, diag_two, cross_one, cross_two, adjoint):
    if adjoint:
        return (diag_one + diag_two, cross_one - cross_two)
    return (diag_one - diag_two, cross_one + cross_two)


def depth_apply(current, pade_ops, adjoint):
    factor_count = pade_ops.shape[0]
    sequence = range(factor_count - 1, -1, -1) if adjoint else range(factor_count)
    for factor in sequence:
        contract = 1 if adjoint else 2
        product = lax.dot_general(
            current,
            pade_ops[factor],
            (((3,), (contract,)), ((), ())),
            preferred_element_type=jnp.float32,
        )
        real_part, imag_part = pair_terms(
            product[0, :, :, 0],
            product[1, :, :, 1],
            product[1, :, :, 0],
            product[0, :, :, 1],
            adjoint,
        )
        current = jnp.stack([real_part, imag_part]).astype(jnp.bfloat16)
    return current


def azimuth_apply(field_in, inverse, adjoint):
    block_width = inverse.shape[1]
    blocked = field_in.reshape(2, field_in.shape[1] // block_width, block_width, field_in.shape[2])
    contract = 1 if adjoint else 2
    product = lax.dot_general(
        inverse, blocked, (((contract,), (2,)), ((), ())), preferred_element_type=jnp.float32
    )
    real_part, imag_part = pair_terms(
        product[0, :, 0], product[1, :, 1], product[0, :, 1], product[1, :, 0], adjoint
    )
    joined = jnp.stack([real_part, imag_part])
    return joined.transpose(0, 2, 1, 3).reshape(field_in.shape)


def numerator_map(field_in):
    return field_in + coupling * (
        jnp.roll(field_in, 1, axis=1) + jnp.roll(field_in, -1, axis=1) - 2.0 * field_in
    )


def screen_phase(profile, bottom_row, depth_start):
    depths = depth_start + jnp.arange(profile.shape[0], dtype=jnp.int32)
    in_water = depths[None, :] < bottom_row[:, None]
    water_phase = phase_scale * (1.0 / (profile * profile) - 1.0)
    return (jnp.where(in_water, water_phase[None, :], bed_phase), in_water)


def depth_segment(field_in, pade_factors, adjoint):
    block_size = pade_factors.shape[3]
    if field_in.shape[2] % block_size == 0:
        worked = depth_apply(
            field_in.reshape(2, field_in.shape[1], field_in.shape[2] // block_size, block_size),
            pade_factors,
            adjoint,
        )
        return worked.reshape(field_in.shape)
    turned = lax.all_to_all(field_in, "line", split_axis=1, concat_axis=2, tiled=True)
    full_depth = turned.shape[2]
    worked = depth_apply(
        turned.reshape(2, turned.shape[1], full_depth // block_size, block_size),
        pade_factors,
        adjoint,
    )
    return lax.all_to_all(
        worked.reshape(turned.shape), "line", split_axis=2, concat_axis=1, tiled=True
    )


def general_local(
    checkpoint, adjoint_start, misfit, pade_factors, azimuth_inverse, bottom, base_speed, speed_step
):
    depth_rows = checkpoint.shape[3]
    depth_start = lax.axis_index("line") * depth_rows
    every_step = lax.all_gather(speed_step, "range", axis=0, tiled=True)
    running = jnp.cumsum(every_step, axis=0)
    profile = base_speed + lax.dynamic_index_in_dim(
        running, lax.axis_index("range"), 0, keepdims=False
    )
    phase_angle, in_water = screen_phase(profile, bottom[0], depth_start)
    cosine = jnp.cos(phase_angle)
    sine_term = jnp.sin(phase_angle)
    source = checkpoint[0].astype(jnp.float32)
    screened = jnp.stack(
        [cosine * source[0] - sine_term * source[1], sine_term * source[0] + cosine * source[1]]
    ).astype(jnp.bfloat16)
    depth_out = depth_segment(screened, pade_factors, False)
    numerator = numerator_map(depth_out.astype(jnp.float32)).astype(jnp.bfloat16)
    inverse = azimuth_inverse[0]
    field_end = azimuth_apply(numerator, inverse, False).astype(jnp.bfloat16)
    arrival = passed_along(adjoint_start, "range", -1)
    lam_end = (arrival[0].astype(jnp.float32) + misfit[0].astype(jnp.float32)).astype(jnp.bfloat16)
    backward = numerator_map(azimuth_apply(lam_end, inverse, True)).astype(jnp.bfloat16)
    backward = depth_segment(backward, pade_factors, True)
    cotangent = backward.astype(jnp.float32)
    adjoint_begin = jnp.stack(
        [
            cosine * cotangent[0] + sine_term * cotangent[1],
            cosine * cotangent[1] - sine_term * cotangent[0],
        ]
    ).astype(jnp.bfloat16)
    screened_f = screened.astype(jnp.float32)
    weight = jnp.where(in_water, cotangent[1] * screened_f[0] - cotangent[0] * screened_f[1], 0.0)
    grad_here = (
        jnp.sum(weight, axis=0) * (-8.0 / (profile * profile * profile)) / checkpoint.shape[2]
    )[None, :]
    all_grads = lax.all_gather(grad_here, "range", axis=0, tiled=True)
    suffix = jnp.flip(jnp.cumsum(jnp.flip(all_grads, 0), axis=0), 0)
    grad_increment = lax.dynamic_slice_in_dim(suffix, lax.axis_index("range"), 1, 0)
    return (field_end[None], adjoint_begin[None], grad_increment)


def dot_nt(left, right):
    return lax.dot_general(
        left, right, (((1,), (1,)), ((), ())), preferred_element_type=jnp.float32
    )


def dot_nn(left, right):
    return jnp.dot(left, right, preferred_element_type=jnp.float32)


def numerator_rows(field_in):
    rows = field_in.shape[0]
    return field_in + coupling * (
        pltpu.roll(field_in, 1, 0) + pltpu.roll(field_in, rows - 1, 0) - 2.0 * field_in
    )


def phase_tile(trig_ref, limit_ref, block_index, shape):
    columns = lax.broadcasted_iota(jnp.int32, shape, 1) + block_index * shape[1]
    in_water = columns < limit_ref[...]
    trig = trig_ref[...]
    cosine = jnp.where(in_water, trig[0:1], trig[2:3])
    sine_term = jnp.where(in_water, trig[1:2], trig[3:4])
    return cosine, sine_term, in_water


def screen_tile(source_ref, cosine, sine_term):
    source_r = source_ref[0].astype(jnp.float32)
    source_i = source_ref[1].astype(jnp.float32)
    screened_r = (cosine * source_r - sine_term * source_i).astype(jnp.bfloat16)
    screened_i = (sine_term * source_r + cosine * source_i).astype(jnp.bfloat16)
    return screened_r, screened_i


def forward_kernel(source_ref, trig_ref, limit_ref, pade_ref, inverse_ref, out_ref):
    block_index = pl.program_id(0)
    rows, width = source_ref.shape[1], source_ref.shape[2]
    cosine, sine_term, _ = phase_tile(trig_ref, limit_ref, block_index, (rows, width))
    cur_r, cur_i = screen_tile(source_ref, cosine, sine_term)
    for factor in range(pade_ref.shape[0]):
        pade_r = pade_ref[factor, 0]
        pade_i = pade_ref[factor, 1]
        real_part = dot_nt(cur_r, pade_r) - dot_nt(cur_i, pade_i)
        imag_part = dot_nt(cur_i, pade_r) + dot_nt(cur_r, pade_i)
        cur_r = real_part.astype(jnp.bfloat16)
        cur_i = imag_part.astype(jnp.bfloat16)
    num_r = numerator_rows(cur_r.astype(jnp.float32)).astype(jnp.bfloat16)
    num_i = numerator_rows(cur_i.astype(jnp.float32)).astype(jnp.bfloat16)
    inv_r = inverse_ref[0]
    inv_i = inverse_ref[1]
    block_width = inv_r.shape[0]
    for start in range(0, rows, block_width):
        part_r = num_r[start : start + block_width]
        part_i = num_i[start : start + block_width]
        out_ref[0, start : start + block_width, :] = (
            dot_nn(inv_r, part_r) - dot_nn(inv_i, part_i)
        ).astype(jnp.bfloat16)
        out_ref[1, start : start + block_width, :] = (
            dot_nn(inv_r, part_i) + dot_nn(inv_i, part_r)
        ).astype(jnp.bfloat16)


def make_backward_kernel(block_index):
    def backward_kernel(
        lead_ref, rest_ref, misfit_ref, source_ref, trig_ref, limit_ref, pade_ref, inverse_t_ref,
        out_ref, grad_ref,
    ):
        rows, width = source_ref.shape[1], source_ref.shape[2]
        arrival_r = jnp.concatenate([lead_ref[0], rest_ref[0]], axis=0)
        arrival_i = jnp.concatenate([lead_ref[1], rest_ref[1]], axis=0)
        lam_r = (
            arrival_r.astype(jnp.float32) + misfit_ref[0].astype(jnp.float32)
        ).astype(jnp.bfloat16)
        lam_i = (
            arrival_i.astype(jnp.float32) + misfit_ref[1].astype(jnp.float32)
        ).astype(jnp.bfloat16)
        inv_r = inverse_t_ref[0].T
        inv_i = inverse_t_ref[1].T
        block_width = inv_r.shape[0]
        pieces_r = []
        pieces_i = []
        for start in range(0, rows, block_width):
            part_r = lam_r[start : start + block_width]
            part_i = lam_i[start : start + block_width]
            pieces_r.append(dot_nn(inv_r, part_r) + dot_nn(inv_i, part_i))
            pieces_i.append(dot_nn(inv_r, part_i) - dot_nn(inv_i, part_r))
        cur_r = numerator_rows(jnp.concatenate(pieces_r, axis=0)).astype(jnp.bfloat16)
        cur_i = numerator_rows(jnp.concatenate(pieces_i, axis=0)).astype(jnp.bfloat16)
        for factor in range(pade_ref.shape[0] - 1, -1, -1):
            pade_r = pade_ref[factor, 0]
            pade_i = pade_ref[factor, 1]
            real_part = dot_nn(cur_r, pade_r) + dot_nn(cur_i, pade_i)
            imag_part = dot_nn(cur_i, pade_r) - dot_nn(cur_r, pade_i)
            cur_r = real_part.astype(jnp.bfloat16)
            cur_i = imag_part.astype(jnp.bfloat16)
        cot_r = cur_r.astype(jnp.float32)
        cot_i = cur_i.astype(jnp.float32)
        cosine, sine_term, in_water = phase_tile(trig_ref, limit_ref, block_index, (rows, width))
        out_ref[0] = (cosine * cot_r + sine_term * cot_i).astype(jnp.bfloat16)
        out_ref[1] = (cosine * cot_i - sine_term * cot_r).astype(jnp.bfloat16)
        screened_r, screened_i = screen_tile(source_ref, cosine, sine_term)
        weight = jnp.where(
            in_water,
            cot_i * screened_r.astype(jnp.float32) - cot_r * screened_i.astype(jnp.float32),
            0.0,
        )
        grad_ref[...] = jnp.sum(weight, axis=0, keepdims=True)

    return backward_kernel


def lam_rows(arrival, misfit_part):
    return (arrival.astype(jnp.float32) + misfit_part.astype(jnp.float32)).astype(jnp.bfloat16)


def azimuth_adjoint(inv_r, inv_i, part_r, part_i):
    return (
        dot_nn(inv_r, part_r) + dot_nn(inv_i, part_i),
        dot_nn(inv_r, part_i) - dot_nn(inv_i, part_r),
    )


def depth_adjoint(cur_r, cur_i, pade_ref):
    for factor in range(pade_ref.shape[0] - 1, -1, -1):
        pade_r = pade_ref[factor, 0]
        pade_i = pade_ref[factor, 1]
        real_part = dot_nn(cur_r, pade_r) + dot_nn(cur_i, pade_i)
        imag_part = dot_nn(cur_i, pade_r) - dot_nn(cur_r, pade_i)
        cur_r = real_part.astype(jnp.bfloat16)
        cur_i = imag_part.astype(jnp.bfloat16)
    return cur_r.astype(jnp.float32), cur_i.astype(jnp.float32)


def finish_rows(cot_r, cot_i, trig_ref, limit_rows, source_r, source_i, block_index):
    shape = cot_r.shape
    columns = lax.broadcasted_iota(jnp.int32, shape, 1) + block_index * shape[1]
    in_water = columns < limit_rows
    trig = trig_ref[...]
    cosine = jnp.where(in_water, trig[0:1], trig[2:3])
    sine_term = jnp.where(in_water, trig[1:2], trig[3:4])
    out_r = cosine * cot_r + sine_term * cot_i
    out_i = cosine * cot_i - sine_term * cot_r
    screened_r = (cosine * source_r - sine_term * source_i).astype(jnp.bfloat16)
    screened_i = (sine_term * source_r + cosine * source_i).astype(jnp.bfloat16)
    weight = jnp.where(
        in_water,
        cot_i * screened_r.astype(jnp.float32) - cot_r * screened_i.astype(jnp.float32),
        0.0,
    )
    return out_r, out_i, jnp.sum(weight, axis=0, keepdims=True)


HALO = 8


def make_first_half_kernel(block_index):
    def kernel(
        arrival_ref, misfit_ref, source_ref, trig_ref, limit_ref, pade_ref, inverse_t_ref,
        begin_in, begin_out, grad_ref, halo_ref, stage_ref, copy_sem,
    ):
        half, width = arrival_ref.shape[1], arrival_ref.shape[2]
        lam_r = lam_rows(arrival_ref[0], misfit_ref[0])
        lam_i = lam_rows(arrival_ref[1], misfit_ref[1])
        inv_r = inverse_t_ref[0].T
        inv_i = inverse_t_ref[1].T
        block_width = inv_r.shape[0]
        pieces_r = []
        pieces_i = []
        for start in range(0, half, block_width):
            piece_r, piece_i = azimuth_adjoint(
                inv_r, inv_i, lam_r[start : start + block_width], lam_i[start : start + block_width]
            )
            pieces_r.append(piece_r)
            pieces_i.append(piece_i)
        whole_r = jnp.concatenate(pieces_r, axis=0)
        whole_i = jnp.concatenate(pieces_i, axis=0)
        edge = 2 * HALO
        halo_ref[0] = whole_r[half - edge :]
        halo_ref[1] = whole_i[half - edge :]
        halo_ref[2] = whole_r[:edge]
        halo_ref[3] = whole_i[:edge]
        num_r = numerator_rows(whole_r)[HALO : half - HALO]
        num_i = numerator_rows(whole_i)[HALO : half - HALO]
        cot_r, cot_i = depth_adjoint(
            num_r.astype(jnp.bfloat16), num_i.astype(jnp.bfloat16), pade_ref
        )
        source_r = source_ref[0].astype(jnp.float32)[HALO : half - HALO]
        source_i = source_ref[1].astype(jnp.float32)[HALO : half - HALO]
        out_r, out_i, grad_row = finish_rows(
            cot_r, cot_i, trig_ref, limit_ref[HALO : half - HALO], source_r, source_i, block_index
        )
        stage_ref[0] = out_r.astype(jnp.bfloat16)
        stage_ref[1] = out_i.astype(jnp.bfloat16)
        copy = pltpu.make_async_copy(
            stage_ref,
            begin_out.at[0, :, pl.ds(HALO, half - 2 * HALO), pl.ds(block_index * width, width)],
            copy_sem.at[0],
        )
        copy.start()
        grad_ref[...] = grad_row
        copy.wait()

    return kernel


def make_second_half_kernel(block_index):
    def kernel(
        halo_ref, arrival_ref, misfit_ref, source_hbm, trig_ref, limit_hbm, pade_hbm,
        inverse_t_ref, begin_in, begin_out, grad_ref, pade_ref, source_main, source_wrap,
        limit_main, limit_wrap, main_ref, wrap_ref, copy_sem,
    ):
        tail, width = arrival_ref.shape[1], arrival_ref.shape[2]
        half = source_hbm.shape[2] - tail
        columns = pl.ds(block_index * width, width)
        loads = [
            pltpu.make_async_copy(pade_hbm, pade_ref, copy_sem.at[0]),
            pltpu.make_async_copy(
                source_hbm.at[0, :, pl.ds(half - HALO, tail + HALO), columns],
                source_main,
                copy_sem.at[1],
            ),
            pltpu.make_async_copy(
                source_hbm.at[0, :, pl.ds(0, HALO), columns], source_wrap, copy_sem.at[2]
            ),
            pltpu.make_async_copy(
                limit_hbm.at[pl.ds(half - HALO, tail + HALO)], limit_main, copy_sem.at[3]
            ),
            pltpu.make_async_copy(limit_hbm.at[pl.ds(0, HALO)], limit_wrap, copy_sem.at[4]),
        ]
        for load in loads:
            load.start()
        inv_r = inverse_t_ref[0].T
        inv_i = inverse_t_ref[1].T
        block_width = inv_r.shape[0]
        lam_r = lam_rows(arrival_ref[0], misfit_ref[0])
        lam_i = lam_rows(arrival_ref[1], misfit_ref[1])
        pieces_r = [halo_ref[0]]
        pieces_i = [halo_ref[1]]
        for start in range(0, tail, block_width):
            piece_r, piece_i = azimuth_adjoint(
                inv_r, inv_i, lam_r[start : start + block_width], lam_i[start : start + block_width]
            )
            pieces_r.append(piece_r)
            pieces_i.append(piece_i)
        pieces_r.append(halo_ref[2])
        pieces_i.append(halo_ref[3])
        span = tail + 2 * HALO
        num_r = numerator_rows(jnp.concatenate(pieces_r, axis=0))[HALO : HALO + span]
        num_i = numerator_rows(jnp.concatenate(pieces_i, axis=0))[HALO : HALO + span]
        loads[0].wait()
        cot_r, cot_i = depth_adjoint(
            num_r.astype(jnp.bfloat16), num_i.astype(jnp.bfloat16), pade_ref
        )
        for load in loads[1:]:
            load.wait()
        source_r = jnp.concatenate(
            [source_main[0].astype(jnp.float32), source_wrap[0].astype(jnp.float32)], axis=0
        )
        source_i = jnp.concatenate(
            [source_main[1].astype(jnp.float32), source_wrap[1].astype(jnp.float32)], axis=0
        )
        limit_rows = jnp.concatenate([limit_main[...], limit_wrap[...]], axis=0)
        out_r, out_i, grad_row = finish_rows(
            cot_r, cot_i, trig_ref, limit_rows, source_r, source_i, block_index
        )
        main_ref[0] = out_r[: tail + HALO].astype(jnp.bfloat16)
        main_ref[1] = out_i[: tail + HALO].astype(jnp.bfloat16)
        wrap_ref[0] = out_r[tail + HALO :].astype(jnp.bfloat16)
        wrap_ref[1] = out_i[tail + HALO :].astype(jnp.bfloat16)
        main_copy = pltpu.make_async_copy(
            main_ref, begin_out.at[0, :, pl.ds(half - HALO, tail + HALO), columns], copy_sem.at[5]
        )
        wrap_copy = pltpu.make_async_copy(
            wrap_ref, begin_out.at[0, :, pl.ds(0, HALO), columns], copy_sem.at[6]
        )
        main_copy.start()
        wrap_copy.start()
        grad_ref[...] = grad_row
        main_copy.wait()
        wrap_copy.wait()

    return kernel


def range_scan(value, direction):
    count = lax.axis_size("range")
    total = value
    for reach in range(1, count):
        total = total + passed_along(value, "range", direction * reach)
    return total


def fused_local(
    checkpoint, adjoint_start, misfit, pade_factors, azimuth_inverse, bottom, base_speed, speed_step
):
    depth_rows = checkpoint.shape[3]
    rows = checkpoint.shape[2]
    block_size = pade_factors.shape[3]
    block_count = depth_rows // block_size
    depth_start = lax.axis_index("line") * depth_rows
    half = rows // 2
    last = block_count - 1
    arrivals = []
    for index in range(last):
        lead_part = adjoint_start[:, :, :half, index * block_size : (index + 1) * block_size]
        lead_part, adjoint_start = lax.optimization_barrier((lead_part, adjoint_start))
        columns = adjoint_start[:, :, :, index * block_size : (index + 1) * block_size]
        lead = passed_along(lead_part, "range", -1)
        rest = passed_along(columns[:, :, half:], "range", -1)
        arrivals.append((lead, rest))
    last_columns = adjoint_start[:, :, :, last * block_size :]
    first_half = passed_along(last_columns[:, :, :half], "range", -1)
    second_half = passed_along(last_columns[:, :, half:], "range", -1)
    halves = [first_half, second_half]
    profile = base_speed + range_scan(speed_step, 1)[0]
    water_phase = phase_scale * (1.0 / (profile * profile) - 1.0)
    bed_row = jnp.full_like(water_phase, bed_phase)
    trig = jnp.stack(
        [jnp.cos(water_phase), jnp.sin(water_phase), jnp.cos(bed_row), jnp.sin(bed_row)]
    )
    limit = (bottom[0] - depth_start)[:, None]
    inverse = azimuth_inverse[0]
    inverse_t = inverse
    field_spec = pl.BlockSpec((None, 2, rows, block_size), lambda b: (0, 0, 0, b))
    trig_spec = pl.BlockSpec((4, block_size), lambda b: (0, b))
    limit_spec = pl.BlockSpec((rows, 1), lambda b: (0, 0))
    pade_spec = pl.BlockSpec(pade_factors.shape, lambda b: (0, 0, 0, 0))
    inverse_spec = pl.BlockSpec(inverse.shape, lambda b: (0, 0, 0))
    field_end = pl.pallas_call(
        forward_kernel,
        grid=(block_count,),
        in_specs=[field_spec, trig_spec, limit_spec, pade_spec, inverse_spec],
        out_specs=field_spec,
        out_shape=jax.ShapeDtypeStruct(checkpoint.shape, jnp.bfloat16),
    )(checkpoint, trig, limit, pade_factors, inverse)
    field_end, arrivals[0] = lax.optimization_barrier((field_end, arrivals[0]))
    adjoint_begin = None
    grads = []
    for index in range(last):
        fixed = lambda b, index=index: (0, 0, 0, index)
        chunk_spec = pl.BlockSpec((None, 2, half, block_size), lambda b: (0, 0, 0, 0))
        block_spec = pl.BlockSpec((None, 2, rows, block_size), fixed)
        in_specs = [
            chunk_spec,
            chunk_spec,
            block_spec,
            block_spec,
            pl.BlockSpec((4, block_size), lambda b, index=index: (0, index)),
            limit_spec,
            pade_spec,
            inverse_spec,
        ]
        operands = [*arrivals[index], misfit, checkpoint, trig, limit, pade_factors, inverse_t]
        aliases = {}
        kernel = make_backward_kernel(index)
        if adjoint_begin is not None:
            in_specs.append(pl.BlockSpec(memory_space=pl.ANY))
            operands.append(adjoint_begin)
            aliases = {len(operands) - 1: 0}
            kernel = lambda *refs, kernel=kernel: kernel(*refs[:8], *refs[9:])
        adjoint_begin, grad_part = pl.pallas_call(
            kernel,
            grid=(1,),
            in_specs=in_specs,
            out_specs=[
                block_spec,
                pl.BlockSpec((1, block_size), lambda b: (0, 0)),
            ],
            out_shape=[
                jax.ShapeDtypeStruct(checkpoint.shape, jnp.bfloat16),
                jax.ShapeDtypeStruct((1, block_size), jnp.float32),
            ],
            input_output_aliases=aliases,
        )(*operands)
        grads.append(grad_part)
    any_spec = pl.BlockSpec(memory_space=pl.ANY)
    fixed_last = lambda b: (0, 0, 0, last)
    half_spec = pl.BlockSpec((None, 2, half, block_size), lambda b: (0, 0, 0, 0))
    trig_last = pl.BlockSpec((4, block_size), lambda b: (0, last))
    grad_spec = pl.BlockSpec((1, block_size), lambda b: (0, 0))
    begin_shape = jax.ShapeDtypeStruct(checkpoint.shape, jnp.bfloat16)
    grad_shape = jax.ShapeDtypeStruct((1, block_size), jnp.float32)
    edge = 2 * HALO
    adjoint_begin, grad_first, halo = pl.pallas_call(
        make_first_half_kernel(last),
        grid=(1,),
        in_specs=[
            half_spec,
            pl.BlockSpec((None, 2, half, block_size), fixed_last),
            pl.BlockSpec((None, 2, half, block_size), fixed_last),
            trig_last,
            limit_spec,
            pade_spec,
            inverse_spec,
            any_spec,
        ],
        out_specs=[any_spec, grad_spec, pl.BlockSpec((4, edge, block_size), lambda b: (0, 0, 0))],
        out_shape=[
            begin_shape, grad_shape, jax.ShapeDtypeStruct((4, edge, block_size), jnp.float32)
        ],
        scratch_shapes=[
            pltpu.VMEM((2, half - 2 * HALO, block_size), jnp.bfloat16),
            pltpu.SemaphoreType.DMA((1,)),
        ],
        input_output_aliases={7: 0},
    )(halves[0], misfit, checkpoint, trig, limit, pade_factors, inverse_t, adjoint_begin)
    tail = rows - half
    adjoint_begin, grad_second = pl.pallas_call(
        make_second_half_kernel(last),
        grid=(1,),
        in_specs=[
            pl.BlockSpec((4, edge, block_size), lambda b: (0, 0, 0)),
            pl.BlockSpec((None, 2, tail, block_size), lambda b: (0, 0, 0, 0)),
            pl.BlockSpec((None, 2, tail, block_size), lambda b: (0, 0, 1, last)),
            any_spec,
            trig_last,
            any_spec,
            any_spec,
            inverse_spec,
            any_spec,
        ],
        out_specs=[any_spec, grad_spec],
        out_shape=[begin_shape, grad_shape],
        scratch_shapes=[
            pltpu.VMEM(pade_factors.shape, jnp.bfloat16),
            pltpu.VMEM((2, tail + HALO, block_size), jnp.bfloat16),
            pltpu.VMEM((2, HALO, block_size), jnp.bfloat16),
            pltpu.VMEM((tail + HALO, 1), jnp.int32),
            pltpu.VMEM((HALO, 1), jnp.int32),
            pltpu.VMEM((2, tail + HALO, block_size), jnp.bfloat16),
            pltpu.VMEM((2, HALO, block_size), jnp.bfloat16),
            pltpu.SemaphoreType.DMA((7,)),
        ],
        input_output_aliases={8: 0},
    )(
        halo, halves[1], misfit, checkpoint, trig, limit, pade_factors, inverse_t,
        adjoint_begin,
    )
    grads.append(grad_first + grad_second)
    grad_sum = jnp.concatenate(grads, axis=1)
    grad_here = grad_sum * (-8.0 / (profile * profile * profile)) / rows
    grad_increment = range_scan(grad_here, -1)
    return (field_end, adjoint_begin, grad_increment)


def local(
    checkpoint, adjoint_start, misfit, pade_factors, azimuth_inverse, bottom, base_speed, speed_step
):
    if (
        checkpoint.shape[3] % pade_factors.shape[3] == 0
        and checkpoint.shape[3] >= 2 * pade_factors.shape[3]
        and checkpoint.shape[2] % (2 * azimuth_inverse.shape[2]) == 0
    ):
        return fused_local(
            checkpoint, adjoint_start, misfit, pade_factors, azimuth_inverse, bottom,
            base_speed, speed_step,
        )
    return general_local(
        checkpoint, adjoint_start, misfit, pade_factors, azimuth_inverse, bottom,
        base_speed, speed_step,
    )


def solution(mesh):
    in_specs = (
        P("range", "freq", None, "line"),
        P("range", "freq", None, "line"),
        P("range", "freq", None, "line"),
        P(None, "freq", None, None),
        P("range", "freq", None, None),
        P("range", None),
        P("line"),
        P("range", "line"),
    )
    out_specs = (
        P("range", "freq", None, "line"),
        P("range", "freq", None, "line"),
        P(("freq", "range"), "line"),
    )
    return jax.shard_map(local, mesh=mesh, in_specs=in_specs, out_specs=out_specs, check_vma=False)
```

```python
import jax
import jax.numpy as jnp
from jax import lax
from jax.sharding import PartitionSpec as P
from jax.experimental import pallas as pl
from jax.experimental.pallas import tpu as pltpu

phase_scale = 4.0
bed_phase = -1.8
coupling = 0.3


def passed_along(value, axis, by):
    count = lax.axis_size(axis)
    pairs = [(i, i + by) for i in range(count) if 0 <= i + by < count]
    return lax.ppermute(value, axis, pairs)


def pair_terms(diag_one, diag_two, cross_one, cross_two, adjoint):
    if adjoint:
        return (diag_one + diag_two, cross_one - cross_two)
    return (diag_one - diag_two, cross_one + cross_two)


def depth_apply(current, pade_ops, adjoint):
    factor_count = pade_ops.shape[0]
    sequence = range(factor_count - 1, -1, -1) if adjoint else range(factor_count)
    for factor in sequence:
        contract = 1 if adjoint else 2
        product = lax.dot_general(
            current,
            pade_ops[factor],
            (((3,), (contract,)), ((), ())),
            preferred_element_type=jnp.float32,
        )
        real_part, imag_part = pair_terms(
            product[0, :, :, 0],
            product[1, :, :, 1],
            product[1, :, :, 0],
            product[0, :, :, 1],
            adjoint,
        )
        current = jnp.stack([real_part, imag_part]).astype(jnp.bfloat16)
    return current


def azimuth_apply(field_in, inverse, adjoint):
    block_width = inverse.shape[1]
    blocked = field_in.reshape(2, field_in.shape[1] // block_width, block_width, field_in.shape[2])
    contract = 1 if adjoint else 2
    product = lax.dot_general(
        inverse, blocked, (((contract,), (2,)), ((), ())), preferred_element_type=jnp.float32
    )
    real_part, imag_part = pair_terms(
        product[0, :, 0], product[1, :, 1], product[0, :, 1], product[1, :, 0], adjoint
    )
    joined = jnp.stack([real_part, imag_part])
    return joined.transpose(0, 2, 1, 3).reshape(field_in.shape)


def numerator_map(field_in):
    return field_in + coupling * (
        jnp.roll(field_in, 1, axis=1) + jnp.roll(field_in, -1, axis=1) - 2.0 * field_in
    )


def screen_phase(profile, bottom_row, depth_start):
    depths = depth_start + jnp.arange(profile.shape[0], dtype=jnp.int32)
    in_water = depths[None, :] < bottom_row[:, None]
    water_phase = phase_scale * (1.0 / (profile * profile) - 1.0)
    return (jnp.where(in_water, water_phase[None, :], bed_phase), in_water)


def depth_segment(field_in, pade_factors, adjoint):
    block_size = pade_factors.shape[3]
    if field_in.shape[2] % block_size == 0:
        worked = depth_apply(
            field_in.reshape(2, field_in.shape[1], field_in.shape[2] // block_size, block_size),
            pade_factors,
            adjoint,
        )
        return worked.reshape(field_in.shape)
    turned = lax.all_to_all(field_in, "line", split_axis=1, concat_axis=2, tiled=True)
    full_depth = turned.shape[2]
    worked = depth_apply(
        turned.reshape(2, turned.shape[1], full_depth // block_size, block_size),
        pade_factors,
        adjoint,
    )
    return lax.all_to_all(
        worked.reshape(turned.shape), "line", split_axis=2, concat_axis=1, tiled=True
    )


def general_local(
    checkpoint, adjoint_start, misfit, pade_factors, azimuth_inverse, bottom, base_speed, speed_step
):
    depth_rows = checkpoint.shape[3]
    depth_start = lax.axis_index("line") * depth_rows
    every_step = lax.all_gather(speed_step, "range", axis=0, tiled=True)
    running = jnp.cumsum(every_step, axis=0)
    profile = base_speed + lax.dynamic_index_in_dim(
        running, lax.axis_index("range"), 0, keepdims=False
    )
    phase_angle, in_water = screen_phase(profile, bottom[0], depth_start)
    cosine = jnp.cos(phase_angle)
    sine_term = jnp.sin(phase_angle)
    source = checkpoint[0].astype(jnp.float32)
    screened = jnp.stack(
        [cosine * source[0] - sine_term * source[1], sine_term * source[0] + cosine * source[1]]
    ).astype(jnp.bfloat16)
    depth_out = depth_segment(screened, pade_factors, False)
    numerator = numerator_map(depth_out.astype(jnp.float32)).astype(jnp.bfloat16)
    inverse = azimuth_inverse[0]
    field_end = azimuth_apply(numerator, inverse, False).astype(jnp.bfloat16)
    arrival = passed_along(adjoint_start, "range", -1)
    lam_end = (arrival[0].astype(jnp.float32) + misfit[0].astype(jnp.float32)).astype(jnp.bfloat16)
    backward = numerator_map(azimuth_apply(lam_end, inverse, True)).astype(jnp.bfloat16)
    backward = depth_segment(backward, pade_factors, True)
    cotangent = backward.astype(jnp.float32)
    adjoint_begin = jnp.stack(
        [
            cosine * cotangent[0] + sine_term * cotangent[1],
            cosine * cotangent[1] - sine_term * cotangent[0],
        ]
    ).astype(jnp.bfloat16)
    screened_f = screened.astype(jnp.float32)
    weight = jnp.where(in_water, cotangent[1] * screened_f[0] - cotangent[0] * screened_f[1], 0.0)
    grad_here = (
        jnp.sum(weight, axis=0) * (-8.0 / (profile * profile * profile)) / checkpoint.shape[2]
    )[None, :]
    all_grads = lax.all_gather(grad_here, "range", axis=0, tiled=True)
    suffix = jnp.flip(jnp.cumsum(jnp.flip(all_grads, 0), axis=0), 0)
    grad_increment = lax.dynamic_slice_in_dim(suffix, lax.axis_index("range"), 1, 0)
    return (field_end[None], adjoint_begin[None], grad_increment)


def dot_nt(left, right):
    return lax.dot_general(
        left, right, (((1,), (1,)), ((), ())), preferred_element_type=jnp.float32
    )


def dot_nn(left, right):
    return jnp.dot(left, right, preferred_element_type=jnp.float32)


def numerator_rows(field_in):
    rows = field_in.shape[0]
    return field_in + coupling * (
        pltpu.roll(field_in, 1, 0) + pltpu.roll(field_in, rows - 1, 0) - 2.0 * field_in
    )


def phase_tile(trig_ref, limit_ref, block_index, shape):
    columns = lax.broadcasted_iota(jnp.int32, shape, 1) + block_index * shape[1]
    in_water = columns < limit_ref[...]
    trig = trig_ref[...]
    cosine = jnp.where(in_water, trig[0:1], trig[2:3])
    sine_term = jnp.where(in_water, trig[1:2], trig[3:4])
    return cosine, sine_term, in_water


def screen_tile(source_ref, cosine, sine_term):
    source_r = source_ref[0].astype(jnp.float32)
    source_i = source_ref[1].astype(jnp.float32)
    screened_r = (cosine * source_r - sine_term * source_i).astype(jnp.bfloat16)
    screened_i = (sine_term * source_r + cosine * source_i).astype(jnp.bfloat16)
    return screened_r, screened_i


def forward_kernel(source_ref, trig_ref, limit_ref, pade_ref, inverse_ref, out_ref):
    block_index = pl.program_id(0)
    rows, width = source_ref.shape[1], source_ref.shape[2]
    cosine, sine_term, _ = phase_tile(trig_ref, limit_ref, block_index, (rows, width))
    cur_r, cur_i = screen_tile(source_ref, cosine, sine_term)
    for factor in range(pade_ref.shape[0]):
        pade_r = pade_ref[factor, 0]
        pade_i = pade_ref[factor, 1]
        real_part = dot_nt(cur_r, pade_r) - dot_nt(cur_i, pade_i)
        imag_part = dot_nt(cur_i, pade_r) + dot_nt(cur_r, pade_i)
        cur_r = real_part.astype(jnp.bfloat16)
        cur_i = imag_part.astype(jnp.bfloat16)
    num_r = numerator_rows(cur_r.astype(jnp.float32)).astype(jnp.bfloat16)
    num_i = numerator_rows(cur_i.astype(jnp.float32)).astype(jnp.bfloat16)
    inv_r = inverse_ref[0]
    inv_i = inverse_ref[1]
    block_width = inv_r.shape[0]
    for start in range(0, rows, block_width):
        part_r = num_r[start : start + block_width]
        part_i = num_i[start : start + block_width]
        out_ref[0, start : start + block_width, :] = (
            dot_nn(inv_r, part_r) - dot_nn(inv_i, part_i)
        ).astype(jnp.bfloat16)
        out_ref[1, start : start + block_width, :] = (
            dot_nn(inv_r, part_i) + dot_nn(inv_i, part_r)
        ).astype(jnp.bfloat16)


def make_backward_kernel(block_index):
    def backward_kernel(
        arrival_ref, misfit_ref, source_ref, trig_ref, limit_ref, pade_ref, inverse_t_ref,
        out_ref, grad_ref,
    ):
        rows, width = source_ref.shape[1], source_ref.shape[2]
        lam_r = (
            arrival_ref[0].astype(jnp.float32) + misfit_ref[0].astype(jnp.float32)
        ).astype(jnp.bfloat16)
        lam_i = (
            arrival_ref[1].astype(jnp.float32) + misfit_ref[1].astype(jnp.float32)
        ).astype(jnp.bfloat16)
        inv_r = inverse_t_ref[0]
        inv_i = inverse_t_ref[1]
        block_width = inv_r.shape[0]
        pieces_r = []
        pieces_i = []
        for start in range(0, rows, block_width):
            part_r = lam_r[start : start + block_width]
            part_i = lam_i[start : start + block_width]
            pieces_r.append(dot_nn(inv_r, part_r) + dot_nn(inv_i, part_i))
            pieces_i.append(dot_nn(inv_r, part_i) - dot_nn(inv_i, part_r))
        cur_r = numerator_rows(jnp.concatenate(pieces_r, axis=0)).astype(jnp.bfloat16)
        cur_i = numerator_rows(jnp.concatenate(pieces_i, axis=0)).astype(jnp.bfloat16)
        for factor in range(pade_ref.shape[0] - 1, -1, -1):
            pade_r = pade_ref[factor, 0]
            pade_i = pade_ref[factor, 1]
            real_part = dot_nn(cur_r, pade_r) + dot_nn(cur_i, pade_i)
            imag_part = dot_nn(cur_i, pade_r) - dot_nn(cur_r, pade_i)
            cur_r = real_part.astype(jnp.bfloat16)
            cur_i = imag_part.astype(jnp.bfloat16)
        cot_r = cur_r.astype(jnp.float32)
        cot_i = cur_i.astype(jnp.float32)
        cosine, sine_term, in_water = phase_tile(trig_ref, limit_ref, block_index, (rows, width))
        out_ref[0] = (cosine * cot_r + sine_term * cot_i).astype(jnp.bfloat16)
        out_ref[1] = (cosine * cot_i - sine_term * cot_r).astype(jnp.bfloat16)
        screened_r, screened_i = screen_tile(source_ref, cosine, sine_term)
        weight = jnp.where(
            in_water,
            cot_i * screened_r.astype(jnp.float32) - cot_r * screened_i.astype(jnp.float32),
            0.0,
        )
        grad_ref[...] = jnp.sum(weight, axis=0, keepdims=True)

    return backward_kernel


def lam_rows(arrival, misfit_part):
    return (arrival.astype(jnp.float32) + misfit_part.astype(jnp.float32)).astype(jnp.bfloat16)


def azimuth_adjoint(inv_r, inv_i, part_r, part_i):
    return (
        dot_nn(inv_r, part_r) + dot_nn(inv_i, part_i),
        dot_nn(inv_r, part_i) - dot_nn(inv_i, part_r),
    )


def depth_adjoint(cur_r, cur_i, pade_ref):
    for factor in range(pade_ref.shape[0] - 1, -1, -1):
        pade_r = pade_ref[factor, 0]
        pade_i = pade_ref[factor, 1]
        real_part = dot_nn(cur_r, pade_r) + dot_nn(cur_i, pade_i)
        imag_part = dot_nn(cur_i, pade_r) - dot_nn(cur_r, pade_i)
        cur_r = real_part.astype(jnp.bfloat16)
        cur_i = imag_part.astype(jnp.bfloat16)
    return cur_r.astype(jnp.float32), cur_i.astype(jnp.float32)


def finish_rows(cot_r, cot_i, trig_ref, limit_rows, source_r, source_i, block_index):
    shape = cot_r.shape
    columns = lax.broadcasted_iota(jnp.int32, shape, 1) + block_index * shape[1]
    in_water = columns < limit_rows
    trig = trig_ref[...]
    cosine = jnp.where(in_water, trig[0:1], trig[2:3])
    sine_term = jnp.where(in_water, trig[1:2], trig[3:4])
    out_r = cosine * cot_r + sine_term * cot_i
    out_i = cosine * cot_i - sine_term * cot_r
    screened_r = (cosine * source_r - sine_term * source_i).astype(jnp.bfloat16)
    screened_i = (sine_term * source_r + cosine * source_i).astype(jnp.bfloat16)
    weight = jnp.where(
        in_water,
        cot_i * screened_r.astype(jnp.float32) - cot_r * screened_i.astype(jnp.float32),
        0.0,
    )
    return out_r, out_i, jnp.sum(weight, axis=0, keepdims=True)


HALO = 8


def make_first_half_kernel(block_index):
    def kernel(
        arrival_ref, misfit_ref, source_ref, trig_ref, limit_ref, pade_ref, inverse_t_ref,
        begin_in, begin_out, grad_ref, halo_ref, stage_ref, copy_sem,
    ):
        half, width = arrival_ref.shape[1], arrival_ref.shape[2]
        lam_r = lam_rows(arrival_ref[0], misfit_ref[0])
        lam_i = lam_rows(arrival_ref[1], misfit_ref[1])
        inv_r = inverse_t_ref[0]
        inv_i = inverse_t_ref[1]
        block_width = inv_r.shape[0]
        pieces_r = []
        pieces_i = []
        for start in range(0, half, block_width):
            piece_r, piece_i = azimuth_adjoint(
                inv_r, inv_i, lam_r[start : start + block_width], lam_i[start : start + block_width]
            )
            pieces_r.append(piece_r)
            pieces_i.append(piece_i)
        whole_r = jnp.concatenate(pieces_r, axis=0)
        whole_i = jnp.concatenate(pieces_i, axis=0)
        edge = 2 * HALO
        halo_ref[0] = whole_r[half - edge :]
        halo_ref[1] = whole_i[half - edge :]
        halo_ref[2] = whole_r[:edge]
        halo_ref[3] = whole_i[:edge]
        num_r = numerator_rows(whole_r)[HALO : half - HALO]
        num_i = numerator_rows(whole_i)[HALO : half - HALO]
        cot_r, cot_i = depth_adjoint(
            num_r.astype(jnp.bfloat16), num_i.astype(jnp.bfloat16), pade_ref
        )
        source_r = source_ref[0].astype(jnp.float32)[HALO : half - HALO]
        source_i = source_ref[1].astype(jnp.float32)[HALO : half - HALO]
        out_r, out_i, grad_row = finish_rows(
            cot_r, cot_i, trig_ref, limit_ref[HALO : half - HALO], source_r, source_i, block_index
        )
        stage_ref[0] = out_r.astype(jnp.bfloat16)
        stage_ref[1] = out_i.astype(jnp.bfloat16)
        copy = pltpu.make_async_copy(
            stage_ref,
            begin_out.at[0, :, pl.ds(HALO, half - 2 * HALO), pl.ds(block_index * width, width)],
            copy_sem.at[0],
        )
        copy.start()
        grad_ref[...] = grad_row
        copy.wait()

    return kernel


def make_second_half_kernel(block_index):
    def kernel(
        halo_ref, arrival_ref, misfit_ref, source_hbm, trig_ref, limit_hbm, pade_hbm,
        inverse_t_ref, begin_in, whole_grad_ref, first_grad_ref, scale_ref,
        begin_out, grad_ref, pade_ref, source_main, source_wrap,
        limit_main, limit_wrap, main_ref, wrap_ref, copy_sem,
    ):
        tail, width = arrival_ref.shape[1], arrival_ref.shape[2]
        half = source_hbm.shape[2] - tail
        columns = pl.ds(block_index * width, width)
        loads = [
            pltpu.make_async_copy(pade_hbm, pade_ref, copy_sem.at[0]),
            pltpu.make_async_copy(
                source_hbm.at[0, :, pl.ds(half - HALO, tail + HALO), columns],
                source_main,
                copy_sem.at[1],
            ),
            pltpu.make_async_copy(
                source_hbm.at[0, :, pl.ds(0, HALO), columns], source_wrap, copy_sem.at[2]
            ),
            pltpu.make_async_copy(
                limit_hbm.at[pl.ds(half - HALO, tail + HALO)], limit_main, copy_sem.at[3]
            ),
            pltpu.make_async_copy(limit_hbm.at[pl.ds(0, HALO)], limit_wrap, copy_sem.at[4]),
        ]
        for load in loads:
            load.start()
        inv_r = inverse_t_ref[0]
        inv_i = inverse_t_ref[1]
        block_width = inv_r.shape[0]
        lam_r = lam_rows(arrival_ref[0], misfit_ref[0])
        lam_i = lam_rows(arrival_ref[1], misfit_ref[1])
        pieces_r = [halo_ref[0]]
        pieces_i = [halo_ref[1]]
        for start in range(0, tail, block_width):
            piece_r, piece_i = azimuth_adjoint(
                inv_r, inv_i, lam_r[start : start + block_width], lam_i[start : start + block_width]
            )
            pieces_r.append(piece_r)
            pieces_i.append(piece_i)
        pieces_r.append(halo_ref[2])
        pieces_i.append(halo_ref[3])
        span = tail + 2 * HALO
        num_r = numerator_rows(jnp.concatenate(pieces_r, axis=0))[HALO : HALO + span]
        num_i = numerator_rows(jnp.concatenate(pieces_i, axis=0))[HALO : HALO + span]
        loads[0].wait()
        cot_r, cot_i = depth_adjoint(
            num_r.astype(jnp.bfloat16), num_i.astype(jnp.bfloat16), pade_ref
        )
        for load in loads[1:]:
            load.wait()
        source_r = jnp.concatenate(
            [source_main[0].astype(jnp.float32), source_wrap[0].astype(jnp.float32)], axis=0
        )
        source_i = jnp.concatenate(
            [source_main[1].astype(jnp.float32), source_wrap[1].astype(jnp.float32)], axis=0
        )
        limit_rows = jnp.concatenate([limit_main[...], limit_wrap[...]], axis=0)
        out_r, out_i, grad_row = finish_rows(
            cot_r, cot_i, trig_ref, limit_rows, source_r, source_i, block_index
        )
        main_ref[0] = out_r[: tail + HALO].astype(jnp.bfloat16)
        main_ref[1] = out_i[: tail + HALO].astype(jnp.bfloat16)
        wrap_ref[0] = out_r[tail + HALO :].astype(jnp.bfloat16)
        wrap_ref[1] = out_i[tail + HALO :].astype(jnp.bfloat16)
        main_copy = pltpu.make_async_copy(
            main_ref, begin_out.at[0, :, pl.ds(half - HALO, tail + HALO), columns], copy_sem.at[5]
        )
        wrap_copy = pltpu.make_async_copy(
            wrap_ref, begin_out.at[0, :, pl.ds(0, HALO), columns], copy_sem.at[6]
        )
        main_copy.start()
        wrap_copy.start()
        scale = scale_ref[...]
        lead = block_index * width
        grad_ref[:, :lead] = whole_grad_ref[...] * scale[:, :lead] / (half + tail)
        grad_ref[:, lead:] = (first_grad_ref[...] + grad_row) * scale[:, lead:] / (half + tail)
        main_copy.wait()
        wrap_copy.wait()

    return kernel


def range_scan(value, direction):
    count = lax.axis_size("range")
    total = value
    for reach in range(1, count):
        total = total + passed_along(value, "range", direction * reach)
    return total


def fused_local(
    checkpoint, adjoint_start, misfit, pade_factors, azimuth_inverse, bottom, base_speed, speed_step
):
    depth_rows = checkpoint.shape[3]
    rows = checkpoint.shape[2]
    block_size = pade_factors.shape[3]
    block_count = depth_rows // block_size
    depth_start = lax.axis_index("line") * depth_rows
    half = rows // 2
    last = block_count - 1
    arrivals = [
        passed_along(
            adjoint_start[:, :, :, index * block_size : (index + 1) * block_size], "range", -1
        )
        for index in range(last)
    ]
    last_columns = adjoint_start[:, :, :, last * block_size :]
    first_half = passed_along(last_columns[:, :, :half], "range", -1)
    second_half = passed_along(last_columns[:, :, half:], "range", -1)
    halves = [first_half, second_half]
    profile = base_speed + range_scan(speed_step, 1)[0]
    water_phase = phase_scale * (1.0 / (profile * profile) - 1.0)
    bed_row = jnp.full_like(water_phase, bed_phase)
    trig = jnp.stack(
        [jnp.cos(water_phase), jnp.sin(water_phase), jnp.cos(bed_row), jnp.sin(bed_row)]
    )
    limit = (bottom[0] - depth_start)[:, None]
    inverse = azimuth_inverse[0]
    inverse_t = jnp.swapaxes(inverse, 1, 2)
    field_spec = pl.BlockSpec((None, 2, rows, block_size), lambda b: (0, 0, 0, b))
    trig_spec = pl.BlockSpec((4, block_size), lambda b: (0, b))
    limit_spec = pl.BlockSpec((rows, 1), lambda b: (0, 0))
    pade_spec = pl.BlockSpec(pade_factors.shape, lambda b: (0, 0, 0, 0))
    inverse_spec = pl.BlockSpec(inverse.shape, lambda b: (0, 0, 0))
    field_end = pl.pallas_call(
        forward_kernel,
        grid=(block_count,),
        in_specs=[field_spec, trig_spec, limit_spec, pade_spec, inverse_spec],
        out_specs=field_spec,
        out_shape=jax.ShapeDtypeStruct(checkpoint.shape, jnp.bfloat16),
    )(checkpoint, trig, limit, pade_factors, inverse)
    field_end, arrivals[0] = lax.optimization_barrier((field_end, arrivals[0]))
    adjoint_begin = None
    grads = []
    for index in range(last):
        fixed = lambda b, index=index: (0, 0, 0, index)
        chunk_spec = pl.BlockSpec((None, 2, rows, block_size), lambda b: (0, 0, 0, 0))
        block_spec = pl.BlockSpec((None, 2, rows, block_size), fixed)
        in_specs = [
            chunk_spec,
            block_spec,
            block_spec,
            pl.BlockSpec((4, block_size), lambda b, index=index: (0, index)),
            limit_spec,
            pade_spec,
            inverse_spec,
        ]
        operands = [arrivals[index], misfit, checkpoint, trig, limit, pade_factors, inverse_t]
        aliases = {}
        kernel = make_backward_kernel(index)
        if adjoint_begin is not None:
            in_specs.append(pl.BlockSpec(memory_space=pl.ANY))
            operands.append(adjoint_begin)
            aliases = {len(operands) - 1: 0}
            kernel = lambda *refs, kernel=kernel: kernel(*refs[:7], *refs[8:])
        adjoint_begin, grad_part = pl.pallas_call(
            kernel,
            grid=(1,),
            in_specs=in_specs,
            out_specs=[
                block_spec,
                pl.BlockSpec((1, block_size), lambda b: (0, 0)),
            ],
            out_shape=[
                jax.ShapeDtypeStruct(checkpoint.shape, jnp.bfloat16),
                jax.ShapeDtypeStruct((1, block_size), jnp.float32),
            ],
            input_output_aliases=aliases,
        )(*operands)
        grads.append(grad_part)
    any_spec = pl.BlockSpec(memory_space=pl.ANY)
    fixed_last = lambda b: (0, 0, 0, last)
    half_spec = pl.BlockSpec((None, 2, half, block_size), lambda b: (0, 0, 0, 0))
    trig_last = pl.BlockSpec((4, block_size), lambda b: (0, last))
    grad_spec = pl.BlockSpec((1, block_size), lambda b: (0, 0))
    begin_shape = jax.ShapeDtypeStruct(checkpoint.shape, jnp.bfloat16)
    grad_shape = jax.ShapeDtypeStruct((1, block_size), jnp.float32)
    edge = 2 * HALO
    adjoint_begin, grad_first, halo = pl.pallas_call(
        make_first_half_kernel(last),
        grid=(1,),
        in_specs=[
            half_spec,
            pl.BlockSpec((None, 2, half, block_size), fixed_last),
            pl.BlockSpec((None, 2, half, block_size), fixed_last),
            trig_last,
            limit_spec,
            pade_spec,
            inverse_spec,
            any_spec,
        ],
        out_specs=[any_spec, grad_spec, pl.BlockSpec((4, edge, block_size), lambda b: (0, 0, 0))],
        out_shape=[
            begin_shape, grad_shape, jax.ShapeDtypeStruct((4, edge, block_size), jnp.float32)
        ],
        scratch_shapes=[
            pltpu.VMEM((2, half - 2 * HALO, block_size), jnp.bfloat16),
            pltpu.SemaphoreType.DMA((1,)),
        ],
        input_output_aliases={7: 0},
    )(halves[0], misfit, checkpoint, trig, limit, pade_factors, inverse_t, adjoint_begin)
    tail = rows - half
    scale = (-8.0 / (profile * profile * profile))[None, :]
    whole_row = pl.BlockSpec((1, depth_rows), lambda b: (0, 0))
    adjoint_begin, grad_here = pl.pallas_call(
        make_second_half_kernel(last),
        grid=(1,),
        in_specs=[
            pl.BlockSpec((4, edge, block_size), lambda b: (0, 0, 0)),
            pl.BlockSpec((None, 2, tail, block_size), lambda b: (0, 0, 0, 0)),
            pl.BlockSpec((None, 2, tail, block_size), lambda b: (0, 0, 1, last)),
            any_spec,
            trig_last,
            any_spec,
            any_spec,
            inverse_spec,
            any_spec,
            pl.BlockSpec((1, last * block_size), lambda b: (0, 0)),
            grad_spec,
            whole_row,
        ],
        out_specs=[any_spec, whole_row],
        out_shape=[begin_shape, jax.ShapeDtypeStruct((1, depth_rows), jnp.float32)],
        scratch_shapes=[
            pltpu.VMEM(pade_factors.shape, jnp.bfloat16),
            pltpu.VMEM((2, tail + HALO, block_size), jnp.bfloat16),
            pltpu.VMEM((2, HALO, block_size), jnp.bfloat16),
            pltpu.VMEM((tail + HALO, 1), jnp.int32),
            pltpu.VMEM((HALO, 1), jnp.int32),
            pltpu.VMEM((2, tail + HALO, block_size), jnp.bfloat16),
            pltpu.VMEM((2, HALO, block_size), jnp.bfloat16),
            pltpu.SemaphoreType.DMA((7,)),
        ],
        input_output_aliases={8: 0},
    )(
        halo, halves[1], misfit, checkpoint, trig, limit, pade_factors, inverse_t,
        adjoint_begin, jnp.concatenate(grads, axis=1), grad_first, scale,
    )
    grad_increment = range_scan(grad_here, -1)
    return (field_end, adjoint_begin, grad_increment)


def local(
    checkpoint, adjoint_start, misfit, pade_factors, azimuth_inverse, bottom, base_speed, speed_step
):
    if (
        checkpoint.shape[3] % pade_factors.shape[3] == 0
        and checkpoint.shape[3] >= 2 * pade_factors.shape[3]
        and checkpoint.shape[2] % (2 * azimuth_inverse.shape[2]) == 0
    ):
        return fused_local(
            checkpoint, adjoint_start, misfit, pade_factors, azimuth_inverse, bottom,
            base_speed, speed_step,
        )
    return general_local(
        checkpoint, adjoint_start, misfit, pade_factors, azimuth_inverse, bottom,
        base_speed, speed_step,
    )


def solution(mesh):
    in_specs = (
        P("range", "freq", None, "line"),
        P("range", "freq", None, "line"),
        P("range", "freq", None, "line"),
        P(None, "freq", None, None),
        P("range", "freq", None, None),
        P("range", None),
        P("line"),
        P("range", "line"),
    )
    out_specs = (
        P("range", "freq", None, "line"),
        P("range", "freq", None, "line"),
        P(("freq", "range"), "line"),
    )
    return jax.shard_map(local, mesh=mesh, in_specs=in_specs, out_specs=out_specs, check_vma=False)
```

```python
import jax
import jax.numpy as jnp
from jax import lax
from jax.sharding import PartitionSpec as P
from jax.experimental import pallas as pl
from jax.experimental.pallas import tpu as pltpu

phase_scale = 4.0
bed_phase = -1.8
coupling = 0.3


def passed_along(value, axis, by):
    count = lax.axis_size(axis)
    pairs = [(i, i + by) for i in range(count) if 0 <= i + by < count]
    return lax.ppermute(value, axis, pairs)


def pair_terms(diag_one, diag_two, cross_one, cross_two, adjoint):
    if adjoint:
        return (diag_one + diag_two, cross_one - cross_two)
    return (diag_one - diag_two, cross_one + cross_two)


def depth_apply(current, pade_ops, adjoint):
    factor_count = pade_ops.shape[0]
    sequence = range(factor_count - 1, -1, -1) if adjoint else range(factor_count)
    for factor in sequence:
        contract = 1 if adjoint else 2
        product = lax.dot_general(
            current,
            pade_ops[factor],
            (((3,), (contract,)), ((), ())),
            preferred_element_type=jnp.float32,
        )
        real_part, imag_part = pair_terms(
            product[0, :, :, 0],
            product[1, :, :, 1],
            product[1, :, :, 0],
            product[0, :, :, 1],
            adjoint,
        )
        current = jnp.stack([real_part, imag_part]).astype(jnp.bfloat16)
    return current


def azimuth_apply(field_in, inverse, adjoint):
    block_width = inverse.shape[1]
    blocked = field_in.reshape(2, field_in.shape[1] // block_width, block_width, field_in.shape[2])
    contract = 1 if adjoint else 2
    product = lax.dot_general(
        inverse, blocked, (((contract,), (2,)), ((), ())), preferred_element_type=jnp.float32
    )
    real_part, imag_part = pair_terms(
        product[0, :, 0], product[1, :, 1], product[0, :, 1], product[1, :, 0], adjoint
    )
    joined = jnp.stack([real_part, imag_part])
    return joined.transpose(0, 2, 1, 3).reshape(field_in.shape)


def numerator_map(field_in):
    return field_in + coupling * (
        jnp.roll(field_in, 1, axis=1) + jnp.roll(field_in, -1, axis=1) - 2.0 * field_in
    )


def screen_phase(profile, bottom_row, depth_start):
    depths = depth_start + jnp.arange(profile.shape[0], dtype=jnp.int32)
    in_water = depths[None, :] < bottom_row[:, None]
    water_phase = phase_scale * (1.0 / (profile * profile) - 1.0)
    return (jnp.where(in_water, water_phase[None, :], bed_phase), in_water)


def depth_segment(field_in, pade_factors, adjoint):
    block_size = pade_factors.shape[3]
    if field_in.shape[2] % block_size == 0:
        worked = depth_apply(
            field_in.reshape(2, field_in.shape[1], field_in.shape[2] // block_size, block_size),
            pade_factors,
            adjoint,
        )
        return worked.reshape(field_in.shape)
    turned = lax.all_to_all(field_in, "line", split_axis=1, concat_axis=2, tiled=True)
    full_depth = turned.shape[2]
    worked = depth_apply(
        turned.reshape(2, turned.shape[1], full_depth // block_size, block_size),
        pade_factors,
        adjoint,
    )
    return lax.all_to_all(
        worked.reshape(turned.shape), "line", split_axis=2, concat_axis=1, tiled=True
    )


def general_local(
    checkpoint, adjoint_start, misfit, pade_factors, azimuth_inverse, bottom, base_speed, speed_step
):
    depth_rows = checkpoint.shape[3]
    depth_start = lax.axis_index("line") * depth_rows
    every_step = lax.all_gather(speed_step, "range", axis=0, tiled=True)
    running = jnp.cumsum(every_step, axis=0)
    profile = base_speed + lax.dynamic_index_in_dim(
        running, lax.axis_index("range"), 0, keepdims=False
    )
    phase_angle, in_water = screen_phase(profile, bottom[0], depth_start)
    cosine = jnp.cos(phase_angle)
    sine_term = jnp.sin(phase_angle)
    source = checkpoint[0].astype(jnp.float32)
    screened = jnp.stack(
        [cosine * source[0] - sine_term * source[1], sine_term * source[0] + cosine * source[1]]
    ).astype(jnp.bfloat16)
    depth_out = depth_segment(screened, pade_factors, False)
    numerator = numerator_map(depth_out.astype(jnp.float32)).astype(jnp.bfloat16)
    inverse = azimuth_inverse[0]
    field_end = azimuth_apply(numerator, inverse, False).astype(jnp.bfloat16)
    arrival = passed_along(adjoint_start, "range", -1)
    lam_end = (arrival[0].astype(jnp.float32) + misfit[0].astype(jnp.float32)).astype(jnp.bfloat16)
    backward = numerator_map(azimuth_apply(lam_end, inverse, True)).astype(jnp.bfloat16)
    backward = depth_segment(backward, pade_factors, True)
    cotangent = backward.astype(jnp.float32)
    adjoint_begin = jnp.stack(
        [
            cosine * cotangent[0] + sine_term * cotangent[1],
            cosine * cotangent[1] - sine_term * cotangent[0],
        ]
    ).astype(jnp.bfloat16)
    screened_f = screened.astype(jnp.float32)
    weight = jnp.where(in_water, cotangent[1] * screened_f[0] - cotangent[0] * screened_f[1], 0.0)
    grad_here = (
        jnp.sum(weight, axis=0) * (-8.0 / (profile * profile * profile)) / checkpoint.shape[2]
    )[None, :]
    all_grads = lax.all_gather(grad_here, "range", axis=0, tiled=True)
    suffix = jnp.flip(jnp.cumsum(jnp.flip(all_grads, 0), axis=0), 0)
    grad_increment = lax.dynamic_slice_in_dim(suffix, lax.axis_index("range"), 1, 0)
    return (field_end[None], adjoint_begin[None], grad_increment)


def dot_nt(left, right):
    return lax.dot_general(
        left, right, (((1,), (1,)), ((), ())), preferred_element_type=jnp.float32
    )


def dot_nn(left, right):
    return jnp.dot(left, right, preferred_element_type=jnp.float32)


def numerator_rows(field_in):
    rows = field_in.shape[0]
    return field_in + coupling * (
        pltpu.roll(field_in, 1, 0) + pltpu.roll(field_in, rows - 1, 0) - 2.0 * field_in
    )


def phase_tile(trig_ref, limit_ref, block_index, shape):
    columns = lax.broadcasted_iota(jnp.int32, shape, 1) + block_index * shape[1]
    in_water = columns < limit_ref[...]
    trig = trig_ref[...]
    cosine = jnp.where(in_water, trig[0:1], trig[2:3])
    sine_term = jnp.where(in_water, trig[1:2], trig[3:4])
    return cosine, sine_term, in_water


def screen_tile(source_ref, cosine, sine_term):
    source_r = source_ref[0].astype(jnp.float32)
    source_i = source_ref[1].astype(jnp.float32)
    screened_r = (cosine * source_r - sine_term * source_i).astype(jnp.bfloat16)
    screened_i = (sine_term * source_r + cosine * source_i).astype(jnp.bfloat16)
    return screened_r, screened_i


def forward_kernel(source_ref, trig_ref, limit_ref, pade_ref, inverse_ref, out_ref):
    block_index = pl.program_id(0)
    rows, width = source_ref.shape[1], source_ref.shape[2]
    cosine, sine_term, _ = phase_tile(trig_ref, limit_ref, block_index, (rows, width))
    cur_r, cur_i = screen_tile(source_ref, cosine, sine_term)
    for factor in range(pade_ref.shape[0]):
        pade_r = pade_ref[factor, 0]
        pade_i = pade_ref[factor, 1]
        real_part = dot_nt(cur_r, pade_r) - dot_nt(cur_i, pade_i)
        imag_part = dot_nt(cur_i, pade_r) + dot_nt(cur_r, pade_i)
        cur_r = real_part.astype(jnp.bfloat16)
        cur_i = imag_part.astype(jnp.bfloat16)
    num_r = numerator_rows(cur_r.astype(jnp.float32)).astype(jnp.bfloat16)
    num_i = numerator_rows(cur_i.astype(jnp.float32)).astype(jnp.bfloat16)
    inv_r = inverse_ref[0]
    inv_i = inverse_ref[1]
    block_width = inv_r.shape[0]
    for start in range(0, rows, block_width):
        part_r = num_r[start : start + block_width]
        part_i = num_i[start : start + block_width]
        out_ref[0, start : start + block_width, :] = (
            dot_nn(inv_r, part_r) - dot_nn(inv_i, part_i)
        ).astype(jnp.bfloat16)
        out_ref[1, start : start + block_width, :] = (
            dot_nn(inv_r, part_i) + dot_nn(inv_i, part_r)
        ).astype(jnp.bfloat16)


def make_backward_kernel(block_index):
    def backward_kernel(
        arrival_ref, misfit_ref, source_ref, trig_ref, limit_ref, pade_ref, inverse_t_ref,
        out_ref, grad_ref,
    ):
        rows, width = source_ref.shape[1], source_ref.shape[2]
        lam_r = (
            arrival_ref[0].astype(jnp.float32) + misfit_ref[0].astype(jnp.float32)
        ).astype(jnp.bfloat16)
        lam_i = (
            arrival_ref[1].astype(jnp.float32) + misfit_ref[1].astype(jnp.float32)
        ).astype(jnp.bfloat16)
        inv_r = inverse_t_ref[0]
        inv_i = inverse_t_ref[1]
        block_width = inv_r.shape[0]
        pieces_r = []
        pieces_i = []
        for start in range(0, rows, block_width):
            part_r = lam_r[start : start + block_width]
            part_i = lam_i[start : start + block_width]
            pieces_r.append(dot_nn(inv_r, part_r) + dot_nn(inv_i, part_i))
            pieces_i.append(dot_nn(inv_r, part_i) - dot_nn(inv_i, part_r))
        cur_r = numerator_rows(jnp.concatenate(pieces_r, axis=0)).astype(jnp.bfloat16)
        cur_i = numerator_rows(jnp.concatenate(pieces_i, axis=0)).astype(jnp.bfloat16)
        for factor in range(pade_ref.shape[0] - 1, -1, -1):
            pade_r = pade_ref[factor, 0]
            pade_i = pade_ref[factor, 1]
            real_part = dot_nn(cur_r, pade_r) + dot_nn(cur_i, pade_i)
            imag_part = dot_nn(cur_i, pade_r) - dot_nn(cur_r, pade_i)
            cur_r = real_part.astype(jnp.bfloat16)
            cur_i = imag_part.astype(jnp.bfloat16)
        cot_r = cur_r.astype(jnp.float32)
        cot_i = cur_i.astype(jnp.float32)
        cosine, sine_term, in_water = phase_tile(trig_ref, limit_ref, block_index, (rows, width))
        out_ref[0] = (cosine * cot_r + sine_term * cot_i).astype(jnp.bfloat16)
        out_ref[1] = (cosine * cot_i - sine_term * cot_r).astype(jnp.bfloat16)
        screened_r, screened_i = screen_tile(source_ref, cosine, sine_term)
        weight = jnp.where(
            in_water,
            cot_i * screened_r.astype(jnp.float32) - cot_r * screened_i.astype(jnp.float32),
            0.0,
        )
        grad_ref[...] = jnp.sum(weight, axis=0, keepdims=True)

    return backward_kernel


def lam_rows(arrival, misfit_part):
    return (arrival.astype(jnp.float32) + misfit_part.astype(jnp.float32)).astype(jnp.bfloat16)


def azimuth_adjoint(inv_r, inv_i, part_r, part_i):
    return (
        dot_nn(inv_r, part_r) + dot_nn(inv_i, part_i),
        dot_nn(inv_r, part_i) - dot_nn(inv_i, part_r),
    )


def depth_adjoint(cur_r, cur_i, pade_ref):
    for factor in range(pade_ref.shape[0] - 1, -1, -1):
        pade_r = pade_ref[factor, 0]
        pade_i = pade_ref[factor, 1]
        real_part = dot_nn(cur_r, pade_r) + dot_nn(cur_i, pade_i)
        imag_part = dot_nn(cur_i, pade_r) - dot_nn(cur_r, pade_i)
        cur_r = real_part.astype(jnp.bfloat16)
        cur_i = imag_part.astype(jnp.bfloat16)
    return cur_r.astype(jnp.float32), cur_i.astype(jnp.float32)


def finish_rows(cot_r, cot_i, trig_ref, limit_rows, source_r, source_i, block_index):
    shape = cot_r.shape
    columns = lax.broadcasted_iota(jnp.int32, shape, 1) + block_index * shape[1]
    in_water = columns < limit_rows
    trig = trig_ref[...]
    cosine = jnp.where(in_water, trig[0:1], trig[2:3])
    sine_term = jnp.where(in_water, trig[1:2], trig[3:4])
    out_r = cosine * cot_r + sine_term * cot_i
    out_i = cosine * cot_i - sine_term * cot_r
    screened_r = (cosine * source_r - sine_term * source_i).astype(jnp.bfloat16)
    screened_i = (sine_term * source_r + cosine * source_i).astype(jnp.bfloat16)
    weight = jnp.where(
        in_water,
        cot_i * screened_r.astype(jnp.float32) - cot_r * screened_i.astype(jnp.float32),
        0.0,
    )
    return out_r, out_i, jnp.sum(weight, axis=0, keepdims=True)


HALO = 8


def make_first_half_kernel(block_index):
    def kernel(
        arrival_ref, misfit_ref, source_ref, trig_ref, limit_ref, pade_ref, inverse_t_ref,
        begin_in, begin_out, grad_ref, halo_ref, stage_ref, copy_sem,
    ):
        half, width = arrival_ref.shape[1], arrival_ref.shape[2]
        lam_r = lam_rows(arrival_ref[0], misfit_ref[0])
        lam_i = lam_rows(arrival_ref[1], misfit_ref[1])
        inv_r = inverse_t_ref[0]
        inv_i = inverse_t_ref[1]
        block_width = inv_r.shape[0]
        pieces_r = []
        pieces_i = []
        for start in range(0, half, block_width):
            piece_r, piece_i = azimuth_adjoint(
                inv_r, inv_i, lam_r[start : start + block_width], lam_i[start : start + block_width]
            )
            pieces_r.append(piece_r)
            pieces_i.append(piece_i)
        whole_r = jnp.concatenate(pieces_r, axis=0)
        whole_i = jnp.concatenate(pieces_i, axis=0)
        edge = 2 * HALO
        halo_ref[0] = whole_r[half - edge :]
        halo_ref[1] = whole_i[half - edge :]
        halo_ref[2] = whole_r[:edge]
        halo_ref[3] = whole_i[:edge]
        num_r = numerator_rows(whole_r)[HALO : half - HALO]
        num_i = numerator_rows(whole_i)[HALO : half - HALO]
        cot_r, cot_i = depth_adjoint(
            num_r.astype(jnp.bfloat16), num_i.astype(jnp.bfloat16), pade_ref
        )
        source_r = source_ref[0].astype(jnp.float32)[HALO : half - HALO]
        source_i = source_ref[1].astype(jnp.float32)[HALO : half - HALO]
        out_r, out_i, grad_row = finish_rows(
            cot_r, cot_i, trig_ref, limit_ref[HALO : half - HALO], source_r, source_i, block_index
        )
        stage_ref[0] = out_r.astype(jnp.bfloat16)
        stage_ref[1] = out_i.astype(jnp.bfloat16)
        copy = pltpu.make_async_copy(
            stage_ref,
            begin_out.at[0, :, pl.ds(HALO, half - 2 * HALO), pl.ds(block_index * width, width)],
            copy_sem.at[0],
        )
        copy.start()
        grad_ref[...] = grad_row
        copy.wait()

    return kernel


def make_second_half_kernel(block_index):
    def kernel(
        halo_ref, arrival_ref, misfit_ref, source_hbm, trig_ref, limit_hbm, pade_hbm,
        inverse_hbm, begin_in, begin_out, grad_ref, pade_ref, source_main, source_wrap,
        limit_main, limit_wrap, main_ref, wrap_ref, inverse_t_ref, copy_sem,
    ):
        tail, width = arrival_ref.shape[1], arrival_ref.shape[2]
        half = source_hbm.shape[2] - tail
        columns = pl.ds(block_index * width, width)
        loads = [
            pltpu.make_async_copy(pade_hbm, pade_ref, copy_sem.at[0]),
            pltpu.make_async_copy(
                source_hbm.at[0, :, pl.ds(half - HALO, tail + HALO), columns],
                source_main,
                copy_sem.at[1],
            ),
            pltpu.make_async_copy(
                source_hbm.at[0, :, pl.ds(0, HALO), columns], source_wrap, copy_sem.at[2]
            ),
            pltpu.make_async_copy(
                limit_hbm.at[pl.ds(half - HALO, tail + HALO)], limit_main, copy_sem.at[3]
            ),
            pltpu.make_async_copy(limit_hbm.at[pl.ds(0, HALO)], limit_wrap, copy_sem.at[4]),
        ]
        inverse_load = pltpu.make_async_copy(inverse_hbm, inverse_t_ref, copy_sem.at[7])
        inverse_load.start()
        for load in loads:
            load.start()
        lam_r = lam_rows(arrival_ref[0], misfit_ref[0])
        lam_i = lam_rows(arrival_ref[1], misfit_ref[1])
        inverse_load.wait()
        inv_r = inverse_t_ref[0]
        inv_i = inverse_t_ref[1]
        block_width = inv_r.shape[0]
        pieces_r = [halo_ref[0]]
        pieces_i = [halo_ref[1]]
        for start in range(0, tail, block_width):
            piece_r, piece_i = azimuth_adjoint(
                inv_r, inv_i, lam_r[start : start + block_width], lam_i[start : start + block_width]
            )
            pieces_r.append(piece_r)
            pieces_i.append(piece_i)
        pieces_r.append(halo_ref[2])
        pieces_i.append(halo_ref[3])
        span = tail + 2 * HALO
        num_r = numerator_rows(jnp.concatenate(pieces_r, axis=0))[HALO : HALO + span]
        num_i = numerator_rows(jnp.concatenate(pieces_i, axis=0))[HALO : HALO + span]
        loads[0].wait()
        cot_r, cot_i = depth_adjoint(
            num_r.astype(jnp.bfloat16), num_i.astype(jnp.bfloat16), pade_ref
        )
        for load in loads[1:]:
            load.wait()
        source_r = jnp.concatenate(
            [source_main[0].astype(jnp.float32), source_wrap[0].astype(jnp.float32)], axis=0
        )
        source_i = jnp.concatenate(
            [source_main[1].astype(jnp.float32), source_wrap[1].astype(jnp.float32)], axis=0
        )
        limit_rows = jnp.concatenate([limit_main[...], limit_wrap[...]], axis=0)
        out_r, out_i, grad_row = finish_rows(
            cot_r, cot_i, trig_ref, limit_rows, source_r, source_i, block_index
        )
        main_ref[0] = out_r[: tail + HALO].astype(jnp.bfloat16)
        main_ref[1] = out_i[: tail + HALO].astype(jnp.bfloat16)
        wrap_ref[0] = out_r[tail + HALO :].astype(jnp.bfloat16)
        wrap_ref[1] = out_i[tail + HALO :].astype(jnp.bfloat16)
        main_copy = pltpu.make_async_copy(
            main_ref, begin_out.at[0, :, pl.ds(half - HALO, tail + HALO), columns], copy_sem.at[5]
        )
        wrap_copy = pltpu.make_async_copy(
            wrap_ref, begin_out.at[0, :, pl.ds(0, HALO), columns], copy_sem.at[6]
        )
        main_copy.start()
        wrap_copy.start()
        grad_ref[...] = grad_row
        main_copy.wait()
        wrap_copy.wait()

    return kernel


def range_scan(value, direction):
    count = lax.axis_size("range")
    total = value
    for reach in range(1, count):
        total = total + passed_along(value, "range", direction * reach)
    return total


def fused_local(
    checkpoint, adjoint_start, misfit, pade_factors, azimuth_inverse, bottom, base_speed, speed_step
):
    depth_rows = checkpoint.shape[3]
    rows = checkpoint.shape[2]
    block_size = pade_factors.shape[3]
    block_count = depth_rows // block_size
    depth_start = lax.axis_index("line") * depth_rows
    half = rows // 2
    last = block_count - 1
    arrivals = [
        passed_along(
            adjoint_start[:, :, :, index * block_size : (index + 1) * block_size], "range", -1
        )
        for index in range(last)
    ]
    last_columns = adjoint_start[:, :, :, last * block_size :]
    first_half = passed_along(last_columns[:, :, :half], "range", -1)
    second_half = passed_along(last_columns[:, :, half:], "range", -1)
    halves = [first_half, second_half]
    profile = base_speed + range_scan(speed_step, 1)[0]
    water_phase = phase_scale * (1.0 / (profile * profile) - 1.0)
    bed_row = jnp.full_like(water_phase, bed_phase)
    trig = jnp.stack(
        [jnp.cos(water_phase), jnp.sin(water_phase), jnp.cos(bed_row), jnp.sin(bed_row)]
    )
    limit = (bottom[0] - depth_start)[:, None]
    inverse = azimuth_inverse[0]
    inverse_t = jnp.swapaxes(inverse, 1, 2)
    field_spec = pl.BlockSpec((None, 2, rows, block_size), lambda b: (0, 0, 0, b))
    trig_spec = pl.BlockSpec((4, block_size), lambda b: (0, b))
    limit_spec = pl.BlockSpec((rows, 1), lambda b: (0, 0))
    pade_spec = pl.BlockSpec(pade_factors.shape, lambda b: (0, 0, 0, 0))
    inverse_spec = pl.BlockSpec(inverse.shape, lambda b: (0, 0, 0))
    field_end = pl.pallas_call(
        forward_kernel,
        grid=(block_count,),
        in_specs=[field_spec, trig_spec, limit_spec, pade_spec, inverse_spec],
        out_specs=field_spec,
        out_shape=jax.ShapeDtypeStruct(checkpoint.shape, jnp.bfloat16),
    )(checkpoint, trig, limit, pade_factors, inverse)
    field_end, arrivals[0] = lax.optimization_barrier((field_end, arrivals[0]))
    adjoint_begin = None
    grads = []
    for index in range(last):
        fixed = lambda b, index=index: (0, 0, 0, index)
        chunk_spec = pl.BlockSpec((None, 2, rows, block_size), lambda b: (0, 0, 0, 0))
        block_spec = pl.BlockSpec((None, 2, rows, block_size), fixed)
        in_specs = [
            chunk_spec,
            block_spec,
            block_spec,
            pl.BlockSpec((4, block_size), lambda b, index=index: (0, index)),
            limit_spec,
            pade_spec,
            inverse_spec,
        ]
        operands = [arrivals[index], misfit, checkpoint, trig, limit, pade_factors, inverse_t]
        aliases = {}
        kernel = make_backward_kernel(index)
        if adjoint_begin is not None:
            in_specs.append(pl.BlockSpec(memory_space=pl.ANY))
            operands.append(adjoint_begin)
            aliases = {len(operands) - 1: 0}
            kernel = lambda *refs, kernel=kernel: kernel(*refs[:7], *refs[8:])
        adjoint_begin, grad_part = pl.pallas_call(
            kernel,
            grid=(1,),
            in_specs=in_specs,
            out_specs=[
                block_spec,
                pl.BlockSpec((1, block_size), lambda b: (0, 0)),
            ],
            out_shape=[
                jax.ShapeDtypeStruct(checkpoint.shape, jnp.bfloat16),
                jax.ShapeDtypeStruct((1, block_size), jnp.float32),
            ],
            input_output_aliases=aliases,
        )(*operands)
        grads.append(grad_part)
    any_spec = pl.BlockSpec(memory_space=pl.ANY)
    fixed_last = lambda b: (0, 0, 0, last)
    half_spec = pl.BlockSpec((None, 2, half, block_size), lambda b: (0, 0, 0, 0))
    trig_last = pl.BlockSpec((4, block_size), lambda b: (0, last))
    grad_spec = pl.BlockSpec((1, block_size), lambda b: (0, 0))
    begin_shape = jax.ShapeDtypeStruct(checkpoint.shape, jnp.bfloat16)
    grad_shape = jax.ShapeDtypeStruct((1, block_size), jnp.float32)
    edge = 2 * HALO
    adjoint_begin, grad_first, halo = pl.pallas_call(
        make_first_half_kernel(last),
        grid=(1,),
        in_specs=[
            half_spec,
            pl.BlockSpec((None, 2, half, block_size), fixed_last),
            pl.BlockSpec((None, 2, half, block_size), fixed_last),
            trig_last,
            limit_spec,
            pade_spec,
            inverse_spec,
            any_spec,
        ],
        out_specs=[any_spec, grad_spec, pl.BlockSpec((4, edge, block_size), lambda b: (0, 0, 0))],
        out_shape=[
            begin_shape, grad_shape, jax.ShapeDtypeStruct((4, edge, block_size), jnp.float32)
        ],
        scratch_shapes=[
            pltpu.VMEM((2, half - 2 * HALO, block_size), jnp.bfloat16),
            pltpu.SemaphoreType.DMA((1,)),
        ],
        input_output_aliases={7: 0},
    )(halves[0], misfit, checkpoint, trig, limit, pade_factors, inverse_t, adjoint_begin)
    tail = rows - half
    adjoint_begin, grad_second = pl.pallas_call(
        make_second_half_kernel(last),
        grid=(1,),
        in_specs=[
            pl.BlockSpec((4, edge, block_size), lambda b: (0, 0, 0)),
            pl.BlockSpec((None, 2, tail, block_size), lambda b: (0, 0, 0, 0)),
            pl.BlockSpec((None, 2, tail, block_size), lambda b: (0, 0, 1, last)),
            any_spec,
            trig_last,
            any_spec,
            any_spec,
            any_spec,
            any_spec,
        ],
        out_specs=[any_spec, grad_spec],
        out_shape=[begin_shape, grad_shape],
        scratch_shapes=[
            pltpu.VMEM(pade_factors.shape, jnp.bfloat16),
            pltpu.VMEM((2, tail + HALO, block_size), jnp.bfloat16),
            pltpu.VMEM((2, HALO, block_size), jnp.bfloat16),
            pltpu.VMEM((tail + HALO, 1), jnp.int32),
            pltpu.VMEM((HALO, 1), jnp.int32),
            pltpu.VMEM((2, tail + HALO, block_size), jnp.bfloat16),
            pltpu.VMEM((2, HALO, block_size), jnp.bfloat16),
            pltpu.VMEM(inverse_t.shape, jnp.bfloat16),
            pltpu.SemaphoreType.DMA((8,)),
        ],
        input_output_aliases={8: 0},
    )(
        halo, halves[1], misfit, checkpoint, trig, limit, pade_factors, inverse_t,
        adjoint_begin,
    )
    grads.append(grad_first + grad_second)
    grad_sum = jnp.concatenate(grads, axis=1)
    grad_here = grad_sum * (-8.0 / (profile * profile * profile)) / rows
    grad_increment = range_scan(grad_here, -1)
    return (field_end, adjoint_begin, grad_increment)


def local(
    checkpoint, adjoint_start, misfit, pade_factors, azimuth_inverse, bottom, base_speed, speed_step
):
    if (
        checkpoint.shape[3] % pade_factors.shape[3] == 0
        and checkpoint.shape[3] >= 2 * pade_factors.shape[3]
        and checkpoint.shape[2] % (2 * azimuth_inverse.shape[2]) == 0
    ):
        return fused_local(
            checkpoint, adjoint_start, misfit, pade_factors, azimuth_inverse, bottom,
            base_speed, speed_step,
        )
    return general_local(
        checkpoint, adjoint_start, misfit, pade_factors, azimuth_inverse, bottom,
        base_speed, speed_step,
    )


def solution(mesh):
    in_specs = (
        P("range", "freq", None, "line"),
        P("range", "freq", None, "line"),
        P("range", "freq", None, "line"),
        P(None, "freq", None, None),
        P("range", "freq", None, None),
        P("range", None),
        P("line"),
        P("range", "line"),
    )
    out_specs = (
        P("range", "freq", None, "line"),
        P("range", "freq", None, "line"),
        P(("freq", "range"), "line"),
    )
    return jax.shard_map(local, mesh=mesh, in_specs=in_specs, out_specs=out_specs, check_vma=False)
```
